32 devices in a mesh: section: 2 (over core), expert: 8 (over z, y), tensor: 2 (over x).
Axes of the slice: x: 2, y: 2, z: 4, core: 2. Of those that a mesh axis runs over, the one named last changes fastest.
Arguments:
- hidden_in: bfloat16 [1, 1024, 2560], P(None, 'expert', 'tensor'), may hold values from -6 to 6
- segment_ids: int32 [1, 1024], P(None, 'expert'), may hold values from -1 to 7, as said below
- prompt_lengths: int32 [1, 8], replicated, may hold values from 1 to 682, as said below
- expert_choice: int32 [2, 1, 1024, 4], P('section', None, 'expert'), may hold values from 0 to 7, all different within a row; in each aligned block of 128 rows (0 to 127, 128 to 255, ..., all dimensions but the last counted through in order) at most 80 rows name the same one
- attn_gain: float32 [2, 2560], P('section', 'tensor'), may hold values from 0.1 to 1.9
- ffn_gain: float32 [2, 2560], P('section', 'tensor'), may hold values from 0.1 to 1.9
- w_qkv: bfloat16 [2, 2560, 4, 896], P('section', 'expert', 'tensor'), may hold values from -0.125 to 0.125
- w_out: bfloat16 [2, 2560, 2560], P('section', 'expert', 'tensor'), may hold values from -0.125 to 0.125
- w_shared_in: bfloat16 [2, 2560, 2, 3072], P('section', 'expert', None, 'tensor'), may hold values from -0.125 to 0.125
- w_shared_down: bfloat16 [2, 2560, 3072], P('section', 'expert', 'tensor'), may hold values from -0.109375 to 0.109375
- router_weight: float32 [2, 2560, 8], P('section', 'tensor'), may hold values from -0.125 to 0.125
- w_in: bfloat16 [2, 8, 2560, 2, 1536], P('section', 'expert', None, None, 'tensor'), may hold values from -0.125 to 0.125
- w_down: bfloat16 [2, 8, 1536, 2560], P('section', 'expert', 'tensor'), may hold values from -0.15625 to 0.15625
Outputs:
- hidden_states: bfloat16 [2, 1, 1024, 2560], P('section', None, 'expert', 'tensor')
- kv_cache: bfloat16 [2, 1, 1024, 2, 512], P('section', None, 'expert', None, 'tensor')
The draws below stay inside these ranges and needn't reach their ends.
Inputs may be any that keep to these rules, and one draw needn't show every extreme that they name: segment_ids agree with prompt_lengths: slot s of micro-batch m lies in prompt j where the first j lengths of m sum to at most s and the first j + 1 to more than s; slots past all 8 prompts hold -1. `prompt_lengths`: in every micro-batch exactly one prompt has 682 slots; the 8 lengths sum to at most 1024. `expert_choice`: the 4 entries of a row differ; in each aligned block of 128 rows (section, micro-batch and slot taken together in order) no expert is named by more than 80 rows.
All inputs are finite; a program needn't handle non-finite values.
Results may differ from the reference program's by a relative error of at most 0.02.
Values may be sent and summed in bfloat16 or wider, within the bound.
No kernel may reach another device: no remote copies, remote signals or barrier semaphores. Data moves between devices by JAX's collectives and lax.ppermute only.
A program may use at most 192 MiB of HBM per device.

```python
import math
import jax
import jax.numpy as jnp
import numpy as np
from jax import lax

D = 2560
HEADS = 20
KV_HEADS = 4
HD = 128
FFE = 1536
SHARED_FF = 3072
TOK_DEV = 128
MB = 1
SEGS = 8
EXPERTS = 8
TOP = 4
SLOTS_MB = 1024
CAP = 80
SEG_MOST = 682
N_SECTION = 2
N_EXPERT = 8
N_TENSOR = 2


def segment_layout(key):
    long_key = jax.random.fold_in(key, 11)
    other_key = jax.random.fold_in(key, 12)
    longest = jax.random.randint(long_key, (MB,), 0, SEGS)
    others = jax.random.randint(other_key, (MB, SEGS), 1, (SLOTS_MB - SEG_MOST) // (SEGS - 1) + 1)
    lengths = jnp.where(jnp.arange(SEGS)[None, :] == longest[:, None], SEG_MOST, others).astype(jnp.int32)
    starts = (jnp.cumsum(lengths, axis=1) - lengths).astype(jnp.int32)
    totals = jnp.sum(lengths, axis=1).astype(jnp.int32)
    slot_index = jnp.arange(SLOTS_MB, dtype=jnp.int32)
    segments = jnp.sum((slot_index[None, :, None] >= starts[:, None, :]).astype(jnp.int32), axis=2) - 1
    segments = jnp.where(slot_index[None, :] < totals[:, None], segments, -1)
    return (lengths, segments.astype(jnp.int32))


def draw_segment_ids(key, part):
    return segment_layout(key)[1]


def draw_prompt_lengths(key, part):
    return segment_layout(key)[0]


def level_of(rng, extent, pieces, least, high):
    def one(position, parts):
        heights = jax.random.uniform(jax.random.fold_in(jax.random.fold_in(rng, 6), position), (parts,), jnp.float32, least / len(pieces), high / len(pieces))
        return jnp.repeat(jnp.exp(heights), extent[position] // parts).reshape((-1,) + (1,) * (len(extent) - position - 1))

    factor_of = one(*pieces[0])
    for cut in pieces[1:]:
        factor_of = factor_of * one(*cut)
    return factor_of


def deal_out(own_key, own, number, rows, count, top, reach, skew):
    order = jax.random.permutation(own_key, count)
    crowded, ordinary = load_shares(count, rows * top, reach, skew, True), load_shares(count, rows * top, reach, skew, False)
    places = jnp.arange(count)

    def named(sizes, offset_by):
        used = int((sizes > 0).sum())
        fixed = max(1, used // 4)
        shifted = fixed + (places - fixed + offset_by * (used - fixed)) % max(1, count - fixed)
        return jnp.zeros((count,), jnp.int32).at[order[jnp.where(places < fixed, places, shifted)]].set(jnp.asarray(sizes, jnp.int32))

    sizes = jnp.where(number % 4 == 0, named(crowded, number // 4), named(ordinary, number - number // 4 - 1))
    mixed = jax.random.permutation(jax.random.fold_in(own, 3), count)
    giver, receiver = mixed[0:count // 2 * 2:2], mixed[1:count // 2 * 2:2]
    slack = jnp.minimum(sizes[giver] - 1, reach - sizes[receiver]) // 2
    slack = jnp.where((giver == order[0]) | (receiver == order[0]) | (sizes[receiver] == 0), 0, jnp.maximum(slack, 0))
    shifted = jax.random.randint(jax.random.fold_in(own, 4), (count // 2,), 0, 1 << 20) % (slack + 1)
    sizes = sizes.at[giver].add(-shifted).at[receiver].add(shifted)
    labels = jnp.searchsorted(jnp.cumsum(sizes), jnp.arange(rows * top), side="right").astype(jnp.int32)
    table = labels.reshape(top, rows).T
    table = table[jax.random.permutation(jax.random.fold_in(own, 1), rows)]
    offset_by = jax.random.randint(jax.random.fold_in(own, 2), (rows, 1), 0, top)
    return jnp.take_along_axis(table, (jnp.arange(top)[None, :] + offset_by) % top, axis=1)


def load_shares(amount, total, bound, lean, full):
    portions = [(1 << 20) // math.isqrt(standing ** lean) + 1 for standing in range(1, amount + 1)]
    largest = bound if full else min(bound, max(-(-total // amount), total * portions[0] // sum(portions)))
    least = 1 if total - largest >= amount - 1 else 0
    given, spare = [largest] + [least] * (amount - 1), total - largest - least * (amount - 1)
    while spare > 0:
        candidates = [i for i in range(1, amount) if given[i] < largest] or [i for i in range(1, amount) if given[i] < bound]
        mass, budget = sum([portions[i] for i in candidates]), spare
        for i in candidates:
            extra = min(bound - given[i], max(1, budget * portions[i] // mass), spare)
            given[i] = given[i] + extra
            spare = spare - extra
    return np.array(given)


def centred(own_key, shape, deviation, bound, shards=(), kind=jnp.bfloat16):
    level = level_of(own_key, shape, shards, -0.22, 0.18) if shards else 1.0
    values = jax.random.normal(own_key, shape, jnp.float32) * deviation * level
    return jnp.minimum(jnp.maximum(values, -bound), bound).astype(kind)


def setup_inputs(seed: int = 0) -> dict:
    key_list = jax.random.split(jax.random.key(seed), 14)
    hidden_in = centred(key_list[0], (MB, SLOTS_MB, D), 1.0, 6.0, ((1, 8), (2, 2)))
    segment_ids = draw_segment_ids(jax.random.fold_in(key_list[13], 71), 0)
    prompt_lengths = draw_prompt_lengths(jax.random.fold_in(key_list[13], 71), 0)
    expert_choice_keys = jax.random.split(jax.random.fold_in(key_list[3], 1), N_SECTION * MB * SLOTS_MB // TOK_DEV)
    expert_choice_turns = jax.random.permutation(jax.random.fold_in(key_list[3], 3), N_SECTION * MB * SLOTS_MB // TOK_DEV)
    expert_choice = jax.vmap(lambda own, number: deal_out(jax.random.fold_in(key_list[3], 2), own, number, TOK_DEV, EXPERTS, TOP, CAP, 2))(expert_choice_keys, expert_choice_turns).reshape((N_SECTION, MB, SLOTS_MB, TOP))
    attn_gain = jnp.clip(1.0 + 0.18 * jax.random.normal(key_list[4], (N_SECTION, D), jnp.float32), 0.1, 1.9)
    ffn_gain = jnp.clip(1.0 + 0.18 * jax.random.normal(key_list[5], (N_SECTION, D), jnp.float32), 0.1, 1.9)
    w_qkv = centred(key_list[6], (N_SECTION, D, KV_HEADS, (HEADS // KV_HEADS + 2) * HD), D ** -0.5, 0.125, ((0, 2), (1, 8), (2, 2)))
    w_out = centred(key_list[7], (N_SECTION, D, HEADS * HD), (HEADS * HD) ** -0.5, 0.125, ((0, 2), (1, 8), (2, 2)))
    w_shared_in = centred(key_list[8], (N_SECTION, D, 2, SHARED_FF), D ** -0.5, 0.125, ((0, 2), (1, 8), (3, 2)))
    w_shared_down = centred(key_list[9], (N_SECTION, D, SHARED_FF), SHARED_FF ** -0.5, 0.109375, ((0, 2), (1, 8), (2, 2)))
    router_weight = centred(key_list[10], (N_SECTION, D, EXPERTS), D ** -0.5, 0.125, ((0, 2), (1, 2)), jnp.float32)
    w_in = centred(key_list[11], (N_SECTION, EXPERTS, D, 2, FFE), D ** -0.5, 0.125, ((0, 2), (1, 8), (4, 2)))
    w_down = centred(key_list[12], (N_SECTION, EXPERTS, FFE, D), FFE ** -0.5, 0.15625, ((0, 2), (1, 8), (2, 2)))
    return {"hidden_in": hidden_in, "segment_ids": segment_ids, "prompt_lengths": prompt_lengths, "expert_choice": expert_choice, "attn_gain": attn_gain, "ffn_gain": ffn_gain, "w_qkv": w_qkv, "w_out": w_out, "w_shared_in": w_shared_in, "w_shared_down": w_shared_down, "router_weight": router_weight, "w_in": w_in, "w_down": w_down}


NORM_EPS = 1e-05
ROPE_BASE = 500000.0

def norm_rows(values_in, gain_row):
    widened = values_in.astype(jnp.float32)
    mean_square = lax.optimization_barrier(jnp.mean(widened * widened, axis=-1, keepdims=True))
    return (widened * lax.rsqrt(mean_square + NORM_EPS) * gain_row).astype(jnp.bfloat16)

def rotate_heads(values_in, positions):
    head_width = values_in.shape[-1]
    half_width = head_width // 2
    frequency = ROPE_BASE ** (-(jnp.arange(half_width, dtype=jnp.float32) * (2.0 / head_width)))
    angles = positions[:, None] * frequency[None, :]
    angles = angles.reshape((positions.shape[0],) + (1,) * (values_in.ndim - 2) + (half_width,))
    cosines = jnp.cos(angles)
    sines = jnp.sin(angles)
    first_half = values_in[..., :half_width]
    second_half = values_in[..., half_width:]
    return jnp.concatenate([first_half * cosines - second_half * sines, second_half * cosines + first_half * sines], axis=-1)

def slot_positions(slot_index, segments, lengths):
    starts = (jnp.cumsum(lengths) - lengths).astype(jnp.int32)
    member = segments[:, None] == jnp.arange(lengths.shape[0], dtype=jnp.int32)[None, :]
    first_slot = lax.optimization_barrier(jnp.sum(jnp.where(member, starts[None, :], 0), axis=1)).astype(jnp.int32)
    return jnp.where(segments >= 0, slot_index - first_slot, 0).astype(jnp.float32)

def attend(queries, key_rows, value_rows, segments):
    slot_count = queries.shape[0]
    scale = queries.shape[-1] ** (-0.5)
    slot_index = jnp.arange(slot_count, dtype=jnp.int32)
    key_wide = key_rows.astype(jnp.float32)
    value_wide = value_rows.astype(jnp.float32)
    query_blocks = queries.reshape((N_EXPERT, TOK_DEV) + queries.shape[1:])

    def one_block(inputs):
        block_queries, block_segments, block_slots = inputs
        scores = jnp.einsum('tagd,nad->tagn', block_queries.astype(jnp.float32), key_wide) * scale
        allowed = (block_segments[:, None] == segments[None, :]) & (block_segments[:, None] >= 0) & (slot_index[None, :] <= block_slots[:, None]) | (slot_index[None, :] == block_slots[:, None])
        weights_full = jnp.where(allowed[:, None, None, :], jnp.exp(scores), 0.0)
        denominator = lax.optimization_barrier(jnp.sum(weights_full, axis=-1))
        rounded = lax.optimization_barrier(weights_full.astype(jnp.bfloat16)).astype(jnp.float32)
        numerator = jnp.einsum('tagn,nad->tagd', rounded, value_wide)
        return (numerator / denominator[..., None]).astype(jnp.bfloat16)
    outputs = lax.map(one_block, (query_blocks, segments.reshape(N_EXPERT, TOK_DEV), slot_index.reshape(N_EXPERT, TOK_DEV)))
    return outputs.reshape(slot_count, -1)

def shared_outputs(moe_in, shared_in_layer, shared_down_layer):
    model_width = moe_in.shape[1]
    shared_width = shared_down_layer.shape[1]
    hidden = jnp.dot(moe_in, shared_in_layer.reshape(model_width, 2 * shared_width), preferred_element_type=jnp.float32)
    activated = (jax.nn.silu(hidden[:, :shared_width]) * hidden[:, shared_width:]).astype(jnp.bfloat16)
    block_width = shared_width // N_TENSOR
    summed = jnp.zeros((moe_in.shape[0], model_width), jnp.float32)
    for shard in range(N_TENSOR):
        partial_value = jnp.dot(activated[:, shard * block_width:(shard + 1) * block_width], shared_down_layer[:, shard * block_width:(shard + 1) * block_width].T, preferred_element_type=jnp.float32)
        summed = summed + lax.optimization_barrier(partial_value.astype(jnp.bfloat16)).astype(jnp.float32)
    rounded = lax.optimization_barrier(summed.astype(jnp.bfloat16))
    return rounded.astype(jnp.float32)

def expert_outputs(moe_in, choices, gate_weights, w_in_layer, w_down_layer):
    slot_count, model_width = moe_in.shape
    top_count = choices.shape[1]
    blocks = choices.reshape(N_EXPERT, TOK_DEV * top_count)
    onehot = (blocks[:, :, None] == jnp.arange(EXPERTS, dtype=jnp.int32)[None, None, :]).astype(jnp.int32)
    slot_rank = lax.optimization_barrier(jnp.sum(onehot * (jnp.cumsum(onehot, axis=1).astype(jnp.int32) - onehot), axis=2)).astype(jnp.int32)
    column_at = (jnp.arange(N_EXPERT, dtype=jnp.int32)[:, None] * CAP + slot_rank).astype(jnp.int32)
    row_source = (jnp.arange(N_EXPERT * TOK_DEV * top_count, dtype=jnp.int32) // top_count).reshape(N_EXPERT, -1)
    table = jnp.zeros((EXPERTS, N_EXPERT * CAP), jnp.int32).at[blocks, column_at].set(row_source)
    filled = jnp.zeros((EXPERTS, N_EXPERT * CAP), jnp.bool_).at[blocks, column_at].set(True)
    gathered = jnp.where(filled[..., None], moe_in[table], jnp.zeros((), jnp.bfloat16))
    block_width = FFE // N_TENSOR

    def one_expert(inputs):
        row_block, weight_in, weight_down = inputs
        hidden = jnp.dot(row_block, weight_in.reshape(model_width, 2 * FFE), preferred_element_type=jnp.float32)
        activated = (jax.nn.silu(hidden[:, :FFE]) * hidden[:, FFE:]).astype(jnp.bfloat16)
        summed = jnp.zeros((row_block.shape[0], model_width), jnp.float32)
        for shard in range(N_TENSOR):
            partial_value = jnp.dot(activated[:, shard * block_width:(shard + 1) * block_width], weight_down[shard * block_width:(shard + 1) * block_width], preferred_element_type=jnp.float32)
            summed = summed + lax.optimization_barrier(partial_value.astype(jnp.bfloat16)).astype(jnp.float32)
        return summed.astype(jnp.bfloat16)
    results = lax.map(one_expert, (gathered, w_in_layer, w_down_layer))
    picked = results[blocks, column_at].reshape(slot_count, top_count, model_width).astype(jnp.float32)
    return lax.optimization_barrier(jnp.sum(picked * gate_weights[:, :, None], axis=1))

def layer_step(hidden, segments, lengths, choices, attn_gain_row, ffn_gain_row, w_qkv_layer, w_out_layer, shared_in_layer, shared_down_layer, router_layer, w_in_layer, w_down_layer):
    slot_count, model_width = hidden.shape
    kv_count = w_qkv_layer.shape[1]
    group = w_qkv_layer.shape[2] // HD - 2
    slot_index = jnp.arange(slot_count, dtype=jnp.int32)
    positions = slot_positions(slot_index, segments, lengths)
    normed = norm_rows(hidden, attn_gain_row)
    projected = jnp.dot(normed, w_qkv_layer.reshape(model_width, -1), preferred_element_type=jnp.float32)
    projected = projected.reshape(slot_count, kv_count, group + 2, HD)
    queries = rotate_heads(projected[:, :, :group], positions).astype(jnp.bfloat16)
    key_rows = rotate_heads(projected[:, :, group], positions).astype(jnp.bfloat16)
    value_rows = projected[:, :, group + 1].astype(jnp.bfloat16)
    cache = jnp.stack([key_rows.reshape(slot_count, -1), value_rows.reshape(slot_count, -1)], axis=1)
    attended = attend(queries, key_rows, value_rows, segments)
    columns = attended.shape[1] // N_TENSOR
    attn_sum = jnp.zeros((slot_count, model_width), jnp.float32)
    for shard in range(N_TENSOR):
        partial_value = jnp.dot(attended[:, shard * columns:(shard + 1) * columns], w_out_layer[:, shard * columns:(shard + 1) * columns].T, preferred_element_type=jnp.float32)
        attn_sum = attn_sum + lax.optimization_barrier(partial_value.astype(jnp.bfloat16)).astype(jnp.float32)
    after_attn = (hidden.astype(jnp.float32) + attn_sum).astype(jnp.bfloat16)
    moe_in = norm_rows(after_attn, ffn_gain_row)
    shared_out = shared_outputs(moe_in, shared_in_layer, shared_down_layer)
    logits = jnp.dot(moe_in.astype(jnp.float32), router_layer, precision=lax.Precision.HIGHEST)
    picked = jnp.take_along_axis(logits, choices, axis=1)
    raised = jnp.exp(picked)
    gate_weights = raised / lax.optimization_barrier(jnp.sum(raised, axis=1, keepdims=True))
    moe_out = expert_outputs(moe_in, choices, gate_weights, w_in_layer, w_down_layer)
    return ((after_attn.astype(jnp.float32) + shared_out + moe_out).astype(jnp.bfloat16), cache)

def reference(hidden_in, segment_ids, prompt_lengths, expert_choice, attn_gain, ffn_gain, w_qkv, w_out, w_shared_in, w_shared_down, router_weight, w_in, w_down):
    current = hidden_in
    states = []
    caches = []
    for layer_index in range(N_SECTION):
        layer_states = []
        layer_caches = []
        for micro_index in range(MB):
            output, cache = layer_step(current[micro_index], segment_ids[micro_index], prompt_lengths[micro_index], expert_choice[layer_index, micro_index], attn_gain[layer_index], ffn_gain[layer_index], w_qkv[layer_index], w_out[layer_index], w_shared_in[layer_index], w_shared_down[layer_index], router_weight[layer_index], w_in[layer_index], w_down[layer_index])
            layer_states.append(output)
            layer_caches.append(cache)
        current = jnp.stack(layer_states)
        states.append(current)
        caches.append(jnp.stack(layer_caches))
    return (jnp.stack(states), jnp.stack(caches))
```

```python
import jax
import jax.numpy as jnp
from jax import lax
from jax.sharding import PartitionSpec as P

HD = 128


NORM_EPS = 1e-05
ROPE_BASE = 500000.0


def passed_along(value, axis, steps):
    count = lax.axis_size(axis)
    leading, last = (max(0, -steps), min(count, count - steps))
    return lax.ppermute(value, axis, [(source, source + steps) for source in range(leading, last)])


def rotate_heads(values_in, positions):
    head_width = values_in.shape[-1]
    half_width = head_width // 2
    frequency = ROPE_BASE ** (-(jnp.arange(half_width, dtype=jnp.float32) * (2.0 / head_width)))
    angles = positions[:, None] * frequency[None, :]
    angles = angles.reshape((positions.shape[0],) + (1,) * (values_in.ndim - 2) + (half_width,))
    cosines = jnp.cos(angles)
    sines = jnp.sin(angles)
    first_half = values_in[..., :half_width]
    second_half = values_in[..., half_width:]
    return jnp.concatenate(
        [first_half * cosines - second_half * sines, second_half * cosines + first_half * sines],
        axis=-1,
    )


def norm_rows(values_in, gain_row, model_width):
    widened = values_in.astype(jnp.float32)
    squares = lax.psum(jnp.sum(widened * widened, axis=-1), "tensor")
    return (widened * lax.rsqrt(squares / model_width + NORM_EPS)[:, None] * gain_row).astype(
        jnp.bfloat16
    )


def terms_to_slots(terms):
    by_slot = lax.all_to_all(terms, "expert", split_axis=0, concat_axis=1, tiled=True)
    return lax.psum_scatter(by_slot, "tensor", scatter_dimension=1, tiled=True)


def expert_path(full_rows, w_in_local, w_down_local):
    sources, slot_count, model_width = full_rows.shape
    local_width = w_down_local.shape[0]
    hidden = jnp.dot(
        full_rows.reshape(sources * slot_count, model_width),
        w_in_local.reshape(model_width, 2 * local_width),
        preferred_element_type=jnp.float32,
    )
    activated = (jax.nn.silu(hidden[:, :local_width]) * hidden[:, local_width:]).astype(
        jnp.bfloat16
    )
    partial_value = jnp.dot(activated, w_down_local, preferred_element_type=jnp.float32)
    partial_value = partial_value.reshape(sources, slot_count, model_width)
    summed = lax.psum_scatter(
        partial_value.astype(jnp.bfloat16), "tensor", scatter_dimension=2, tiled=True
    )
    return lax.all_to_all(summed, "expert", split_axis=0, concat_axis=0, tiled=True)


def local(
    hidden_in,
    segment_ids,
    prompt_lengths,
    expert_choice,
    attn_gain,
    ffn_gain,
    w_qkv,
    w_out,
    w_shared_in,
    w_shared_down,
    router_weight,
    w_in,
    w_down,
):
    sections = lax.axis_size("section")
    section_id = lax.axis_index("section")
    experts_count = lax.axis_size("expert")
    expert_id = lax.axis_index("expert")
    micro_count, tokens_dev, columns = hidden_in.shape
    qkv_full = lax.all_gather(w_qkv[0], "expert", axis=0, tiled=True)
    out_local = w_out[0]
    shared_down_local = w_shared_down[0]
    shared_in_cols = lax.all_to_all(w_shared_in[0], "expert", split_axis=2, concat_axis=0, tiled=True)
    model_width, kv_local, group_cols = qkv_full.shape
    shared_cols = shared_in_cols.shape[2]
    head_width = HD
    group = group_cols // head_width - 2
    scale = head_width ** (-0.5)
    top_count = expert_choice.shape[-1]
    capacity = 5 * tokens_dev * top_count // (4 * experts_count)
    slot_index = expert_id * tokens_dev + jnp.arange(tokens_dev, dtype=jnp.int32)
    w_in_local = w_in[0, 0]
    w_down_local = w_down[0, 0]
    carried_rows = jnp.zeros((tokens_dev, columns), jnp.bfloat16)
    states = jnp.zeros((micro_count, tokens_dev, columns), jnp.bfloat16)
    caches = jnp.zeros((micro_count, tokens_dev, 2, kv_local * head_width), jnp.bfloat16)
    ticks = micro_count + sections - 1
    for tick_index in range(ticks):
        micro_index = jnp.clip(tick_index - section_id, 0, micro_count - 1)
        incoming = jnp.where(
            section_id == 0, hidden_in[min(tick_index, micro_count - 1)], carried_rows
        )
        active = (tick_index - section_id >= 0) & (tick_index - section_id < micro_count)
        segments = segment_ids[micro_index]
        lengths = prompt_lengths[micro_index]
        choices = expert_choice[0, micro_index]
        starts = jnp.cumsum(lengths) - lengths
        member = segments[:, None] == jnp.arange(lengths.shape[0], dtype=jnp.int32)[None, :]
        first_slot = jnp.sum(jnp.where(member, starts[None, :], 0), axis=1)
        positions = jnp.where(segments >= 0, slot_index - first_slot, 0).astype(jnp.float32)
        normed = norm_rows(incoming, attn_gain[0], model_width)
        normed_full = lax.all_gather(normed, "tensor", axis=1, tiled=True)
        projected = jnp.dot(
            normed_full, qkv_full.reshape(model_width, -1), preferred_element_type=jnp.float32
        )
        projected = projected.reshape(tokens_dev, kv_local, group + 2, head_width)
        queries = rotate_heads(projected[:, :, :group], positions).astype(jnp.bfloat16)
        key_rows = rotate_heads(projected[:, :, group], positions).astype(jnp.bfloat16)
        value_rows = projected[:, :, group + 1].astype(jnp.bfloat16)
        cache = jnp.stack(
            [key_rows.reshape(tokens_dev, -1), value_rows.reshape(tokens_dev, -1)], axis=1
        )
        kv_piece = lax.all_gather(cache.reshape(tokens_dev, -1), "expert", axis=0, tiled=True)
        seg_piece = lax.all_gather(segments, "expert", axis=0, tiled=True)
        key_count = kv_piece.shape[0]
        kv_piece = kv_piece.reshape(key_count, 2, kv_local, head_width)
        key_slots = jnp.arange(key_count, dtype=jnp.int32)
        allowed = (segments[:, None] == seg_piece[None, :]) & (segments[:, None] >= 0) & (
            key_slots[None, :] <= slot_index[:, None]
        ) | (key_slots[None, :] == slot_index[:, None])
        scores = (
            jnp.einsum(
                "tagd,nad->tagn", queries, kv_piece[:, 0], preferred_element_type=jnp.float32
            )
            * scale
        )
        weights_full = jnp.where(allowed[:, None, None, :], jnp.exp(scores), 0.0)
        numerator = jnp.einsum(
            "tagn,nad->tagd",
            weights_full.astype(jnp.bfloat16),
            kv_piece[:, 1],
            preferred_element_type=jnp.float32,
        )
        numerator, denominator = (numerator, jnp.sum(weights_full, axis=-1))
        attended = (numerator / denominator[..., None]).astype(jnp.bfloat16).reshape(tokens_dev, -1)
        attended_all = lax.all_gather(attended, "expert", axis=0, tiled=True)
        attn_terms = lax.dot_general(
            attended_all, out_local, (((1,), (1,)), ((), ())), preferred_element_type=jnp.float32
        )
        attn_sum = terms_to_slots(attn_terms.astype(jnp.bfloat16)).astype(jnp.float32)
        after_attn = (incoming.astype(jnp.float32) + attn_sum).astype(jnp.bfloat16)
        moe_in = norm_rows(after_attn, ffn_gain[0], model_width)
        moe_rows = lax.all_gather(moe_in, "tensor", axis=1, tiled=True)
        moe_all = lax.all_gather(moe_rows, "expert", axis=0, tiled=True)
        shared_hidden = jnp.dot(
            moe_all,
            shared_in_cols.reshape(model_width, 2 * shared_cols),
            preferred_element_type=jnp.float32,
        )
        shared_act = (
            jax.nn.silu(shared_hidden[:, :shared_cols]) * shared_hidden[:, shared_cols:]
        ).astype(jnp.bfloat16)
        shared_act = lax.all_gather(shared_act, "expert", axis=1, tiled=True)
        shared_terms = lax.dot_general(
            shared_act,
            shared_down_local,
            (((1,), (1,)), ((), ())),
            preferred_element_type=jnp.float32,
        )
        shared_sum = terms_to_slots(shared_terms.astype(jnp.bfloat16))
        shared_out = lax.optimization_barrier(shared_sum).astype(jnp.float32)
        logits = lax.psum(
            jnp.dot(moe_in.astype(jnp.float32), router_weight[0], precision=lax.Precision.HIGHEST),
            "tensor",
        )
        expert_ids = jnp.arange(logits.shape[1], dtype=jnp.int32)
        picked = jnp.sum(
            jnp.where(choices[:, :, None] == expert_ids[None, None, :], logits[:, None, :], 0.0),
            axis=2,
        )
        raised = jnp.exp(picked)
        gate_weights = raised / jnp.sum(raised, axis=1, keepdims=True)
        flat_choice = choices.reshape(-1)
        onehot = (flat_choice[:, None] == expert_ids[None, :]).astype(jnp.int32)
        slot_rank = jnp.sum(onehot * (jnp.cumsum(onehot, axis=0) - onehot), axis=1)
        slot_ids = flat_choice * capacity + slot_rank
        row_source = jnp.arange(tokens_dev * top_count, dtype=jnp.int32) // top_count
        table = jnp.zeros((experts_count * capacity,), jnp.int32).at[slot_ids].set(row_source)
        filled = jnp.zeros((experts_count * capacity,), jnp.bool_).at[slot_ids].set(True)
        outgoing = jnp.where(filled[:, None], moe_rows[table], jnp.zeros((), jnp.bfloat16))
        outgoing = outgoing.reshape(experts_count, capacity, model_width)
        returned = expert_path(
            lax.all_to_all(outgoing, "expert", split_axis=0, concat_axis=0, tiled=True),
            w_in_local,
            w_down_local,
        )
        combined = returned.reshape(experts_count * capacity, columns)[slot_ids].astype(jnp.float32)
        combined = combined * gate_weights.reshape(-1)[:, None]
        moe_out = jnp.sum(combined.reshape(tokens_dev, top_count, columns), axis=1)
        output = (after_attn.astype(jnp.float32) + shared_out + moe_out).astype(jnp.bfloat16)
        output, cache = (output, cache)
        states = jnp.where(active, states.at[micro_index].set(output), states)
        caches = jnp.where(active, caches.at[micro_index].set(cache), caches)
        if tick_index + 1 < ticks:
            carried_rows = passed_along(output, "section", 1)
    return (states[None], caches[None])


def solution(mesh):
    placed = (
        P(None, "expert", "tensor"),
        P(None, "expert"),
        P(),
        P("section", None, "expert", None),
        P("section", "tensor"),
        P("section", "tensor"),
        P("section", "expert", "tensor", None),
        P("section", "expert", "tensor"),
        P("section", "expert", None, "tensor"),
        P("section", "expert", "tensor"),
        P("section", "tensor", None),
        P("section", "expert", None, None, "tensor"),
        P("section", "expert", "tensor", None),
    )
    return jax.shard_map(
        local,
        mesh=mesh,
        in_specs=placed,
        out_specs=(
            P("section", None, "expert", "tensor"),
            P("section", None, "expert", None, "tensor"),
        ),
        check_vma=False,
    )
```

```python
import jax
import jax.numpy as jnp
from jax import lax
from jax.sharding import PartitionSpec as P

HD = 128


NORM_EPS = 1e-05
ROPE_BASE = 500000.0


def passed_along(value, axis, steps):
    count = lax.axis_size(axis)
    leading, last = (max(0, -steps), min(count, count - steps))
    return lax.ppermute(value, axis, [(source, source + steps) for source in range(leading, last)])


def rotate_heads(values_in, positions):
    head_width = values_in.shape[-1]
    half_width = head_width // 2
    frequency = ROPE_BASE ** (-(jnp.arange(half_width, dtype=jnp.float32) * (2.0 / head_width)))
    angles = positions[:, None] * frequency[None, :]
    angles = angles.reshape((positions.shape[0],) + (1,) * (values_in.ndim - 2) + (half_width,))
    cosines = jnp.cos(angles)
    sines = jnp.sin(angles)
    first_half = values_in[..., :half_width]
    second_half = values_in[..., half_width:]
    return jnp.concatenate(
        [first_half * cosines - second_half * sines, second_half * cosines + first_half * sines],
        axis=-1,
    )


def norm_rows(values_in, gain_row, model_width):
    widened = values_in.astype(jnp.float32)
    squares = lax.psum(jnp.sum(widened * widened, axis=-1), "tensor")
    return (widened * lax.rsqrt(squares / model_width + NORM_EPS)[:, None] * gain_row).astype(
        jnp.bfloat16
    )


def terms_to_slots(terms):
    by_slot = lax.all_to_all(terms, "expert", split_axis=0, concat_axis=1, tiled=True)
    return lax.psum_scatter(by_slot, "tensor", scatter_dimension=1, tiled=True)


def expert_path(full_rows, w_in_local, w_down_local):
    sources, slot_count, model_width = full_rows.shape
    local_width = w_down_local.shape[0]
    hidden = jnp.dot(
        full_rows.reshape(sources * slot_count, model_width),
        w_in_local.reshape(model_width, 2 * local_width),
        preferred_element_type=jnp.float32,
    )
    activated = (jax.nn.silu(hidden[:, :local_width]) * hidden[:, local_width:]).astype(
        jnp.bfloat16
    )
    partial_value = jnp.dot(activated, w_down_local, preferred_element_type=jnp.float32)
    partial_value = partial_value.reshape(sources, slot_count, model_width)
    summed = lax.psum_scatter(
        partial_value.astype(jnp.bfloat16), "tensor", scatter_dimension=2, tiled=True
    )
    return lax.all_to_all(summed, "expert", split_axis=0, concat_axis=0, tiled=True)


def local(
    hidden_in,
    segment_ids,
    prompt_lengths,
    expert_choice,
    attn_gain,
    ffn_gain,
    w_qkv,
    w_out,
    w_shared_in,
    w_shared_down,
    router_weight,
    w_in,
    w_down,
):
    sections = lax.axis_size("section")
    section_id = lax.axis_index("section")
    experts_count = lax.axis_size("expert")
    expert_id = lax.axis_index("expert")
    micro_count, tokens_dev, columns = hidden_in.shape
    qkv_full = lax.all_gather(w_qkv[0], "expert", axis=0, tiled=True)
    out_local = w_out[0]
    shared_down_local = w_shared_down[0]
    shared_in_cols = lax.all_to_all(w_shared_in[0], "expert", split_axis=2, concat_axis=0, tiled=True)
    qkv_full, shared_in_cols = lax.optimization_barrier((qkv_full, shared_in_cols))
    model_width, kv_local, group_cols = qkv_full.shape
    shared_cols = shared_in_cols.shape[2]
    head_width = HD
    group = group_cols // head_width - 2
    scale = head_width ** (-0.5)
    top_count = expert_choice.shape[-1]
    capacity = 5 * tokens_dev * top_count // (4 * experts_count)
    slot_index = expert_id * tokens_dev + jnp.arange(tokens_dev, dtype=jnp.int32)
    w_in_local = w_in[0, 0]
    w_down_local = w_down[0, 0]
    carried_rows = jnp.zeros((tokens_dev, columns), jnp.bfloat16)
    states = jnp.zeros((micro_count, tokens_dev, columns), jnp.bfloat16)
    caches = jnp.zeros((micro_count, tokens_dev, 2, kv_local * head_width), jnp.bfloat16)
    ticks = micro_count + sections - 1
    for tick_index in range(ticks):
        micro_index = jnp.clip(tick_index - section_id, 0, micro_count - 1)
        incoming = jnp.where(
            section_id == 0, hidden_in[min(tick_index, micro_count - 1)], carried_rows
        )
        active = (tick_index - section_id >= 0) & (tick_index - section_id < micro_count)
        segments = segment_ids[micro_index]
        lengths = prompt_lengths[micro_index]
        choices = expert_choice[0, micro_index]
        starts = jnp.cumsum(lengths) - lengths
        member = segments[:, None] == jnp.arange(lengths.shape[0], dtype=jnp.int32)[None, :]
        first_slot = jnp.sum(jnp.where(member, starts[None, :], 0), axis=1)
        positions = jnp.where(segments >= 0, slot_index - first_slot, 0).astype(jnp.float32)
        normed = norm_rows(incoming, attn_gain[0], model_width)
        normed_full = lax.all_gather(normed, "tensor", axis=1, tiled=True)
        projected = jnp.dot(
            normed_full, qkv_full.reshape(model_width, -1), preferred_element_type=jnp.float32
        )
        projected = projected.reshape(tokens_dev, kv_local, group + 2, head_width)
        queries = rotate_heads(projected[:, :, :group], positions).astype(jnp.bfloat16)
        key_rows = rotate_heads(projected[:, :, group], positions).astype(jnp.bfloat16)
        value_rows = projected[:, :, group + 1].astype(jnp.bfloat16)
        cache = jnp.stack(
            [key_rows.reshape(tokens_dev, -1), value_rows.reshape(tokens_dev, -1)], axis=1
        )
        kv_piece = lax.all_gather(cache.reshape(tokens_dev, -1), "expert", axis=0, tiled=True)
        seg_piece = lax.all_gather(segments, "expert", axis=0, tiled=True)
        key_count = kv_piece.shape[0]
        kv_piece = kv_piece.reshape(key_count, 2, kv_local, head_width)
        key_slots = jnp.arange(key_count, dtype=jnp.int32)
        allowed = (segments[:, None] == seg_piece[None, :]) & (segments[:, None] >= 0) & (
            key_slots[None, :] <= slot_index[:, None]
        ) | (key_slots[None, :] == slot_index[:, None])
        scores = (
            jnp.einsum(
                "tagd,nad->tagn", queries, kv_piece[:, 0], preferred_element_type=jnp.float32
            )
            * scale
        )
        weights_full = jnp.where(allowed[:, None, None, :], jnp.exp(scores), 0.0)
        numerator = jnp.einsum(
            "tagn,nad->tagd",
            weights_full.astype(jnp.bfloat16),
            kv_piece[:, 1],
            preferred_element_type=jnp.float32,
        )
        numerator, denominator = (numerator, jnp.sum(weights_full, axis=-1))
        attended = (numerator / denominator[..., None]).astype(jnp.bfloat16).reshape(tokens_dev, -1)
        attended_all = lax.all_gather(attended, "expert", axis=0, tiled=True)
        attn_terms = lax.dot_general(
            attended_all, out_local, (((1,), (1,)), ((), ())), preferred_element_type=jnp.float32
        )
        attn_sum = terms_to_slots(attn_terms.astype(jnp.bfloat16)).astype(jnp.float32)
        after_attn = (incoming.astype(jnp.float32) + attn_sum).astype(jnp.bfloat16)
        moe_in = norm_rows(after_attn, ffn_gain[0], model_width)
        moe_rows = lax.all_gather(moe_in, "tensor", axis=1, tiled=True)
        moe_all = lax.all_gather(moe_rows, "expert", axis=0, tiled=True)
        shared_hidden = jnp.dot(
            moe_all,
            shared_in_cols.reshape(model_width, 2 * shared_cols),
            preferred_element_type=jnp.float32,
        )
        shared_act = (
            jax.nn.silu(shared_hidden[:, :shared_cols]) * shared_hidden[:, shared_cols:]
        ).astype(jnp.bfloat16)
        shared_act = lax.all_gather(shared_act, "expert", axis=1, tiled=True)
        shared_terms = lax.dot_general(
            shared_act,
            shared_down_local,
            (((1,), (1,)), ((), ())),
            preferred_element_type=jnp.float32,
        )
        shared_sum = terms_to_slots(shared_terms.astype(jnp.bfloat16))
        shared_out = lax.optimization_barrier(shared_sum).astype(jnp.float32)
        logits = lax.psum(
            jnp.dot(moe_in.astype(jnp.float32), router_weight[0], precision=lax.Precision.HIGHEST),
            "tensor",
        )
        expert_ids = jnp.arange(logits.shape[1], dtype=jnp.int32)
        picked = jnp.sum(
            jnp.where(choices[:, :, None] == expert_ids[None, None, :], logits[:, None, :], 0.0),
            axis=2,
        )
        raised = jnp.exp(picked)
        gate_weights = raised / jnp.sum(raised, axis=1, keepdims=True)
        flat_choice = choices.reshape(-1)
        onehot = (flat_choice[:, None] == expert_ids[None, :]).astype(jnp.int32)
        slot_rank = jnp.sum(onehot * (jnp.cumsum(onehot, axis=0) - onehot), axis=1)
        slot_ids = flat_choice * capacity + slot_rank
        choices_all = lax.all_gather(choices, "expert", axis=0, tiled=False)
        mine = jnp.any(choices_all == expert_id, axis=2)
        mine_rank = jnp.cumsum(mine.astype(jnp.int32), axis=1) - 1
        source_ids = jnp.broadcast_to(
            jnp.arange(experts_count, dtype=jnp.int32)[:, None], mine.shape
        )
        token_ids = jnp.broadcast_to(jnp.arange(tokens_dev, dtype=jnp.int32)[None, :], mine.shape)
        rank_at = jnp.where(mine, mine_rank, capacity)
        table = (
            jnp.zeros((experts_count, capacity), jnp.int32)
            .at[source_ids, rank_at]
            .set(source_ids * tokens_dev + token_ids, mode="drop")
        )
        filled = (
            jnp.zeros((experts_count, capacity), jnp.bool_)
            .at[source_ids, rank_at]
            .set(True, mode="drop")
        )
        incoming_rows = jnp.where(filled[..., None], moe_all[table], jnp.zeros((), jnp.bfloat16))
        returned = expert_path(incoming_rows, w_in_local, w_down_local)
        combined = returned.reshape(experts_count * capacity, columns)[slot_ids].astype(jnp.float32)
        combined = combined * gate_weights.reshape(-1)[:, None]
        moe_out = jnp.sum(combined.reshape(tokens_dev, top_count, columns), axis=1)
        output = (after_attn.astype(jnp.float32) + shared_out + moe_out).astype(jnp.bfloat16)
        output, cache = (output, cache)
        states = jnp.where(active, states.at[micro_index].set(output), states)
        caches = jnp.where(active, caches.at[micro_index].set(cache), caches)
        if tick_index + 1 < ticks:
            carried_rows = passed_along(output, "section", 1)
    return (states[None], caches[None])


def solution(mesh):
    placed = (
        P(None, "expert", "tensor"),
        P(None, "expert"),
        P(),
        P("section", None, "expert", None),
        P("section", "tensor"),
        P("section", "tensor"),
        P("section", "expert", "tensor", None),
        P("section", "expert", "tensor"),
        P("section", "expert", None, "tensor"),
        P("section", "expert", "tensor"),
        P("section", "tensor", None),
        P("section", "expert", None, None, "tensor"),
        P("section", "expert", "tensor", None),
    )
    return jax.shard_map(
        local,
        mesh=mesh,
        in_specs=placed,
        out_specs=(
            P("section", None, "expert", "tensor"),
            P("section", None, "expert", None, "tensor"),
        ),
        check_vma=False,
    )
```

```python
import jax
import jax.numpy as jnp
from jax import lax
from jax.sharding import PartitionSpec as P

HD = 128


NORM_EPS = 1e-05
ROPE_BASE = 500000.0


def passed_along(value, axis, steps):
    count = lax.axis_size(axis)
    leading, last = (max(0, -steps), min(count, count - steps))
    return lax.ppermute(value, axis, [(source, source + steps) for source in range(leading, last)])


def rotate_heads(values_in, positions):
    head_width = values_in.shape[-1]
    half_width = head_width // 2
    frequency = ROPE_BASE ** (-(jnp.arange(half_width, dtype=jnp.float32) * (2.0 / head_width)))
    angles = positions[:, None] * frequency[None, :]
    angles = angles.reshape((positions.shape[0],) + (1,) * (values_in.ndim - 2) + (half_width,))
    cosines = jnp.cos(angles)
    sines = jnp.sin(angles)
    first_half = values_in[..., :half_width]
    second_half = values_in[..., half_width:]
    return jnp.concatenate(
        [first_half * cosines - second_half * sines, second_half * cosines + first_half * sines],
        axis=-1,
    )


def norm_rows(values_in, gain_row, model_width):
    widened = values_in.astype(jnp.float32)
    squares = lax.psum(jnp.sum(widened * widened, axis=-1), "tensor")
    return (widened * lax.rsqrt(squares / model_width + NORM_EPS)[:, None] * gain_row).astype(
        jnp.bfloat16
    )


def terms_to_slots(terms):
    by_slot = lax.all_to_all(terms, "expert", split_axis=0, concat_axis=1, tiled=True)
    return lax.psum_scatter(by_slot, "tensor", scatter_dimension=1, tiled=True)


def expert_path(full_rows, w_in_local, w_down_local):
    sources, slot_count, model_width = full_rows.shape
    local_width = w_down_local.shape[0]
    hidden = jnp.dot(
        full_rows.reshape(sources * slot_count, model_width),
        w_in_local.reshape(model_width, 2 * local_width),
        preferred_element_type=jnp.float32,
    )
    activated = (jax.nn.silu(hidden[:, :local_width]) * hidden[:, local_width:]).astype(
        jnp.bfloat16
    )
    partial_value = jnp.dot(activated, w_down_local, preferred_element_type=jnp.float32)
    partial_value = partial_value.reshape(sources, slot_count, model_width)
    summed = lax.psum_scatter(
        partial_value.astype(jnp.bfloat16), "tensor", scatter_dimension=2, tiled=True
    )
    return lax.all_to_all(summed, "expert", split_axis=0, concat_axis=0, tiled=True)


def local(
    hidden_in,
    segment_ids,
    prompt_lengths,
    expert_choice,
    attn_gain,
    ffn_gain,
    w_qkv,
    w_out,
    w_shared_in,
    w_shared_down,
    router_weight,
    w_in,
    w_down,
):
    sections = lax.axis_size("section")
    section_id = lax.axis_index("section")
    experts_count = lax.axis_size("expert")
    expert_id = lax.axis_index("expert")
    micro_count, tokens_dev, columns = hidden_in.shape
    qkv_full = lax.all_gather(w_qkv[0], "expert", axis=0, tiled=True)
    out_local = w_out[0]
    shared_down_local = w_shared_down[0]
    shared_in_cols = lax.all_to_all(w_shared_in[0], "expert", split_axis=2, concat_axis=0, tiled=True)
    choices_every = lax.all_gather(expert_choice[0], "expert", axis=0, tiled=False)
    qkv_full, shared_in_cols, choices_every = lax.optimization_barrier(
        (qkv_full, shared_in_cols, choices_every)
    )
    model_width, kv_local, group_cols = qkv_full.shape
    shared_cols = shared_in_cols.shape[2]
    head_width = HD
    group = group_cols // head_width - 2
    scale = head_width ** (-0.5)
    top_count = expert_choice.shape[-1]
    capacity = 5 * tokens_dev * top_count // (4 * experts_count)
    slot_index = expert_id * tokens_dev + jnp.arange(tokens_dev, dtype=jnp.int32)
    w_in_local = w_in[0, 0]
    w_down_local = w_down[0, 0]
    carried_rows = jnp.zeros((tokens_dev, columns), jnp.bfloat16)
    states = jnp.zeros((micro_count, tokens_dev, columns), jnp.bfloat16)
    caches = jnp.zeros((micro_count, tokens_dev, 2, kv_local * head_width), jnp.bfloat16)
    ticks = micro_count + sections - 1
    for tick_index in range(ticks):
        micro_index = jnp.clip(tick_index - section_id, 0, micro_count - 1)
        incoming = jnp.where(
            section_id == 0, hidden_in[min(tick_index, micro_count - 1)], carried_rows
        )
        active = (tick_index - section_id >= 0) & (tick_index - section_id < micro_count)
        segments = segment_ids[micro_index]
        lengths = prompt_lengths[micro_index]
        choices = expert_choice[0, micro_index]
        starts = jnp.cumsum(lengths) - lengths
        member = segments[:, None] == jnp.arange(lengths.shape[0], dtype=jnp.int32)[None, :]
        first_slot = jnp.sum(jnp.where(member, starts[None, :], 0), axis=1)
        positions = jnp.where(segments >= 0, slot_index - first_slot, 0).astype(jnp.float32)
        normed = norm_rows(incoming, attn_gain[0], model_width)
        normed_full = lax.all_gather(normed, "tensor", axis=1, tiled=True)
        projected = jnp.dot(
            normed_full, qkv_full.reshape(model_width, -1), preferred_element_type=jnp.float32
        )
        projected = projected.reshape(tokens_dev, kv_local, group + 2, head_width)
        queries = rotate_heads(projected[:, :, :group], positions).astype(jnp.bfloat16)
        key_rows = rotate_heads(projected[:, :, group], positions).astype(jnp.bfloat16)
        value_rows = projected[:, :, group + 1].astype(jnp.bfloat16)
        cache = jnp.stack(
            [key_rows.reshape(tokens_dev, -1), value_rows.reshape(tokens_dev, -1)], axis=1
        )
        kv_piece = lax.all_gather(cache.reshape(tokens_dev, -1), "expert", axis=0, tiled=True)
        key_count = kv_piece.shape[0]
        kv_piece = kv_piece.reshape(key_count, 2, kv_local, head_width)
        key_slots = jnp.arange(key_count, dtype=jnp.int32)
        ends = jnp.cumsum(lengths)
        seg_piece = jnp.sum((key_slots[:, None] >= ends[None, :]).astype(jnp.int32), axis=1)
        seg_piece = jnp.where(key_slots < ends[-1], seg_piece, -1)
        allowed = (segments[:, None] == seg_piece[None, :]) & (segments[:, None] >= 0) & (
            key_slots[None, :] <= slot_index[:, None]
        ) | (key_slots[None, :] == slot_index[:, None])
        scores = (
            jnp.einsum(
                "tagd,nad->tagn", queries, kv_piece[:, 0], preferred_element_type=jnp.float32
            )
            * scale
        )
        weights_full = jnp.where(allowed[:, None, None, :], jnp.exp(scores), 0.0)
        numerator = jnp.einsum(
            "tagn,nad->tagd",
            weights_full.astype(jnp.bfloat16),
            kv_piece[:, 1],
            preferred_element_type=jnp.float32,
        )
        numerator, denominator = (numerator, jnp.sum(weights_full, axis=-1))
        attended = (numerator / denominator[..., None]).astype(jnp.bfloat16).reshape(tokens_dev, -1)
        attended_all = lax.all_gather(attended, "expert", axis=0, tiled=True)
        attn_terms = lax.dot_general(
            attended_all, out_local, (((1,), (1,)), ((), ())), preferred_element_type=jnp.float32
        )
        attn_sum = terms_to_slots(attn_terms.astype(jnp.bfloat16)).astype(jnp.float32)
        after_attn = (incoming.astype(jnp.float32) + attn_sum).astype(jnp.bfloat16)
        moe_in = norm_rows(after_attn, ffn_gain[0], model_width)
        moe_rows = lax.all_gather(moe_in, "tensor", axis=1, tiled=True)
        moe_all = lax.all_gather(moe_rows, "expert", axis=0, tiled=True)
        shared_hidden = jnp.dot(
            moe_all,
            shared_in_cols.reshape(model_width, 2 * shared_cols),
            preferred_element_type=jnp.float32,
        )
        shared_act = (
            jax.nn.silu(shared_hidden[:, :shared_cols]) * shared_hidden[:, shared_cols:]
        ).astype(jnp.bfloat16)
        shared_act = lax.all_gather(shared_act, "expert", axis=1, tiled=True)
        shared_terms = lax.dot_general(
            shared_act,
            shared_down_local,
            (((1,), (1,)), ((), ())),
            preferred_element_type=jnp.float32,
        )
        shared_sum = terms_to_slots(shared_terms.astype(jnp.bfloat16))
        shared_out = lax.optimization_barrier(shared_sum).astype(jnp.float32)
        logits = lax.psum(
            jnp.dot(moe_in.astype(jnp.float32), router_weight[0], precision=lax.Precision.HIGHEST),
            "tensor",
        )
        expert_ids = jnp.arange(logits.shape[1], dtype=jnp.int32)
        picked = jnp.sum(
            jnp.where(choices[:, :, None] == expert_ids[None, None, :], logits[:, None, :], 0.0),
            axis=2,
        )
        raised = jnp.exp(picked)
        gate_weights = raised / jnp.sum(raised, axis=1, keepdims=True)
        flat_choice = choices.reshape(-1)
        onehot = (flat_choice[:, None] == expert_ids[None, :]).astype(jnp.int32)
        slot_rank = jnp.sum(onehot * (jnp.cumsum(onehot, axis=0) - onehot), axis=1)
        slot_ids = flat_choice * capacity + slot_rank
        choices_all = choices_every[:, micro_index]
        mine = jnp.any(choices_all == expert_id, axis=2)
        mine_rank = jnp.cumsum(mine.astype(jnp.int32), axis=1) - 1
        source_ids = jnp.broadcast_to(
            jnp.arange(experts_count, dtype=jnp.int32)[:, None], mine.shape
        )
        token_ids = jnp.broadcast_to(jnp.arange(tokens_dev, dtype=jnp.int32)[None, :], mine.shape)
        rank_at = jnp.where(mine, mine_rank, capacity)
        table = (
            jnp.zeros((experts_count, capacity), jnp.int32)
            .at[source_ids, rank_at]
            .set(source_ids * tokens_dev + token_ids, mode="drop")
        )
        filled = (
            jnp.zeros((experts_count, capacity), jnp.bool_)
            .at[source_ids, rank_at]
            .set(True, mode="drop")
        )
        incoming_rows = jnp.where(filled[..., None], moe_all[table], jnp.zeros((), jnp.bfloat16))
        returned = expert_path(incoming_rows, w_in_local, w_down_local)
        combined = returned.reshape(experts_count * capacity, columns)[slot_ids].astype(jnp.float32)
        combined = combined * gate_weights.reshape(-1)[:, None]
        moe_out = jnp.sum(combined.reshape(tokens_dev, top_count, columns), axis=1)
        output = (after_attn.astype(jnp.float32) + shared_out + moe_out).astype(jnp.bfloat16)
        output, cache = (output, cache)
        states = jnp.where(active, states.at[micro_index].set(output), states)
        caches = jnp.where(active, caches.at[micro_index].set(cache), caches)
        if tick_index + 1 < ticks:
            carried_rows = passed_along(output, "section", 1)
    return (states[None], caches[None])


def solution(mesh):
    placed = (
        P(None, "expert", "tensor"),
        P(None, "expert"),
        P(),
        P("section", None, "expert", None),
        P("section", "tensor"),
        P("section", "tensor"),
        P("section", "expert", "tensor", None),
        P("section", "expert", "tensor"),
        P("section", "expert", None, "tensor"),
        P("section", "expert", "tensor"),
        P("section", "tensor", None),
        P("section", "expert", None, None, "tensor"),
        P("section", "expert", "tensor", None),
    )
    return jax.shard_map(
        local,
        mesh=mesh,
        in_specs=placed,
        out_specs=(
            P("section", None, "expert", "tensor"),
            P("section", None, "expert", None, "tensor"),
        ),
        check_vma=False,
    )
```

```python
import jax
import jax.numpy as jnp
from jax import lax
from jax.sharding import PartitionSpec as P

HD = 128


NORM_EPS = 1e-05
ROPE_BASE = 500000.0


def passed_along(value, axis, steps):
    count = lax.axis_size(axis)
    leading, last = (max(0, -steps), min(count, count - steps))
    return lax.ppermute(value, axis, [(source, source + steps) for source in range(leading, last)])


def rotate_heads(values_in, positions):
    head_width = values_in.shape[-1]
    half_width = head_width // 2
    frequency = ROPE_BASE ** (-(jnp.arange(half_width, dtype=jnp.float32) * (2.0 / head_width)))
    angles = positions[:, None] * frequency[None, :]
    angles = angles.reshape((positions.shape[0],) + (1,) * (values_in.ndim - 2) + (half_width,))
    cosines = jnp.cos(angles)
    sines = jnp.sin(angles)
    first_half = values_in[..., :half_width]
    second_half = values_in[..., half_width:]
    return jnp.concatenate(
        [first_half * cosines - second_half * sines, second_half * cosines + first_half * sines],
        axis=-1,
    )


def norm_rows(values_in, gain_row, model_width):
    widened = values_in.astype(jnp.float32)
    squares = lax.psum(jnp.sum(widened * widened, axis=-1), "tensor")
    return (widened * lax.rsqrt(squares / model_width + NORM_EPS)[:, None] * gain_row).astype(
        jnp.bfloat16
    )


def gather_slots(rows):
    count = lax.axis_size("expert")
    half = rows.shape[1] // 2
    first = lax.all_gather(rows[:, :half], "expert", axis=0, tiled=True)
    copies = jnp.broadcast_to(rows[None, :, half:], (count,) + rows[:, half:].shape)
    second = lax.all_to_all(copies, "expert", split_axis=0, concat_axis=0, tiled=True)
    return jnp.concatenate([first, second.reshape(first.shape[0], -1)], axis=1)


def terms_to_slots(terms):
    by_slot = lax.all_to_all(terms, "expert", split_axis=0, concat_axis=1, tiled=True)
    return lax.psum_scatter(by_slot, "tensor", scatter_dimension=1, tiled=True)


def expert_path(full_rows, w_in_local, w_down_local):
    sources, slot_count, model_width = full_rows.shape
    local_width = w_down_local.shape[0]
    hidden = jnp.dot(
        full_rows.reshape(sources * slot_count, model_width),
        w_in_local.reshape(model_width, 2 * local_width),
        preferred_element_type=jnp.float32,
    )
    activated = (jax.nn.silu(hidden[:, :local_width]) * hidden[:, local_width:]).astype(
        jnp.bfloat16
    )
    partial_value = jnp.dot(activated, w_down_local, preferred_element_type=jnp.float32)
    partial_value = partial_value.reshape(sources, slot_count, model_width)
    summed = lax.psum_scatter(
        partial_value.astype(jnp.bfloat16), "tensor", scatter_dimension=2, tiled=True
    )
    return lax.all_to_all(summed, "expert", split_axis=0, concat_axis=0, tiled=True)


def local(
    hidden_in,
    segment_ids,
    prompt_lengths,
    expert_choice,
    attn_gain,
    ffn_gain,
    w_qkv,
    w_out,
    w_shared_in,
    w_shared_down,
    router_weight,
    w_in,
    w_down,
):
    sections = lax.axis_size("section")
    section_id = lax.axis_index("section")
    experts_count = lax.axis_size("expert")
    expert_id = lax.axis_index("expert")
    micro_count, tokens_dev, columns = hidden_in.shape
    qkv_full = lax.all_gather(w_qkv[0], "expert", axis=0, tiled=True)
    out_local = w_out[0]
    shared_down_local = w_shared_down[0]
    shared_in_cols = lax.all_to_all(w_shared_in[0], "expert", split_axis=2, concat_axis=0, tiled=True)
    choices_every = lax.all_gather(expert_choice[0], "expert", axis=0, tiled=False)
    qkv_full, shared_in_cols, choices_every = lax.optimization_barrier(
        (qkv_full, shared_in_cols, choices_every)
    )
    model_width, kv_local, group_cols = qkv_full.shape
    shared_cols = shared_in_cols.shape[2]
    head_width = HD
    group = group_cols // head_width - 2
    scale = head_width ** (-0.5)
    top_count = expert_choice.shape[-1]
    capacity = 5 * tokens_dev * top_count // (4 * experts_count)
    slot_index = expert_id * tokens_dev + jnp.arange(tokens_dev, dtype=jnp.int32)
    w_in_local = w_in[0, 0]
    w_down_local = w_down[0, 0]
    carried_rows = jnp.zeros((tokens_dev, columns), jnp.bfloat16)
    states = jnp.zeros((micro_count, tokens_dev, columns), jnp.bfloat16)
    caches = jnp.zeros((micro_count, tokens_dev, 2, kv_local * head_width), jnp.bfloat16)
    ticks = micro_count + sections - 1
    for tick_index in range(ticks):
        micro_index = jnp.clip(tick_index - section_id, 0, micro_count - 1)
        incoming = jnp.where(
            section_id == 0, hidden_in[min(tick_index, micro_count - 1)], carried_rows
        )
        active = (tick_index - section_id >= 0) & (tick_index - section_id < micro_count)
        segments = segment_ids[micro_index]
        lengths = prompt_lengths[micro_index]
        choices = expert_choice[0, micro_index]
        starts = jnp.cumsum(lengths) - lengths
        member = segments[:, None] == jnp.arange(lengths.shape[0], dtype=jnp.int32)[None, :]
        first_slot = jnp.sum(jnp.where(member, starts[None, :], 0), axis=1)
        positions = jnp.where(segments >= 0, slot_index - first_slot, 0).astype(jnp.float32)
        normed = norm_rows(incoming, attn_gain[0], model_width)
        normed_full = lax.all_gather(normed, "tensor", axis=1, tiled=True)
        projected = jnp.dot(
            normed_full, qkv_full.reshape(model_width, -1), preferred_element_type=jnp.float32
        )
        projected = projected.reshape(tokens_dev, kv_local, group + 2, head_width)
        queries = rotate_heads(projected[:, :, :group], positions).astype(jnp.bfloat16)
        key_rows = rotate_heads(projected[:, :, group], positions).astype(jnp.bfloat16)
        value_rows = projected[:, :, group + 1].astype(jnp.bfloat16)
        cache = jnp.stack(
            [key_rows.reshape(tokens_dev, -1), value_rows.reshape(tokens_dev, -1)], axis=1
        )
        kv_piece = lax.all_gather(cache.reshape(tokens_dev, -1), "expert", axis=0, tiled=True)
        key_count = kv_piece.shape[0]
        kv_piece = kv_piece.reshape(key_count, 2, kv_local, head_width)
        key_slots = jnp.arange(key_count, dtype=jnp.int32)
        ends = jnp.cumsum(lengths)
        seg_piece = jnp.sum((key_slots[:, None] >= ends[None, :]).astype(jnp.int32), axis=1)
        seg_piece = jnp.where(key_slots < ends[-1], seg_piece, -1)
        allowed = (segments[:, None] == seg_piece[None, :]) & (segments[:, None] >= 0) & (
            key_slots[None, :] <= slot_index[:, None]
        ) | (key_slots[None, :] == slot_index[:, None])
        scores = (
            jnp.einsum(
                "tagd,nad->tagn", queries, kv_piece[:, 0], preferred_element_type=jnp.float32
            )
            * scale
        )
        weights_full = jnp.where(allowed[:, None, None, :], jnp.exp(scores), 0.0)
        numerator = jnp.einsum(
            "tagn,nad->tagd",
            weights_full.astype(jnp.bfloat16),
            kv_piece[:, 1],
            preferred_element_type=jnp.float32,
        )
        numerator, denominator = (numerator, jnp.sum(weights_full, axis=-1))
        attended = (numerator / denominator[..., None]).astype(jnp.bfloat16).reshape(tokens_dev, -1)
        attended_all = gather_slots(attended)
        attn_terms = lax.dot_general(
            attended_all, out_local, (((1,), (1,)), ((), ())), preferred_element_type=jnp.float32
        )
        attn_sum = terms_to_slots(attn_terms.astype(jnp.bfloat16)).astype(jnp.float32)
        after_attn = (incoming.astype(jnp.float32) + attn_sum).astype(jnp.bfloat16)
        moe_in = norm_rows(after_attn, ffn_gain[0], model_width)
        moe_rows = lax.all_gather(moe_in, "tensor", axis=1, tiled=True)
        moe_all = gather_slots(moe_rows)
        shared_hidden = jnp.dot(
            moe_all,
            shared_in_cols.reshape(model_width, 2 * shared_cols),
            preferred_element_type=jnp.float32,
        )
        shared_act = (
            jax.nn.silu(shared_hidden[:, :shared_cols]) * shared_hidden[:, shared_cols:]
        ).astype(jnp.bfloat16)
        shared_act = lax.all_gather(shared_act, "expert", axis=1, tiled=True)
        shared_terms = lax.dot_general(
            shared_act,
            shared_down_local,
            (((1,), (1,)), ((), ())),
            preferred_element_type=jnp.float32,
        )
        shared_sum = terms_to_slots(shared_terms.astype(jnp.bfloat16))
        shared_out = lax.optimization_barrier(shared_sum).astype(jnp.float32)
        logits = lax.psum(
            jnp.dot(moe_in.astype(jnp.float32), router_weight[0], precision=lax.Precision.HIGHEST),
            "tensor",
        )
        expert_ids = jnp.arange(logits.shape[1], dtype=jnp.int32)
        picked = jnp.sum(
            jnp.where(choices[:, :, None] == expert_ids[None, None, :], logits[:, None, :], 0.0),
            axis=2,
        )
        raised = jnp.exp(picked)
        gate_weights = raised / jnp.sum(raised, axis=1, keepdims=True)
        flat_choice = choices.reshape(-1)
        onehot = (flat_choice[:, None] == expert_ids[None, :]).astype(jnp.int32)
        slot_rank = jnp.sum(onehot * (jnp.cumsum(onehot, axis=0) - onehot), axis=1)
        slot_ids = flat_choice * capacity + slot_rank
        choices_all = choices_every[:, micro_index]
        mine = jnp.any(choices_all == expert_id, axis=2)
        mine_rank = jnp.cumsum(mine.astype(jnp.int32), axis=1) - 1
        source_ids = jnp.broadcast_to(
            jnp.arange(experts_count, dtype=jnp.int32)[:, None], mine.shape
        )
        token_ids = jnp.broadcast_to(jnp.arange(tokens_dev, dtype=jnp.int32)[None, :], mine.shape)
        rank_at = jnp.where(mine, mine_rank, capacity)
        table = (
            jnp.zeros((experts_count, capacity), jnp.int32)
            .at[source_ids, rank_at]
            .set(source_ids * tokens_dev + token_ids, mode="drop")
        )
        filled = (
            jnp.zeros((experts_count, capacity), jnp.bool_)
            .at[source_ids, rank_at]
            .set(True, mode="drop")
        )
        incoming_rows = jnp.where(filled[..., None], moe_all[table], jnp.zeros((), jnp.bfloat16))
        returned = expert_path(incoming_rows, w_in_local, w_down_local)
        combined = returned.reshape(experts_count * capacity, columns)[slot_ids].astype(jnp.float32)
        combined = combined * gate_weights.reshape(-1)[:, None]
        moe_out = jnp.sum(combined.reshape(tokens_dev, top_count, columns), axis=1)
        output = (after_attn.astype(jnp.float32) + shared_out + moe_out).astype(jnp.bfloat16)
        output, cache = (output, cache)
        states = jnp.where(active, states.at[micro_index].set(output), states)
        caches = jnp.where(active, caches.at[micro_index].set(cache), caches)
        if tick_index + 1 < ticks:
            carried_rows = passed_along(output, "section", 1)
    return (states[None], caches[None])


def solution(mesh):
    placed = (
        P(None, "expert", "tensor"),
        P(None, "expert"),
        P(),
        P("section", None, "expert", None),
        P("section", "tensor"),
        P("section", "tensor"),
        P("section", "expert", "tensor", None),
        P("section", "expert", "tensor"),
        P("section", "expert", None, "tensor"),
        P("section", "expert", "tensor"),
        P("section", "tensor", None),
        P("section", "expert", None, None, "tensor"),
        P("section", "expert", "tensor", None),
    )
    return jax.shard_map(
        local,
        mesh=mesh,
        in_specs=placed,
        out_specs=(
            P("section", None, "expert", "tensor"),
            P("section", None, "expert", None, "tensor"),
        ),
        check_vma=False,
    )
```

```python
import functools

import jax
import jax.numpy as jnp
from jax import lax
from jax.sharding import PartitionSpec as P

HD = 128


NORM_EPS = 1e-05
ROPE_BASE = 500000.0


def passed_along(value, axis, steps):
    count = lax.axis_size(axis)
    leading, last = (max(0, -steps), min(count, count - steps))
    return lax.ppermute(value, axis, [(source, source + steps) for source in range(leading, last)])


def rotate_heads(values_in, positions):
    head_width = values_in.shape[-1]
    half_width = head_width // 2
    frequency = ROPE_BASE ** (-(jnp.arange(half_width, dtype=jnp.float32) * (2.0 / head_width)))
    angles = positions[:, None] * frequency[None, :]
    angles = angles.reshape((positions.shape[0],) + (1,) * (values_in.ndim - 2) + (half_width,))
    cosines = jnp.cos(angles)
    sines = jnp.sin(angles)
    first_half = values_in[..., :half_width]
    second_half = values_in[..., half_width:]
    return jnp.concatenate(
        [first_half * cosines - second_half * sines, second_half * cosines + first_half * sines],
        axis=-1,
    )


def norm_rows(values_in, gain_row, model_width):
    widened = values_in.astype(jnp.float32)
    squares = lax.psum(jnp.sum(widened * widened, axis=-1), "tensor")
    return (widened * lax.rsqrt(squares / model_width + NORM_EPS)[:, None] * gain_row).astype(
        jnp.bfloat16
    )


def swap_cores(value):
    count = lax.axis_size("section")
    return lax.ppermute(value, "section", [(source, (source + 1) % count) for source in range(count)])


def paired_gather(value, axis, split_axis, active):
    value = jnp.where(active, value, swap_cores(value))
    first, second = jnp.split(value, 2, axis=split_axis)
    gathered = lax.all_gather(jnp.where(active, first, second), "expert", axis=axis, tiled=True)
    theirs = swap_cores(gathered)
    lead = jnp.where(active, gathered, theirs)
    trail = jnp.where(active, theirs, gathered)
    return jnp.concatenate([lead, trail], axis=split_axis)


def terms_to_slots(terms):
    by_slot = lax.all_to_all(terms, "expert", split_axis=0, concat_axis=1, tiled=True)
    return lax.psum_scatter(by_slot, "tensor", scatter_dimension=1, tiled=True)


def expert_path(full_rows, w_in_local, w_down_local):
    sources, slot_count, model_width = full_rows.shape
    local_width = w_down_local.shape[0]
    hidden = jnp.dot(
        full_rows.reshape(sources * slot_count, model_width),
        w_in_local.reshape(model_width, 2 * local_width),
        preferred_element_type=jnp.float32,
    )
    activated = (jax.nn.silu(hidden[:, :local_width]) * hidden[:, local_width:]).astype(
        jnp.bfloat16
    )
    partial_value = jnp.dot(activated, w_down_local, preferred_element_type=jnp.float32)
    partial_value = partial_value.reshape(sources, slot_count, model_width)
    summed = lax.psum_scatter(
        partial_value.astype(jnp.bfloat16), "tensor", scatter_dimension=2, tiled=True
    )
    return lax.all_to_all(summed, "expert", split_axis=0, concat_axis=0, tiled=True)


def local(
    hidden_in,
    segment_ids,
    prompt_lengths,
    expert_choice,
    attn_gain,
    ffn_gain,
    w_qkv,
    w_out,
    w_shared_in,
    w_shared_down,
    router_weight,
    w_in,
    w_down,
):
    sections = lax.axis_size("section")
    section_id = lax.axis_index("section")
    experts_count = lax.axis_size("expert")
    expert_id = lax.axis_index("expert")
    micro_count, tokens_dev, columns = hidden_in.shape
    qkv_full = lax.all_gather(w_qkv[0], "expert", axis=0, tiled=True)
    out_local = w_out[0]
    shared_down_local = w_shared_down[0]
    shared_in_cols = lax.all_to_all(w_shared_in[0], "expert", split_axis=2, concat_axis=0, tiled=True)
    choices_every = lax.all_gather(expert_choice[0], "expert", axis=0, tiled=False)
    qkv_full, shared_in_cols, choices_every = lax.optimization_barrier(
        (qkv_full, shared_in_cols, choices_every)
    )
    model_width, kv_local, group_cols = qkv_full.shape
    shared_cols = shared_in_cols.shape[2]
    head_width = HD
    group = group_cols // head_width - 2
    scale = head_width ** (-0.5)
    top_count = expert_choice.shape[-1]
    capacity = 5 * tokens_dev * top_count // (4 * experts_count)
    slot_index = expert_id * tokens_dev + jnp.arange(tokens_dev, dtype=jnp.int32)
    w_in_local = w_in[0, 0]
    w_down_local = w_down[0, 0]
    carried_rows = jnp.zeros((tokens_dev, columns), jnp.bfloat16)
    states = jnp.zeros((micro_count, tokens_dev, columns), jnp.bfloat16)
    caches = jnp.zeros((micro_count, tokens_dev, 2, kv_local * head_width), jnp.bfloat16)
    ticks = micro_count + sections - 1
    for tick_index in range(ticks):
        micro_index = jnp.clip(tick_index - section_id, 0, micro_count - 1)
        incoming = jnp.where(
            section_id == 0, hidden_in[min(tick_index, micro_count - 1)], carried_rows
        )
        active = (tick_index - section_id >= 0) & (tick_index - section_id < micro_count)
        if micro_count == 1 and sections == 2:
            expert_gather = functools.partial(paired_gather, active=active)
        else:
            def expert_gather(value, axis, split_axis):
                return lax.all_gather(value, "expert", axis=axis, tiled=True)
        segments = segment_ids[micro_index]
        lengths = prompt_lengths[micro_index]
        choices = expert_choice[0, micro_index]
        starts = jnp.cumsum(lengths) - lengths
        member = segments[:, None] == jnp.arange(lengths.shape[0], dtype=jnp.int32)[None, :]
        first_slot = jnp.sum(jnp.where(member, starts[None, :], 0), axis=1)
        positions = jnp.where(segments >= 0, slot_index - first_slot, 0).astype(jnp.float32)
        normed = norm_rows(incoming, attn_gain[0], model_width)
        normed_full = lax.all_gather(normed, "tensor", axis=1, tiled=True)
        projected = jnp.dot(
            normed_full, qkv_full.reshape(model_width, -1), preferred_element_type=jnp.float32
        )
        projected = projected.reshape(tokens_dev, kv_local, group + 2, head_width)
        queries = rotate_heads(projected[:, :, :group], positions).astype(jnp.bfloat16)
        key_rows = rotate_heads(projected[:, :, group], positions).astype(jnp.bfloat16)
        value_rows = projected[:, :, group + 1].astype(jnp.bfloat16)
        cache = jnp.stack(
            [key_rows.reshape(tokens_dev, -1), value_rows.reshape(tokens_dev, -1)], axis=1
        )
        kv_piece = expert_gather(cache.reshape(tokens_dev, -1), 0, 1)
        key_count = kv_piece.shape[0]
        kv_piece = kv_piece.reshape(key_count, 2, kv_local, head_width)
        key_slots = jnp.arange(key_count, dtype=jnp.int32)
        ends = jnp.cumsum(lengths)
        seg_piece = jnp.sum((key_slots[:, None] >= ends[None, :]).astype(jnp.int32), axis=1)
        seg_piece = jnp.where(key_slots < ends[-1], seg_piece, -1)
        allowed = (segments[:, None] == seg_piece[None, :]) & (segments[:, None] >= 0) & (
            key_slots[None, :] <= slot_index[:, None]
        ) | (key_slots[None, :] == slot_index[:, None])
        scores = (
            jnp.einsum(
                "tagd,nad->tagn", queries, kv_piece[:, 0], preferred_element_type=jnp.float32
            )
            * scale
        )
        weights_full = jnp.where(allowed[:, None, None, :], jnp.exp(scores), 0.0)
        numerator = jnp.einsum(
            "tagn,nad->tagd",
            weights_full.astype(jnp.bfloat16),
            kv_piece[:, 1],
            preferred_element_type=jnp.float32,
        )
        numerator, denominator = (numerator, jnp.sum(weights_full, axis=-1))
        attended = (numerator / denominator[..., None]).astype(jnp.bfloat16).reshape(tokens_dev, -1)
        attended_all = expert_gather(attended, 0, 1)
        attn_terms = lax.dot_general(
            attended_all, out_local, (((1,), (1,)), ((), ())), preferred_element_type=jnp.float32
        )
        attn_sum = terms_to_slots(attn_terms.astype(jnp.bfloat16)).astype(jnp.float32)
        after_attn = (incoming.astype(jnp.float32) + attn_sum).astype(jnp.bfloat16)
        moe_in = norm_rows(after_attn, ffn_gain[0], model_width)
        moe_rows = lax.all_gather(moe_in, "tensor", axis=1, tiled=True)
        moe_all = expert_gather(moe_rows, 0, 1)
        shared_hidden = jnp.dot(
            moe_all,
            shared_in_cols.reshape(model_width, 2 * shared_cols),
            preferred_element_type=jnp.float32,
        )
        shared_act = (
            jax.nn.silu(shared_hidden[:, :shared_cols]) * shared_hidden[:, shared_cols:]
        ).astype(jnp.bfloat16)
        shared_act = expert_gather(shared_act, 1, 0)
        shared_terms = lax.dot_general(
            shared_act,
            shared_down_local,
            (((1,), (1,)), ((), ())),
            preferred_element_type=jnp.float32,
        )
        shared_sum = terms_to_slots(shared_terms.astype(jnp.bfloat16))
        shared_out = lax.optimization_barrier(shared_sum).astype(jnp.float32)
        logits = lax.psum(
            jnp.dot(moe_in.astype(jnp.float32), router_weight[0], precision=lax.Precision.HIGHEST),
            "tensor",
        )
        expert_ids = jnp.arange(logits.shape[1], dtype=jnp.int32)
        picked = jnp.sum(
            jnp.where(choices[:, :, None] == expert_ids[None, None, :], logits[:, None, :], 0.0),
            axis=2,
        )
        raised = jnp.exp(picked)
        gate_weights = raised / jnp.sum(raised, axis=1, keepdims=True)
        flat_choice = choices.reshape(-1)
        onehot = (flat_choice[:, None] == expert_ids[None, :]).astype(jnp.int32)
        slot_rank = jnp.sum(onehot * (jnp.cumsum(onehot, axis=0) - onehot), axis=1)
        slot_ids = flat_choice * capacity + slot_rank
        choices_all = choices_every[:, micro_index]
        mine = jnp.any(choices_all == expert_id, axis=2)
        mine_rank = jnp.cumsum(mine.astype(jnp.int32), axis=1) - 1
        source_ids = jnp.broadcast_to(
            jnp.arange(experts_count, dtype=jnp.int32)[:, None], mine.shape
        )
        token_ids = jnp.broadcast_to(jnp.arange(tokens_dev, dtype=jnp.int32)[None, :], mine.shape)
        rank_at = jnp.where(mine, mine_rank, capacity)
        table = (
            jnp.zeros((experts_count, capacity), jnp.int32)
            .at[source_ids, rank_at]
            .set(source_ids * tokens_dev + token_ids, mode="drop")
        )
        filled = (
            jnp.zeros((experts_count, capacity), jnp.bool_)
            .at[source_ids, rank_at]
            .set(True, mode="drop")
        )
        incoming_rows = jnp.where(filled[..., None], moe_all[table], jnp.zeros((), jnp.bfloat16))
        returned = expert_path(incoming_rows, w_in_local, w_down_local)
        combined = returned.reshape(experts_count * capacity, columns)[slot_ids].astype(jnp.float32)
        combined = combined * gate_weights.reshape(-1)[:, None]
        moe_out = jnp.sum(combined.reshape(tokens_dev, top_count, columns), axis=1)
        output = (after_attn.astype(jnp.float32) + shared_out + moe_out).astype(jnp.bfloat16)
        output, cache = (output, cache)
        states = jnp.where(active, states.at[micro_index].set(output), states)
        caches = jnp.where(active, caches.at[micro_index].set(cache), caches)
        if tick_index + 1 < ticks:
            carried_rows = passed_along(output, "section", 1)
    return (states[None], caches[None])


def solution(mesh):
    placed = (
        P(None, "expert", "tensor"),
        P(None, "expert"),
        P(),
        P("section", None, "expert", None),
        P("section", "tensor"),
        P("section", "tensor"),
        P("section", "expert", "tensor", None),
        P("section", "expert", "tensor"),
        P("section", "expert", None, "tensor"),
        P("section", "expert", "tensor"),
        P("section", "tensor", None),
        P("section", "expert", None, None, "tensor"),
        P("section", "expert", "tensor", None),
    )
    return jax.shard_map(
        local,
        mesh=mesh,
        in_specs=placed,
        out_specs=(
            P("section", None, "expert", "tensor"),
            P("section", None, "expert", None, "tensor"),
        ),
        check_vma=False,
    )
```

```python
import functools

import jax
import jax.numpy as jnp
from jax import lax
from jax.sharding import PartitionSpec as P

HD = 128


NORM_EPS = 1e-05
ROPE_BASE = 500000.0


def passed_along(value, axis, steps):
    count = lax.axis_size(axis)
    leading, last = (max(0, -steps), min(count, count - steps))
    return lax.ppermute(value, axis, [(source, source + steps) for source in range(leading, last)])


def rotate_heads(values_in, positions):
    head_width = values_in.shape[-1]
    half_width = head_width // 2
    frequency = ROPE_BASE ** (-(jnp.arange(half_width, dtype=jnp.float32) * (2.0 / head_width)))
    angles = positions[:, None] * frequency[None, :]
    angles = angles.reshape((positions.shape[0],) + (1,) * (values_in.ndim - 2) + (half_width,))
    cosines = jnp.cos(angles)
    sines = jnp.sin(angles)
    first_half = values_in[..., :half_width]
    second_half = values_in[..., half_width:]
    return jnp.concatenate(
        [first_half * cosines - second_half * sines, second_half * cosines + first_half * sines],
        axis=-1,
    )


def norm_full_rows(values_in, gain_full):
    widened = lax.all_gather(values_in, "tensor", axis=1, tiled=True).astype(jnp.float32)
    squares = jnp.mean(widened * widened, axis=-1)
    return (widened * lax.rsqrt(squares + NORM_EPS)[:, None] * gain_full).astype(jnp.bfloat16)


def swap_cores(value):
    count = lax.axis_size("section")
    return lax.ppermute(value, "section", [(source, (source + 1) % count) for source in range(count)])


def paired_gather(value, axis, split_axis, active):
    value = jnp.where(active, value, swap_cores(value))
    first, second = jnp.split(value, 2, axis=split_axis)
    gathered = lax.all_gather(jnp.where(active, first, second), "expert", axis=axis, tiled=True)
    theirs = swap_cores(gathered)
    lead = jnp.where(active, gathered, theirs)
    trail = jnp.where(active, theirs, gathered)
    return jnp.concatenate([lead, trail], axis=split_axis)


def terms_to_slots(terms):
    by_slot = lax.all_to_all(terms, "expert", split_axis=0, concat_axis=1, tiled=True)
    return lax.psum_scatter(by_slot, "tensor", scatter_dimension=1, tiled=True)


def expert_path(full_rows, w_in_local, w_down_local):
    sources, slot_count, model_width = full_rows.shape
    local_width = w_down_local.shape[0]
    hidden = jnp.dot(
        full_rows.reshape(sources * slot_count, model_width),
        w_in_local.reshape(model_width, 2 * local_width),
        preferred_element_type=jnp.float32,
    )
    activated = (jax.nn.silu(hidden[:, :local_width]) * hidden[:, local_width:]).astype(
        jnp.bfloat16
    )
    partial_value = jnp.dot(activated, w_down_local, preferred_element_type=jnp.float32)
    partial_value = partial_value.reshape(sources, slot_count, model_width)
    summed = lax.psum_scatter(
        partial_value.astype(jnp.bfloat16), "tensor", scatter_dimension=2, tiled=True
    )
    return lax.all_to_all(summed, "expert", split_axis=0, concat_axis=0, tiled=True)


def local(
    hidden_in,
    segment_ids,
    prompt_lengths,
    expert_choice,
    attn_gain,
    ffn_gain,
    w_qkv,
    w_out,
    w_shared_in,
    w_shared_down,
    router_weight,
    w_in,
    w_down,
):
    sections = lax.axis_size("section")
    section_id = lax.axis_index("section")
    experts_count = lax.axis_size("expert")
    expert_id = lax.axis_index("expert")
    micro_count, tokens_dev, columns = hidden_in.shape
    qkv_full = lax.all_gather(w_qkv[0], "expert", axis=0, tiled=True)
    out_local = w_out[0]
    shared_down_local = w_shared_down[0]
    shared_in_cols = lax.all_to_all(w_shared_in[0], "expert", split_axis=2, concat_axis=0, tiled=True)
    choices_every = lax.all_gather(expert_choice[0], "expert", axis=0, tiled=False)
    router_full = lax.all_gather(router_weight[0], "tensor", axis=0, tiled=True)
    attn_gain_full = lax.all_gather(attn_gain[0], "tensor", axis=0, tiled=True)
    ffn_gain_full = lax.all_gather(ffn_gain[0], "tensor", axis=0, tiled=True)
    qkv_full, shared_in_cols, choices_every, router_full, attn_gain_full, ffn_gain_full = (
        lax.optimization_barrier(
            (qkv_full, shared_in_cols, choices_every, router_full, attn_gain_full, ffn_gain_full)
        )
    )
    model_width, kv_local, group_cols = qkv_full.shape
    shared_cols = shared_in_cols.shape[2]
    head_width = HD
    group = group_cols // head_width - 2
    scale = head_width ** (-0.5)
    top_count = expert_choice.shape[-1]
    capacity = 5 * tokens_dev * top_count // (4 * experts_count)
    slot_index = expert_id * tokens_dev + jnp.arange(tokens_dev, dtype=jnp.int32)
    w_in_local = w_in[0, 0]
    w_down_local = w_down[0, 0]
    carried_rows = jnp.zeros((tokens_dev, columns), jnp.bfloat16)
    states = jnp.zeros((micro_count, tokens_dev, columns), jnp.bfloat16)
    caches = jnp.zeros((micro_count, tokens_dev, 2, kv_local * head_width), jnp.bfloat16)
    ticks = micro_count + sections - 1
    for tick_index in range(ticks):
        micro_index = jnp.clip(tick_index - section_id, 0, micro_count - 1)
        incoming = jnp.where(
            section_id == 0, hidden_in[min(tick_index, micro_count - 1)], carried_rows
        )
        active = (tick_index - section_id >= 0) & (tick_index - section_id < micro_count)
        if micro_count == 1 and sections == 2:
            expert_gather = functools.partial(paired_gather, active=active)
        else:
            def expert_gather(value, axis, split_axis):
                return lax.all_gather(value, "expert", axis=axis, tiled=True)
        segments = segment_ids[micro_index]
        lengths = prompt_lengths[micro_index]
        choices = expert_choice[0, micro_index]
        starts = jnp.cumsum(lengths) - lengths
        member = segments[:, None] == jnp.arange(lengths.shape[0], dtype=jnp.int32)[None, :]
        first_slot = jnp.sum(jnp.where(member, starts[None, :], 0), axis=1)
        positions = jnp.where(segments >= 0, slot_index - first_slot, 0).astype(jnp.float32)
        normed_full = norm_full_rows(incoming, attn_gain_full)
        projected = jnp.dot(
            normed_full, qkv_full.reshape(model_width, -1), preferred_element_type=jnp.float32
        )
        projected = projected.reshape(tokens_dev, kv_local, group + 2, head_width)
        queries = rotate_heads(projected[:, :, :group], positions).astype(jnp.bfloat16)
        key_rows = rotate_heads(projected[:, :, group], positions).astype(jnp.bfloat16)
        value_rows = projected[:, :, group + 1].astype(jnp.bfloat16)
        cache = jnp.stack(
            [key_rows.reshape(tokens_dev, -1), value_rows.reshape(tokens_dev, -1)], axis=1
        )
        kv_piece = expert_gather(cache.reshape(tokens_dev, -1), 0, 1)
        key_count = kv_piece.shape[0]
        kv_piece = kv_piece.reshape(key_count, 2, kv_local, head_width)
        key_slots = jnp.arange(key_count, dtype=jnp.int32)
        ends = jnp.cumsum(lengths)
        seg_piece = jnp.sum((key_slots[:, None] >= ends[None, :]).astype(jnp.int32), axis=1)
        seg_piece = jnp.where(key_slots < ends[-1], seg_piece, -1)
        allowed = (segments[:, None] == seg_piece[None, :]) & (segments[:, None] >= 0) & (
            key_slots[None, :] <= slot_index[:, None]
        ) | (key_slots[None, :] == slot_index[:, None])
        scores = (
            jnp.einsum(
                "tagd,nad->tagn", queries, kv_piece[:, 0], preferred_element_type=jnp.float32
            )
            * scale
        )
        weights_full = jnp.where(allowed[:, None, None, :], jnp.exp(scores), 0.0)
        numerator = jnp.einsum(
            "tagn,nad->tagd",
            weights_full.astype(jnp.bfloat16),
            kv_piece[:, 1],
            preferred_element_type=jnp.float32,
        )
        numerator, denominator = (numerator, jnp.sum(weights_full, axis=-1))
        attended = (numerator / denominator[..., None]).astype(jnp.bfloat16).reshape(tokens_dev, -1)
        attended_all = expert_gather(attended, 0, 1)
        attn_terms = lax.dot_general(
            attended_all, out_local, (((1,), (1,)), ((), ())), preferred_element_type=jnp.float32
        )
        attn_sum = terms_to_slots(attn_terms.astype(jnp.bfloat16)).astype(jnp.float32)
        after_attn = (incoming.astype(jnp.float32) + attn_sum).astype(jnp.bfloat16)
        moe_rows = norm_full_rows(after_attn, ffn_gain_full)
        moe_all = expert_gather(moe_rows, 0, 1)
        shared_hidden = jnp.dot(
            moe_all,
            shared_in_cols.reshape(model_width, 2 * shared_cols),
            preferred_element_type=jnp.float32,
        )
        shared_act = (
            jax.nn.silu(shared_hidden[:, :shared_cols]) * shared_hidden[:, shared_cols:]
        ).astype(jnp.bfloat16)
        shared_act = expert_gather(shared_act, 1, 0)
        shared_terms = lax.dot_general(
            shared_act,
            shared_down_local,
            (((1,), (1,)), ((), ())),
            preferred_element_type=jnp.float32,
        )
        shared_sum = terms_to_slots(shared_terms.astype(jnp.bfloat16))
        shared_out = lax.optimization_barrier(shared_sum).astype(jnp.float32)
        logits = jnp.dot(
            moe_rows.astype(jnp.float32), router_full, precision=lax.Precision.HIGHEST
        )
        expert_ids = jnp.arange(logits.shape[1], dtype=jnp.int32)
        picked = jnp.sum(
            jnp.where(choices[:, :, None] == expert_ids[None, None, :], logits[:, None, :], 0.0),
            axis=2,
        )
        raised = jnp.exp(picked)
        gate_weights = raised / jnp.sum(raised, axis=1, keepdims=True)
        flat_choice = choices.reshape(-1)
        onehot = (flat_choice[:, None] == expert_ids[None, :]).astype(jnp.int32)
        slot_rank = jnp.sum(onehot * (jnp.cumsum(onehot, axis=0) - onehot), axis=1)
        slot_ids = flat_choice * capacity + slot_rank
        choices_all = choices_every[:, micro_index]
        mine = jnp.any(choices_all == expert_id, axis=2)
        mine_rank = jnp.cumsum(mine.astype(jnp.int32), axis=1) - 1
        source_ids = jnp.broadcast_to(
            jnp.arange(experts_count, dtype=jnp.int32)[:, None], mine.shape
        )
        token_ids = jnp.broadcast_to(jnp.arange(tokens_dev, dtype=jnp.int32)[None, :], mine.shape)
        rank_at = jnp.where(mine, mine_rank, capacity)
        table = (
            jnp.zeros((experts_count, capacity), jnp.int32)
            .at[source_ids, rank_at]
            .set(source_ids * tokens_dev + token_ids, mode="drop")
        )
        filled = (
            jnp.zeros((experts_count, capacity), jnp.bool_)
            .at[source_ids, rank_at]
            .set(True, mode="drop")
        )
        incoming_rows = jnp.where(filled[..., None], moe_all[table], jnp.zeros((), jnp.bfloat16))
        returned = expert_path(incoming_rows, w_in_local, w_down_local)
        combined = returned.reshape(experts_count * capacity, columns)[slot_ids].astype(jnp.float32)
        combined = combined * gate_weights.reshape(-1)[:, None]
        moe_out = jnp.sum(combined.reshape(tokens_dev, top_count, columns), axis=1)
        output = (after_attn.astype(jnp.float32) + shared_out + moe_out).astype(jnp.bfloat16)
        output, cache = (output, cache)
        states = jnp.where(active, states.at[micro_index].set(output), states)
        caches = jnp.where(active, caches.at[micro_index].set(cache), caches)
        if tick_index + 1 < ticks:
            carried_rows = passed_along(output, "section", 1)
    return (states[None], caches[None])


def solution(mesh):
    placed = (
        P(None, "expert", "tensor"),
        P(None, "expert"),
        P(),
        P("section", None, "expert", None),
        P("section", "tensor"),
        P("section", "tensor"),
        P("section", "expert", "tensor", None),
        P("section", "expert", "tensor"),
        P("section", "expert", None, "tensor"),
        P("section", "expert", "tensor"),
        P("section", "tensor", None),
        P("section", "expert", None, None, "tensor"),
        P("section", "expert", "tensor", None),
    )
    return jax.shard_map(
        local,
        mesh=mesh,
        in_specs=placed,
        out_specs=(
            P("section", None, "expert", "tensor"),
            P("section", None, "expert", None, "tensor"),
        ),
        check_vma=False,
    )
```

```python
import functools

import jax
import jax.numpy as jnp
from jax import lax
from jax.sharding import PartitionSpec as P

HD = 128


NORM_EPS = 1e-05
ROPE_BASE = 500000.0


def passed_along(value, axis, steps):
    count = lax.axis_size(axis)
    leading, last = (max(0, -steps), min(count, count - steps))
    return lax.ppermute(value, axis, [(source, source + steps) for source in range(leading, last)])


def rotate_heads(values_in, positions):
    head_width = values_in.shape[-1]
    half_width = head_width // 2
    frequency = ROPE_BASE ** (-(jnp.arange(half_width, dtype=jnp.float32) * (2.0 / head_width)))
    angles = positions[:, None] * frequency[None, :]
    angles = angles.reshape((positions.shape[0],) + (1,) * (values_in.ndim - 2) + (half_width,))
    cosines = jnp.cos(angles)
    sines = jnp.sin(angles)
    first_half = values_in[..., :half_width]
    second_half = values_in[..., half_width:]
    return jnp.concatenate(
        [first_half * cosines - second_half * sines, second_half * cosines + first_half * sines],
        axis=-1,
    )


def norm_full_rows(values_in, gain_full):
    widened = tensor_gather(values_in, 1).astype(jnp.float32)
    squares = jnp.mean(widened * widened, axis=-1)
    return (widened * lax.rsqrt(squares + NORM_EPS)[:, None] * gain_full).astype(jnp.bfloat16)


def swap_cores(value):
    count = lax.axis_size("section")
    return lax.ppermute(value, "section", [(source, (source + 1) % count) for source in range(count)])


def paired_gather(value, axis, split_axis, active):
    value = jnp.where(active, value, swap_cores(value))
    first, second = jnp.split(value, 2, axis=split_axis)
    gathered = lax.all_gather(jnp.where(active, first, second), "expert", axis=axis, tiled=True)
    theirs = swap_cores(gathered)
    lead = jnp.where(active, gathered, theirs)
    trail = jnp.where(active, theirs, gathered)
    return jnp.concatenate([lead, trail], axis=split_axis)


def swap_tensor(value):
    count = lax.axis_size("tensor")
    return lax.ppermute(value, "tensor", [(source, (source + 1) % count) for source in range(count)])


def tensor_sum_scatter(value, axis):
    if lax.axis_size("tensor") != 2:
        return lax.psum_scatter(value, "tensor", scatter_dimension=axis, tiled=True)
    first, second = jnp.split(value, 2, axis=axis)
    lower = lax.axis_index("tensor") == 0
    kept = jnp.where(lower, first, second)
    sent = jnp.where(lower, second, first)
    return (kept.astype(jnp.float32) + swap_tensor(sent).astype(jnp.float32)).astype(value.dtype)


def tensor_gather(value, axis):
    if lax.axis_size("tensor") != 2:
        return lax.all_gather(value, "tensor", axis=axis, tiled=True)
    other = swap_tensor(value)
    lower = lax.axis_index("tensor") == 0
    return jnp.concatenate(
        [jnp.where(lower, value, other), jnp.where(lower, other, value)], axis=axis
    )


def terms_to_slots(terms):
    by_slot = lax.all_to_all(terms, "expert", split_axis=0, concat_axis=1, tiled=True)
    return tensor_sum_scatter(by_slot, 1)


def expert_path(full_rows, w_in_local, w_down_local):
    sources, slot_count, model_width = full_rows.shape
    local_width = w_down_local.shape[0]
    hidden = jnp.dot(
        full_rows.reshape(sources * slot_count, model_width),
        w_in_local.reshape(model_width, 2 * local_width),
        preferred_element_type=jnp.float32,
    )
    activated = (jax.nn.silu(hidden[:, :local_width]) * hidden[:, local_width:]).astype(
        jnp.bfloat16
    )
    partial_value = jnp.dot(activated, w_down_local, preferred_element_type=jnp.float32)
    partial_value = partial_value.reshape(sources, slot_count, model_width)
    summed = tensor_sum_scatter(partial_value.astype(jnp.bfloat16), 2)
    return lax.all_to_all(summed, "expert", split_axis=0, concat_axis=0, tiled=True)


def local(
    hidden_in,
    segment_ids,
    prompt_lengths,
    expert_choice,
    attn_gain,
    ffn_gain,
    w_qkv,
    w_out,
    w_shared_in,
    w_shared_down,
    router_weight,
    w_in,
    w_down,
):
    sections = lax.axis_size("section")
    section_id = lax.axis_index("section")
    experts_count = lax.axis_size("expert")
    expert_id = lax.axis_index("expert")
    micro_count, tokens_dev, columns = hidden_in.shape
    qkv_full = lax.all_gather(w_qkv[0], "expert", axis=0, tiled=True)
    out_local = w_out[0]
    shared_down_local = w_shared_down[0]
    shared_in_cols = lax.all_to_all(w_shared_in[0], "expert", split_axis=2, concat_axis=0, tiled=True)
    choices_every = lax.all_gather(expert_choice[0], "expert", axis=0, tiled=False)
    router_full = lax.all_gather(router_weight[0], "tensor", axis=0, tiled=True)
    attn_gain_full = lax.all_gather(attn_gain[0], "tensor", axis=0, tiled=True)
    ffn_gain_full = lax.all_gather(ffn_gain[0], "tensor", axis=0, tiled=True)
    qkv_full, shared_in_cols, choices_every, router_full, attn_gain_full, ffn_gain_full = (
        lax.optimization_barrier(
            (qkv_full, shared_in_cols, choices_every, router_full, attn_gain_full, ffn_gain_full)
        )
    )
    model_width, kv_local, group_cols = qkv_full.shape
    shared_cols = shared_in_cols.shape[2]
    head_width = HD
    group = group_cols // head_width - 2
    scale = head_width ** (-0.5)
    top_count = expert_choice.shape[-1]
    capacity = 5 * tokens_dev * top_count // (4 * experts_count)
    slot_index = expert_id * tokens_dev + jnp.arange(tokens_dev, dtype=jnp.int32)
    w_in_local = w_in[0, 0]
    w_down_local = w_down[0, 0]
    carried_rows = jnp.zeros((tokens_dev, columns), jnp.bfloat16)
    states = jnp.zeros((micro_count, tokens_dev, columns), jnp.bfloat16)
    caches = jnp.zeros((micro_count, tokens_dev, 2, kv_local * head_width), jnp.bfloat16)
    ticks = micro_count + sections - 1
    for tick_index in range(ticks):
        micro_index = jnp.clip(tick_index - section_id, 0, micro_count - 1)
        incoming = jnp.where(
            section_id == 0, hidden_in[min(tick_index, micro_count - 1)], carried_rows
        )
        active = (tick_index - section_id >= 0) & (tick_index - section_id < micro_count)
        if micro_count == 1 and sections == 2:
            expert_gather = functools.partial(paired_gather, active=active)
        else:
            def expert_gather(value, axis, split_axis):
                return lax.all_gather(value, "expert", axis=axis, tiled=True)
        segments = segment_ids[micro_index]
        lengths = prompt_lengths[micro_index]
        choices = expert_choice[0, micro_index]
        starts = jnp.cumsum(lengths) - lengths
        member = segments[:, None] == jnp.arange(lengths.shape[0], dtype=jnp.int32)[None, :]
        first_slot = jnp.sum(jnp.where(member, starts[None, :], 0), axis=1)
        positions = jnp.where(segments >= 0, slot_index - first_slot, 0).astype(jnp.float32)
        normed_full = norm_full_rows(incoming, attn_gain_full)
        projected = jnp.dot(
            normed_full, qkv_full.reshape(model_width, -1), preferred_element_type=jnp.float32
        )
        projected = projected.reshape(tokens_dev, kv_local, group + 2, head_width)
        queries = rotate_heads(projected[:, :, :group], positions).astype(jnp.bfloat16)
        key_rows = rotate_heads(projected[:, :, group], positions).astype(jnp.bfloat16)
        value_rows = projected[:, :, group + 1].astype(jnp.bfloat16)
        cache = jnp.stack(
            [key_rows.reshape(tokens_dev, -1), value_rows.reshape(tokens_dev, -1)], axis=1
        )
        kv_piece = expert_gather(cache.reshape(tokens_dev, -1), 0, 1)
        key_count = kv_piece.shape[0]
        kv_piece = kv_piece.reshape(key_count, 2, kv_local, head_width)
        key_slots = jnp.arange(key_count, dtype=jnp.int32)
        ends = jnp.cumsum(lengths)
        seg_piece = jnp.sum((key_slots[:, None] >= ends[None, :]).astype(jnp.int32), axis=1)
        seg_piece = jnp.where(key_slots < ends[-1], seg_piece, -1)
        allowed = (segments[:, None] == seg_piece[None, :]) & (segments[:, None] >= 0) & (
            key_slots[None, :] <= slot_index[:, None]
        ) | (key_slots[None, :] == slot_index[:, None])
        scores = (
            jnp.einsum(
                "tagd,nad->tagn", queries, kv_piece[:, 0], preferred_element_type=jnp.float32
            )
            * scale
        )
        weights_full = jnp.where(allowed[:, None, None, :], jnp.exp(scores), 0.0)
        numerator = jnp.einsum(
            "tagn,nad->tagd",
            weights_full.astype(jnp.bfloat16),
            kv_piece[:, 1],
            preferred_element_type=jnp.float32,
        )
        numerator, denominator = (numerator, jnp.sum(weights_full, axis=-1))
        attended = (numerator / denominator[..., None]).astype(jnp.bfloat16).reshape(tokens_dev, -1)
        attended_all = expert_gather(attended, 0, 1)
        attn_terms = lax.dot_general(
            attended_all, out_local, (((1,), (1,)), ((), ())), preferred_element_type=jnp.float32
        )
        attn_sum = terms_to_slots(attn_terms.astype(jnp.bfloat16)).astype(jnp.float32)
        after_attn = (incoming.astype(jnp.float32) + attn_sum).astype(jnp.bfloat16)
        moe_rows = norm_full_rows(after_attn, ffn_gain_full)
        moe_all = expert_gather(moe_rows, 0, 1)
        shared_hidden = jnp.dot(
            moe_all,
            shared_in_cols.reshape(model_width, 2 * shared_cols),
            preferred_element_type=jnp.float32,
        )
        shared_act = (
            jax.nn.silu(shared_hidden[:, :shared_cols]) * shared_hidden[:, shared_cols:]
        ).astype(jnp.bfloat16)
        shared_act = expert_gather(shared_act, 1, 0)
        shared_terms = lax.dot_general(
            shared_act,
            shared_down_local,
            (((1,), (1,)), ((), ())),
            preferred_element_type=jnp.float32,
        )
        shared_sum = terms_to_slots(shared_terms.astype(jnp.bfloat16))
        shared_out = lax.optimization_barrier(shared_sum).astype(jnp.float32)
        logits = jnp.dot(
            moe_rows.astype(jnp.float32), router_full, precision=lax.Precision.HIGHEST
        )
        expert_ids = jnp.arange(logits.shape[1], dtype=jnp.int32)
        picked = jnp.sum(
            jnp.where(choices[:, :, None] == expert_ids[None, None, :], logits[:, None, :], 0.0),
            axis=2,
        )
        raised = jnp.exp(picked)
        gate_weights = raised / jnp.sum(raised, axis=1, keepdims=True)
        flat_choice = choices.reshape(-1)
        onehot = (flat_choice[:, None] == expert_ids[None, :]).astype(jnp.int32)
        slot_rank = jnp.sum(onehot * (jnp.cumsum(onehot, axis=0) - onehot), axis=1)
        slot_ids = flat_choice * capacity + slot_rank
        choices_all = choices_every[:, micro_index]
        mine = jnp.any(choices_all == expert_id, axis=2)
        mine_rank = jnp.cumsum(mine.astype(jnp.int32), axis=1) - 1
        source_ids = jnp.broadcast_to(
            jnp.arange(experts_count, dtype=jnp.int32)[:, None], mine.shape
        )
        token_ids = jnp.broadcast_to(jnp.arange(tokens_dev, dtype=jnp.int32)[None, :], mine.shape)
        rank_at = jnp.where(mine, mine_rank, capacity)
        table = (
            jnp.zeros((experts_count, capacity), jnp.int32)
            .at[source_ids, rank_at]
            .set(source_ids * tokens_dev + token_ids, mode="drop")
        )
        filled = (
            jnp.zeros((experts_count, capacity), jnp.bool_)
            .at[source_ids, rank_at]
            .set(True, mode="drop")
        )
        incoming_rows = jnp.where(filled[..., None], moe_all[table], jnp.zeros((), jnp.bfloat16))
        returned = expert_path(incoming_rows, w_in_local, w_down_local)
        combined = returned.reshape(experts_count * capacity, columns)[slot_ids].astype(jnp.float32)
        combined = combined * gate_weights.reshape(-1)[:, None]
        moe_out = jnp.sum(combined.reshape(tokens_dev, top_count, columns), axis=1)
        output = (after_attn.astype(jnp.float32) + shared_out + moe_out).astype(jnp.bfloat16)
        output, cache = (output, cache)
        states = jnp.where(active, states.at[micro_index].set(output), states)
        caches = jnp.where(active, caches.at[micro_index].set(cache), caches)
        if tick_index + 1 < ticks:
            carried_rows = passed_along(output, "section", 1)
    return (states[None], caches[None])


def solution(mesh):
    placed = (
        P(None, "expert", "tensor"),
        P(None, "expert"),
        P(),
        P("section", None, "expert", None),
        P("section", "tensor"),
        P("section", "tensor"),
        P("section", "expert", "tensor", None),
        P("section", "expert", "tensor"),
        P("section", "expert", None, "tensor"),
        P("section", "expert", "tensor"),
        P("section", "tensor", None),
        P("section", "expert", None, None, "tensor"),
        P("section", "expert", "tensor", None),
    )
    return jax.shard_map(
        local,
        mesh=mesh,
        in_specs=placed,
        out_specs=(
            P("section", None, "expert", "tensor"),
            P("section", None, "expert", None, "tensor"),
        ),
        check_vma=False,
    )
```

```python
import functools

import jax
import jax.numpy as jnp
from jax import lax
from jax.sharding import PartitionSpec as P

HD = 128


NORM_EPS = 1e-05
ROPE_BASE = 500000.0


def passed_along(value, axis, steps):
    count = lax.axis_size(axis)
    leading, last = (max(0, -steps), min(count, count - steps))
    return lax.ppermute(value, axis, [(source, source + steps) for source in range(leading, last)])


def rotate_heads(values_in, positions):
    head_width = values_in.shape[-1]
    half_width = head_width // 2
    frequency = ROPE_BASE ** (-(jnp.arange(half_width, dtype=jnp.float32) * (2.0 / head_width)))
    angles = positions[:, None] * frequency[None, :]
    angles = angles.reshape((positions.shape[0],) + (1,) * (values_in.ndim - 2) + (half_width,))
    cosines = jnp.cos(angles)
    sines = jnp.sin(angles)
    first_half = values_in[..., :half_width]
    second_half = values_in[..., half_width:]
    return jnp.concatenate(
        [first_half * cosines - second_half * sines, second_half * cosines + first_half * sines],
        axis=-1,
    )


def norm_full_rows(values_in, gain_full):
    widened = tensor_gather(values_in, 1).astype(jnp.float32)
    squares = jnp.mean(widened * widened, axis=-1)
    return (widened * lax.rsqrt(squares + NORM_EPS)[:, None] * gain_full).astype(jnp.bfloat16)


def swap_cores(value):
    count = lax.axis_size("section")
    return lax.ppermute(value, "section", [(source, (source + 1) % count) for source in range(count)])


def paired_gather(value, axis, split_axis, active):
    value = jnp.where(active, value, swap_cores(value))
    first, second = jnp.split(value, 2, axis=split_axis)
    gathered = lax.all_gather(jnp.where(active, first, second), "expert", axis=axis, tiled=True)
    theirs = swap_cores(gathered)
    lead = jnp.where(active, gathered, theirs)
    trail = jnp.where(active, theirs, gathered)
    return jnp.concatenate([lead, trail], axis=split_axis)


def running_count(flags, axis):
    size = flags.shape[axis]
    steps = jnp.arange(size, dtype=jnp.int32)
    lower = (steps[:, None] >= steps[None, :]).astype(jnp.bfloat16)
    counted = jnp.tensordot(lower, flags.astype(jnp.bfloat16), axes=((1,), (axis,)),
                            preferred_element_type=jnp.float32)
    return jnp.moveaxis(counted, 0, axis).astype(jnp.int32)


def swap_tensor(value):
    count = lax.axis_size("tensor")
    return lax.ppermute(value, "tensor", [(source, (source + 1) % count) for source in range(count)])


def tensor_sum_scatter(value, axis):
    if lax.axis_size("tensor") != 2:
        return lax.psum_scatter(value, "tensor", scatter_dimension=axis, tiled=True)
    first, second = jnp.split(value, 2, axis=axis)
    lower = lax.axis_index("tensor") == 0
    kept = jnp.where(lower, first, second)
    sent = jnp.where(lower, second, first)
    return (kept.astype(jnp.float32) + swap_tensor(sent).astype(jnp.float32)).astype(value.dtype)


def tensor_gather(value, axis):
    if lax.axis_size("tensor") != 2:
        return lax.all_gather(value, "tensor", axis=axis, tiled=True)
    other = swap_tensor(value)
    lower = lax.axis_index("tensor") == 0
    return jnp.concatenate(
        [jnp.where(lower, value, other), jnp.where(lower, other, value)], axis=axis
    )


def terms_to_slots(terms):
    by_slot = lax.all_to_all(terms, "expert", split_axis=0, concat_axis=1, tiled=True)
    return tensor_sum_scatter(by_slot, 1)


def expert_path(full_rows, w_in_local, w_down_local):
    sources, slot_count, model_width = full_rows.shape
    local_width = w_down_local.shape[0]
    hidden = jnp.dot(
        full_rows.reshape(sources * slot_count, model_width),
        w_in_local.reshape(model_width, 2 * local_width),
        preferred_element_type=jnp.float32,
    )
    activated = (jax.nn.silu(hidden[:, :local_width]) * hidden[:, local_width:]).astype(
        jnp.bfloat16
    )
    partial_value = jnp.dot(activated, w_down_local, preferred_element_type=jnp.float32)
    partial_value = partial_value.reshape(sources, slot_count, model_width)
    summed = tensor_sum_scatter(partial_value.astype(jnp.bfloat16), 2)
    return lax.all_to_all(summed, "expert", split_axis=0, concat_axis=0, tiled=True)


def local(
    hidden_in,
    segment_ids,
    prompt_lengths,
    expert_choice,
    attn_gain,
    ffn_gain,
    w_qkv,
    w_out,
    w_shared_in,
    w_shared_down,
    router_weight,
    w_in,
    w_down,
):
    sections = lax.axis_size("section")
    section_id = lax.axis_index("section")
    experts_count = lax.axis_size("expert")
    expert_id = lax.axis_index("expert")
    micro_count, tokens_dev, columns = hidden_in.shape
    qkv_full = lax.all_gather(w_qkv[0], "expert", axis=0, tiled=True)
    out_local = w_out[0]
    shared_down_local = w_shared_down[0]
    shared_in_cols = lax.all_to_all(w_shared_in[0], "expert", split_axis=2, concat_axis=0, tiled=True)
    choices_every = lax.all_gather(expert_choice[0], "expert", axis=0, tiled=False)
    router_full = lax.all_gather(router_weight[0], "tensor", axis=0, tiled=True)
    attn_gain_full = lax.all_gather(attn_gain[0], "tensor", axis=0, tiled=True)
    ffn_gain_full = lax.all_gather(ffn_gain[0], "tensor", axis=0, tiled=True)
    qkv_full, shared_in_cols, choices_every, router_full, attn_gain_full, ffn_gain_full = (
        lax.optimization_barrier(
            (qkv_full, shared_in_cols, choices_every, router_full, attn_gain_full, ffn_gain_full)
        )
    )
    model_width, kv_local, group_cols = qkv_full.shape
    shared_cols = shared_in_cols.shape[2]
    head_width = HD
    group = group_cols // head_width - 2
    scale = head_width ** (-0.5)
    top_count = expert_choice.shape[-1]
    capacity = 5 * tokens_dev * top_count // (4 * experts_count)
    slot_index = expert_id * tokens_dev + jnp.arange(tokens_dev, dtype=jnp.int32)
    w_in_local = w_in[0, 0]
    w_down_local = w_down[0, 0]
    carried_rows = jnp.zeros((tokens_dev, columns), jnp.bfloat16)
    states = jnp.zeros((micro_count, tokens_dev, columns), jnp.bfloat16)
    caches = jnp.zeros((micro_count, tokens_dev, 2, kv_local * head_width), jnp.bfloat16)
    ticks = micro_count + sections - 1
    for tick_index in range(ticks):
        micro_index = jnp.clip(tick_index - section_id, 0, micro_count - 1)
        incoming = jnp.where(
            section_id == 0, hidden_in[min(tick_index, micro_count - 1)], carried_rows
        )
        active = (tick_index - section_id >= 0) & (tick_index - section_id < micro_count)
        if micro_count == 1 and sections == 2:
            expert_gather = functools.partial(paired_gather, active=active)
        else:
            def expert_gather(value, axis, split_axis):
                return lax.all_gather(value, "expert", axis=axis, tiled=True)
        segments = segment_ids[micro_index]
        lengths = prompt_lengths[micro_index]
        choices = expert_choice[0, micro_index]
        starts = jnp.cumsum(lengths) - lengths
        member = segments[:, None] == jnp.arange(lengths.shape[0], dtype=jnp.int32)[None, :]
        first_slot = jnp.sum(jnp.where(member, starts[None, :], 0), axis=1)
        positions = jnp.where(segments >= 0, slot_index - first_slot, 0).astype(jnp.float32)
        normed_full = norm_full_rows(incoming, attn_gain_full)
        projected = jnp.dot(
            normed_full, qkv_full.reshape(model_width, -1), preferred_element_type=jnp.float32
        )
        projected = projected.reshape(tokens_dev, kv_local, group + 2, head_width)
        queries = rotate_heads(projected[:, :, :group], positions).astype(jnp.bfloat16)
        key_rows = rotate_heads(projected[:, :, group], positions).astype(jnp.bfloat16)
        value_rows = projected[:, :, group + 1].astype(jnp.bfloat16)
        cache = jnp.stack(
            [key_rows.reshape(tokens_dev, -1), value_rows.reshape(tokens_dev, -1)], axis=1
        )
        kv_piece = expert_gather(cache.reshape(tokens_dev, -1), 0, 1)
        key_count = kv_piece.shape[0]
        kv_piece = kv_piece.reshape(key_count, 2, kv_local, head_width)
        key_slots = jnp.arange(key_count, dtype=jnp.int32)
        ends = jnp.cumsum(lengths)
        seg_piece = jnp.sum((key_slots[:, None] >= ends[None, :]).astype(jnp.int32), axis=1)
        seg_piece = jnp.where(key_slots < ends[-1], seg_piece, -1)
        allowed = (segments[:, None] == seg_piece[None, :]) & (segments[:, None] >= 0) & (
            key_slots[None, :] <= slot_index[:, None]
        ) | (key_slots[None, :] == slot_index[:, None])
        scores = (
            jnp.einsum(
                "tagd,nad->tagn", queries, kv_piece[:, 0], preferred_element_type=jnp.float32
            )
            * scale
        )
        weights_full = jnp.where(allowed[:, None, None, :], jnp.exp(scores), 0.0)
        numerator = jnp.einsum(
            "tagn,nad->tagd",
            weights_full.astype(jnp.bfloat16),
            kv_piece[:, 1],
            preferred_element_type=jnp.float32,
        )
        numerator, denominator = (numerator, jnp.sum(weights_full, axis=-1))
        attended = (numerator / denominator[..., None]).astype(jnp.bfloat16).reshape(tokens_dev, -1)
        attended_all = expert_gather(attended, 0, 1)
        attn_terms = lax.dot_general(
            attended_all, out_local, (((1,), (1,)), ((), ())), preferred_element_type=jnp.float32
        )
        attn_sum = terms_to_slots(attn_terms.astype(jnp.bfloat16)).astype(jnp.float32)
        after_attn = (incoming.astype(jnp.float32) + attn_sum).astype(jnp.bfloat16)
        moe_rows = norm_full_rows(after_attn, ffn_gain_full)
        moe_all = expert_gather(moe_rows, 0, 1)
        shared_hidden = jnp.dot(
            moe_all,
            shared_in_cols.reshape(model_width, 2 * shared_cols),
            preferred_element_type=jnp.float32,
        )
        shared_act = (
            jax.nn.silu(shared_hidden[:, :shared_cols]) * shared_hidden[:, shared_cols:]
        ).astype(jnp.bfloat16)
        shared_act = expert_gather(shared_act, 1, 0)
        shared_terms = lax.dot_general(
            shared_act,
            shared_down_local,
            (((1,), (1,)), ((), ())),
            preferred_element_type=jnp.float32,
        )
        shared_sum = terms_to_slots(shared_terms.astype(jnp.bfloat16))
        shared_out = lax.optimization_barrier(shared_sum).astype(jnp.float32)
        logits = jnp.dot(
            moe_rows.astype(jnp.float32), router_full, precision=lax.Precision.HIGHEST
        )
        expert_ids = jnp.arange(logits.shape[1], dtype=jnp.int32)
        picked = jnp.sum(
            jnp.where(choices[:, :, None] == expert_ids[None, None, :], logits[:, None, :], 0.0),
            axis=2,
        )
        raised = jnp.exp(picked)
        gate_weights = raised / jnp.sum(raised, axis=1, keepdims=True)
        flat_choice = choices.reshape(-1)
        onehot = (flat_choice[:, None] == expert_ids[None, :]).astype(jnp.int32)
        slot_rank = jnp.sum(onehot * (running_count(onehot, 0) - onehot), axis=1)
        slot_ids = flat_choice * capacity + slot_rank
        choices_all = choices_every[:, micro_index]
        mine = jnp.any(choices_all == expert_id, axis=2)
        mine_rank = running_count(mine, 1) - 1
        source_ids = jnp.broadcast_to(
            jnp.arange(experts_count, dtype=jnp.int32)[:, None], mine.shape
        )
        token_ids = jnp.broadcast_to(jnp.arange(tokens_dev, dtype=jnp.int32)[None, :], mine.shape)
        rank_at = jnp.where(mine, mine_rank, capacity)
        table = (
            jnp.zeros((experts_count, capacity), jnp.int32)
            .at[source_ids, rank_at]
            .set(source_ids * tokens_dev + token_ids, mode="drop")
        )
        filled = (
            jnp.zeros((experts_count, capacity), jnp.bool_)
            .at[source_ids, rank_at]
            .set(True, mode="drop")
        )
        incoming_rows = jnp.where(filled[..., None], moe_all[table], jnp.zeros((), jnp.bfloat16))
        returned = expert_path(incoming_rows, w_in_local, w_down_local)
        combined = returned.reshape(experts_count * capacity, columns)[slot_ids].astype(jnp.float32)
        combined = combined * gate_weights.reshape(-1)[:, None]
        moe_out = jnp.sum(combined.reshape(tokens_dev, top_count, columns), axis=1)
        output = (after_attn.astype(jnp.float32) + shared_out + moe_out).astype(jnp.bfloat16)
        output, cache = (output, cache)
        states = jnp.where(active, states.at[micro_index].set(output), states)
        caches = jnp.where(active, caches.at[micro_index].set(cache), caches)
        if tick_index + 1 < ticks:
            carried_rows = passed_along(output, "section", 1)
    return (states[None], caches[None])


def solution(mesh):
    placed = (
        P(None, "expert", "tensor"),
        P(None, "expert"),
        P(),
        P("section", None, "expert", None),
        P("section", "tensor"),
        P("section", "tensor"),
        P("section", "expert", "tensor", None),
        P("section", "expert", "tensor"),
        P("section", "expert", None, "tensor"),
        P("section", "expert", "tensor"),
        P("section", "tensor", None),
        P("section", "expert", None, None, "tensor"),
        P("section", "expert", "tensor", None),
    )
    return jax.shard_map(
        local,
        mesh=mesh,
        in_specs=placed,
        out_specs=(
            P("section", None, "expert", "tensor"),
            P("section", None, "expert", None, "tensor"),
        ),
        check_vma=False,
    )
```

```python
import functools

import jax
import jax.numpy as jnp
from jax import lax
from jax.sharding import PartitionSpec as P

HD = 128


NORM_EPS = 1e-05
ROPE_BASE = 500000.0


def passed_along(value, axis, steps):
    count = lax.axis_size(axis)
    leading, last = (max(0, -steps), min(count, count - steps))
    return lax.ppermute(value, axis, [(source, source + steps) for source in range(leading, last)])


def rotate_heads(values_in, positions):
    head_width = values_in.shape[-1]
    half_width = head_width // 2
    frequency = ROPE_BASE ** (-(jnp.arange(half_width, dtype=jnp.float32) * (2.0 / head_width)))
    angles = positions[:, None] * frequency[None, :]
    angles = angles.reshape((positions.shape[0],) + (1,) * (values_in.ndim - 2) + (half_width,))
    cosines = jnp.cos(angles)
    sines = jnp.sin(angles)
    first_half = values_in[..., :half_width]
    second_half = values_in[..., half_width:]
    return jnp.concatenate(
        [first_half * cosines - second_half * sines, second_half * cosines + first_half * sines],
        axis=-1,
    )


def norm_full_rows(values_in, gain_full):
    widened = tensor_gather(values_in, 1).astype(jnp.float32)
    squares = jnp.mean(widened * widened, axis=-1)
    return (widened * lax.rsqrt(squares + NORM_EPS)[:, None] * gain_full).astype(jnp.bfloat16)


def swap_cores(value):
    count = lax.axis_size("section")
    return lax.ppermute(value, "section", [(source, (source + 1) % count) for source in range(count)])


def paired_gather(value, axis, split_axis, active):
    value = jnp.where(active, value, swap_cores(value))
    first, second = jnp.split(value, 2, axis=split_axis)
    gathered = lax.all_gather(jnp.where(active, first, second), "expert", axis=axis, tiled=True)
    theirs = swap_cores(gathered)
    lead = jnp.where(active, gathered, theirs)
    trail = jnp.where(active, theirs, gathered)
    return jnp.concatenate([lead, trail], axis=split_axis)


def running_count(flags, axis):
    size = flags.shape[axis]
    steps = jnp.arange(size, dtype=jnp.int32)
    lower = (steps[:, None] >= steps[None, :]).astype(jnp.bfloat16)
    counted = jnp.tensordot(lower, flags.astype(jnp.bfloat16), axes=((1,), (axis,)),
                            preferred_element_type=jnp.float32)
    return jnp.moveaxis(counted, 0, axis).astype(jnp.int32)


def swap_tensor(value):
    count = lax.axis_size("tensor")
    return lax.ppermute(value, "tensor", [(source, (source + 1) % count) for source in range(count)])


def tensor_sum_scatter(value, axis):
    if lax.axis_size("tensor") != 2:
        return lax.psum_scatter(value, "tensor", scatter_dimension=axis, tiled=True)
    first, second = jnp.split(value, 2, axis=axis)
    lower = lax.axis_index("tensor") == 0
    kept = jnp.where(lower, first, second)
    sent = jnp.where(lower, second, first)
    return (kept.astype(jnp.float32) + swap_tensor(sent).astype(jnp.float32)).astype(value.dtype)


def tensor_gather(value, axis):
    if lax.axis_size("tensor") != 2:
        return lax.all_gather(value, "tensor", axis=axis, tiled=True)
    other = swap_tensor(value)
    lower = lax.axis_index("tensor") == 0
    return jnp.concatenate(
        [jnp.where(lower, value, other), jnp.where(lower, other, value)], axis=axis
    )


def paired_apply(step, value, in_axis, out_axis, active):
    if active is None:
        return step(value)
    value = jnp.where(active, value, swap_cores(value))
    first, second = jnp.split(value, 2, axis=in_axis)
    done = step(jnp.where(active, first, second))
    theirs = swap_cores(done)
    return jnp.concatenate(
        [jnp.where(active, done, theirs), jnp.where(active, theirs, done)], axis=out_axis
    )


def terms_to_slots(terms, active):
    count = lax.axis_size("expert")
    blocks = terms.reshape(count, terms.shape[0] // count, terms.shape[1])

    def step(part):
        by_slot = lax.all_to_all(
            part.reshape(-1, part.shape[2]), "expert", split_axis=0, concat_axis=1, tiled=True
        )
        return tensor_sum_scatter(by_slot, 1)

    return paired_apply(step, blocks, 1, 0, active)


def expert_path(full_rows, w_in_local, w_down_local, active):
    sources, slot_count, model_width = full_rows.shape
    local_width = w_down_local.shape[0]
    hidden = jnp.dot(
        full_rows.reshape(sources * slot_count, model_width),
        w_in_local.reshape(model_width, 2 * local_width),
        preferred_element_type=jnp.float32,
    )
    activated = (jax.nn.silu(hidden[:, :local_width]) * hidden[:, local_width:]).astype(
        jnp.bfloat16
    )
    partial_value = jnp.dot(activated, w_down_local, preferred_element_type=jnp.float32)
    partial_value = partial_value.reshape(sources, slot_count, model_width)

    def step(part):
        summed = tensor_sum_scatter(part, 2)
        return lax.all_to_all(summed, "expert", split_axis=0, concat_axis=0, tiled=True)

    return paired_apply(step, partial_value.astype(jnp.bfloat16), 1, 1, active)


def local(
    hidden_in,
    segment_ids,
    prompt_lengths,
    expert_choice,
    attn_gain,
    ffn_gain,
    w_qkv,
    w_out,
    w_shared_in,
    w_shared_down,
    router_weight,
    w_in,
    w_down,
):
    sections = lax.axis_size("section")
    section_id = lax.axis_index("section")
    experts_count = lax.axis_size("expert")
    expert_id = lax.axis_index("expert")
    micro_count, tokens_dev, columns = hidden_in.shape
    qkv_full = lax.all_gather(w_qkv[0], "expert", axis=0, tiled=True)
    out_local = w_out[0]
    shared_down_local = w_shared_down[0]
    shared_in_cols = lax.all_to_all(w_shared_in[0], "expert", split_axis=2, concat_axis=0, tiled=True)
    choices_every = lax.all_gather(expert_choice[0], "expert", axis=0, tiled=False)
    router_full = lax.all_gather(router_weight[0], "tensor", axis=0, tiled=True)
    attn_gain_full = lax.all_gather(attn_gain[0], "tensor", axis=0, tiled=True)
    ffn_gain_full = lax.all_gather(ffn_gain[0], "tensor", axis=0, tiled=True)
    qkv_full, shared_in_cols, choices_every, router_full, attn_gain_full, ffn_gain_full = (
        lax.optimization_barrier(
            (qkv_full, shared_in_cols, choices_every, router_full, attn_gain_full, ffn_gain_full)
        )
    )
    model_width, kv_local, group_cols = qkv_full.shape
    shared_cols = shared_in_cols.shape[2]
    head_width = HD
    group = group_cols // head_width - 2
    scale = head_width ** (-0.5)
    top_count = expert_choice.shape[-1]
    capacity = 5 * tokens_dev * top_count // (4 * experts_count)
    slot_index = expert_id * tokens_dev + jnp.arange(tokens_dev, dtype=jnp.int32)
    w_in_local = w_in[0, 0]
    w_down_local = w_down[0, 0]
    carried_rows = jnp.zeros((tokens_dev, columns), jnp.bfloat16)
    states = jnp.zeros((micro_count, tokens_dev, columns), jnp.bfloat16)
    caches = jnp.zeros((micro_count, tokens_dev, 2, kv_local * head_width), jnp.bfloat16)
    ticks = micro_count + sections - 1
    for tick_index in range(ticks):
        micro_index = jnp.clip(tick_index - section_id, 0, micro_count - 1)
        incoming = jnp.where(
            section_id == 0, hidden_in[min(tick_index, micro_count - 1)], carried_rows
        )
        active = (tick_index - section_id >= 0) & (tick_index - section_id < micro_count)
        pair_active = active if micro_count == 1 and sections == 2 else None
        if pair_active is not None:
            expert_gather = functools.partial(paired_gather, active=active)
        else:
            def expert_gather(value, axis, split_axis):
                return lax.all_gather(value, "expert", axis=axis, tiled=True)
        segments = segment_ids[micro_index]
        lengths = prompt_lengths[micro_index]
        choices = expert_choice[0, micro_index]
        starts = jnp.cumsum(lengths) - lengths
        member = segments[:, None] == jnp.arange(lengths.shape[0], dtype=jnp.int32)[None, :]
        first_slot = jnp.sum(jnp.where(member, starts[None, :], 0), axis=1)
        positions = jnp.where(segments >= 0, slot_index - first_slot, 0).astype(jnp.float32)
        normed_full = norm_full_rows(incoming, attn_gain_full)
        projected = jnp.dot(
            normed_full, qkv_full.reshape(model_width, -1), preferred_element_type=jnp.float32
        )
        projected = projected.reshape(tokens_dev, kv_local, group + 2, head_width)
        queries = rotate_heads(projected[:, :, :group], positions).astype(jnp.bfloat16)
        key_rows = rotate_heads(projected[:, :, group], positions).astype(jnp.bfloat16)
        value_rows = projected[:, :, group + 1].astype(jnp.bfloat16)
        cache = jnp.stack(
            [key_rows.reshape(tokens_dev, -1), value_rows.reshape(tokens_dev, -1)], axis=1
        )
        kv_piece = expert_gather(cache.reshape(tokens_dev, -1), 0, 1)
        key_count = kv_piece.shape[0]
        kv_piece = kv_piece.reshape(key_count, 2, kv_local, head_width)
        key_slots = jnp.arange(key_count, dtype=jnp.int32)
        ends = jnp.cumsum(lengths)
        seg_piece = jnp.sum((key_slots[:, None] >= ends[None, :]).astype(jnp.int32), axis=1)
        seg_piece = jnp.where(key_slots < ends[-1], seg_piece, -1)
        allowed = (segments[:, None] == seg_piece[None, :]) & (segments[:, None] >= 0) & (
            key_slots[None, :] <= slot_index[:, None]
        ) | (key_slots[None, :] == slot_index[:, None])
        scores = (
            jnp.einsum(
                "tagd,nad->tagn", queries, kv_piece[:, 0], preferred_element_type=jnp.float32
            )
            * scale
        )
        weights_full = jnp.where(allowed[:, None, None, :], jnp.exp(scores), 0.0)
        numerator = jnp.einsum(
            "tagn,nad->tagd",
            weights_full.astype(jnp.bfloat16),
            kv_piece[:, 1],
            preferred_element_type=jnp.float32,
        )
        numerator, denominator = (numerator, jnp.sum(weights_full, axis=-1))
        attended = (numerator / denominator[..., None]).astype(jnp.bfloat16).reshape(tokens_dev, -1)
        attended_all = expert_gather(attended, 0, 1)
        attn_terms = lax.dot_general(
            attended_all, out_local, (((1,), (1,)), ((), ())), preferred_element_type=jnp.float32
        )
        attn_sum = terms_to_slots(attn_terms.astype(jnp.bfloat16), pair_active).astype(jnp.float32)
        after_attn = (incoming.astype(jnp.float32) + attn_sum).astype(jnp.bfloat16)
        moe_rows = norm_full_rows(after_attn, ffn_gain_full)
        moe_all = expert_gather(moe_rows, 0, 1)
        shared_hidden = jnp.dot(
            moe_all,
            shared_in_cols.reshape(model_width, 2 * shared_cols),
            preferred_element_type=jnp.float32,
        )
        shared_act = (
            jax.nn.silu(shared_hidden[:, :shared_cols]) * shared_hidden[:, shared_cols:]
        ).astype(jnp.bfloat16)
        shared_act = expert_gather(shared_act, 1, 0)
        shared_terms = lax.dot_general(
            shared_act,
            shared_down_local,
            (((1,), (1,)), ((), ())),
            preferred_element_type=jnp.float32,
        )
        shared_sum = terms_to_slots(shared_terms.astype(jnp.bfloat16), pair_active)
        shared_out = lax.optimization_barrier(shared_sum).astype(jnp.float32)
        logits = jnp.dot(
            moe_rows.astype(jnp.float32), router_full, precision=lax.Precision.HIGHEST
        )
        expert_ids = jnp.arange(logits.shape[1], dtype=jnp.int32)
        picked = jnp.sum(
            jnp.where(choices[:, :, None] == expert_ids[None, None, :], logits[:, None, :], 0.0),
            axis=2,
        )
        raised = jnp.exp(picked)
        gate_weights = raised / jnp.sum(raised, axis=1, keepdims=True)
        flat_choice = choices.reshape(-1)
        onehot = (flat_choice[:, None] == expert_ids[None, :]).astype(jnp.int32)
        slot_rank = jnp.sum(onehot * (running_count(onehot, 0) - onehot), axis=1)
        slot_ids = flat_choice * capacity + slot_rank
        choices_all = choices_every[:, micro_index]
        mine = jnp.any(choices_all == expert_id, axis=2)
        mine_rank = running_count(mine, 1) - 1
        source_ids = jnp.broadcast_to(
            jnp.arange(experts_count, dtype=jnp.int32)[:, None], mine.shape
        )
        token_ids = jnp.broadcast_to(jnp.arange(tokens_dev, dtype=jnp.int32)[None, :], mine.shape)
        rank_at = jnp.where(mine, mine_rank, capacity)
        table = (
            jnp.zeros((experts_count, capacity), jnp.int32)
            .at[source_ids, rank_at]
            .set(source_ids * tokens_dev + token_ids, mode="drop")
        )
        filled = (
            jnp.zeros((experts_count, capacity), jnp.bool_)
            .at[source_ids, rank_at]
            .set(True, mode="drop")
        )
        incoming_rows = jnp.where(filled[..., None], moe_all[table], jnp.zeros((), jnp.bfloat16))
        returned = expert_path(incoming_rows, w_in_local, w_down_local, pair_active)
        combined = returned.reshape(experts_count * capacity, columns)[slot_ids].astype(jnp.float32)
        combined = combined * gate_weights.reshape(-1)[:, None]
        moe_out = jnp.sum(combined.reshape(tokens_dev, top_count, columns), axis=1)
        output = (after_attn.astype(jnp.float32) + shared_out + moe_out).astype(jnp.bfloat16)
        output, cache = (output, cache)
        states = jnp.where(active, states.at[micro_index].set(output), states)
        caches = jnp.where(active, caches.at[micro_index].set(cache), caches)
        if tick_index + 1 < ticks:
            carried_rows = passed_along(output, "section", 1)
    return (states[None], caches[None])


def solution(mesh):
    placed = (
        P(None, "expert", "tensor"),
        P(None, "expert"),
        P(),
        P("section", None, "expert", None),
        P("section", "tensor"),
        P("section", "tensor"),
        P("section", "expert", "tensor", None),
        P("section", "expert", "tensor"),
        P("section", "expert", None, "tensor"),
        P("section", "expert", "tensor"),
        P("section", "tensor", None),
        P("section", "expert", None, None, "tensor"),
        P("section", "expert", "tensor", None),
    )
    return jax.shard_map(
        local,
        mesh=mesh,
        in_specs=placed,
        out_specs=(
            P("section", None, "expert", "tensor"),
            P("section", None, "expert", None, "tensor"),
        ),
        check_vma=False,
    )
```

```python
import functools

import jax
import jax.numpy as jnp
from jax import lax
from jax.sharding import PartitionSpec as P

HD = 128


NORM_EPS = 1e-05
ROPE_BASE = 500000.0


def passed_along(value, axis, steps):
    count = lax.axis_size(axis)
    leading, last = (max(0, -steps), min(count, count - steps))
    return lax.ppermute(value, axis, [(source, source + steps) for source in range(leading, last)])


def rotate_heads(values_in, positions):
    head_width = values_in.shape[-1]
    half_width = head_width // 2
    frequency = ROPE_BASE ** (-(jnp.arange(half_width, dtype=jnp.float32) * (2.0 / head_width)))
    angles = positions[:, None] * frequency[None, :]
    angles = angles.reshape((positions.shape[0],) + (1,) * (values_in.ndim - 2) + (half_width,))
    cosines = jnp.cos(angles)
    sines = jnp.sin(angles)
    first_half = values_in[..., :half_width]
    second_half = values_in[..., half_width:]
    return jnp.concatenate(
        [first_half * cosines - second_half * sines, second_half * cosines + first_half * sines],
        axis=-1,
    )


def norm_full_rows(values_in, gain_full):
    widened = tensor_gather(values_in, 1).astype(jnp.float32)
    squares = jnp.mean(widened * widened, axis=-1)
    return (widened * lax.rsqrt(squares + NORM_EPS)[:, None] * gain_full).astype(jnp.bfloat16)


def swap_cores(value):
    count = lax.axis_size("section")
    return lax.ppermute(value, "section", [(source, (source + 1) % count) for source in range(count)])


def paired_gather(value, axis, split_axis, active):
    value = jnp.where(active, value, swap_cores(value))
    first, second = jnp.split(value, 2, axis=split_axis)
    gathered = lax.all_gather(jnp.where(active, first, second), "expert", axis=axis, tiled=True)
    theirs = swap_cores(gathered)
    lead = jnp.where(active, gathered, theirs)
    trail = jnp.where(active, theirs, gathered)
    return jnp.concatenate([lead, trail], axis=split_axis)


def running_count(flags, axis):
    size = flags.shape[axis]
    steps = jnp.arange(size, dtype=jnp.int32)
    lower = (steps[:, None] >= steps[None, :]).astype(jnp.bfloat16)
    counted = jnp.tensordot(lower, flags.astype(jnp.bfloat16), axes=((1,), (axis,)),
                            preferred_element_type=jnp.float32)
    return jnp.moveaxis(counted, 0, axis).astype(jnp.int32)


def swap_tensor(value):
    count = lax.axis_size("tensor")
    return lax.ppermute(value, "tensor", [(source, (source + 1) % count) for source in range(count)])


def tensor_sum_scatter(value, axis):
    if lax.axis_size("tensor") != 2:
        return lax.psum_scatter(value, "tensor", scatter_dimension=axis, tiled=True)
    first, second = jnp.split(value, 2, axis=axis)
    lower = lax.axis_index("tensor") == 0
    kept = jnp.where(lower, first, second)
    sent = jnp.where(lower, second, first)
    return (kept.astype(jnp.float32) + swap_tensor(sent).astype(jnp.float32)).astype(value.dtype)


def tensor_gather(value, axis):
    if lax.axis_size("tensor") != 2:
        return lax.all_gather(value, "tensor", axis=axis, tiled=True)
    other = swap_tensor(value)
    lower = lax.axis_index("tensor") == 0
    return jnp.concatenate(
        [jnp.where(lower, value, other), jnp.where(lower, other, value)], axis=axis
    )


def paired_apply(step, value, in_axis, out_axis, active):
    if active is None:
        return step(value)
    value = jnp.where(active, value, swap_cores(value))
    first, second = jnp.split(value, 2, axis=in_axis)
    done = step(jnp.where(active, first, second))
    theirs = swap_cores(done)
    return jnp.concatenate(
        [jnp.where(active, done, theirs), jnp.where(active, theirs, done)], axis=out_axis
    )


def terms_to_slots(terms, active):
    count = lax.axis_size("expert")
    blocks = terms.reshape(count, terms.shape[0] // count, terms.shape[1])

    def step(part):
        by_slot = lax.all_to_all(
            part.reshape(-1, part.shape[2]), "expert", split_axis=0, concat_axis=1, tiled=True
        )
        return tensor_sum_scatter(by_slot, 1)

    return paired_apply(step, blocks, 1, 0, active)


def expert_path(full_rows, w_in_local, w_down_local, active):
    sources, slot_count, model_width = full_rows.shape
    local_width = w_down_local.shape[0]
    hidden = jnp.dot(
        full_rows.reshape(sources * slot_count, model_width),
        w_in_local.reshape(model_width, 2 * local_width),
        preferred_element_type=jnp.float32,
    )
    activated = (jax.nn.silu(hidden[:, :local_width]) * hidden[:, local_width:]).astype(
        jnp.bfloat16
    )
    partial_value = jnp.dot(activated, w_down_local, preferred_element_type=jnp.float32)
    partial_value = partial_value.reshape(sources, slot_count, model_width)

    def step(part):
        summed = tensor_sum_scatter(part, 2)
        return lax.all_to_all(summed, "expert", split_axis=0, concat_axis=0, tiled=True)

    return paired_apply(step, partial_value.astype(jnp.bfloat16), 1, 1, active)


def local(
    hidden_in,
    segment_ids,
    prompt_lengths,
    expert_choice,
    attn_gain,
    ffn_gain,
    w_qkv,
    w_out,
    w_shared_in,
    w_shared_down,
    router_weight,
    w_in,
    w_down,
):
    sections = lax.axis_size("section")
    section_id = lax.axis_index("section")
    experts_count = lax.axis_size("expert")
    expert_id = lax.axis_index("expert")
    micro_count, tokens_dev, columns = hidden_in.shape
    qkv_full = lax.all_gather(w_qkv[0], "expert", axis=0, tiled=True)
    out_local = w_out[0]
    shared_down_local = w_shared_down[0]
    shared_in_cols = lax.all_to_all(w_shared_in[0], "expert", split_axis=2, concat_axis=0, tiled=True)
    choices_every = lax.all_gather(expert_choice[0], "expert", axis=0, tiled=False)
    router_full = lax.all_gather(router_weight[0], "tensor", axis=0, tiled=True)
    attn_gain_full = lax.all_gather(attn_gain[0], "tensor", axis=0, tiled=True)
    ffn_gain_full = lax.all_gather(ffn_gain[0], "tensor", axis=0, tiled=True)
    w_in_local = w_in[0, 0]
    w_down_local = w_down[0, 0]
    (
        qkv_full,
        shared_in_cols,
        choices_every,
        router_full,
        attn_gain_full,
        ffn_gain_full,
        w_in_local,
        w_down_local,
    ) = lax.optimization_barrier(
        (
            qkv_full,
            shared_in_cols,
            choices_every,
            router_full,
            attn_gain_full,
            ffn_gain_full,
            w_in_local,
            w_down_local,
        )
    )
    model_width, kv_local, group_cols = qkv_full.shape
    shared_cols = shared_in_cols.shape[2]
    head_width = HD
    group = group_cols // head_width - 2
    scale = head_width ** (-0.5)
    top_count = expert_choice.shape[-1]
    capacity = 5 * tokens_dev * top_count // (4 * experts_count)
    slot_index = expert_id * tokens_dev + jnp.arange(tokens_dev, dtype=jnp.int32)
    carried_rows = jnp.zeros((tokens_dev, columns), jnp.bfloat16)
    states = jnp.zeros((micro_count, tokens_dev, columns), jnp.bfloat16)
    caches = jnp.zeros((micro_count, tokens_dev, 2, kv_local * head_width), jnp.bfloat16)
    ticks = micro_count + sections - 1
    for tick_index in range(ticks):
        micro_index = jnp.clip(tick_index - section_id, 0, micro_count - 1)
        incoming = jnp.where(
            section_id == 0, hidden_in[min(tick_index, micro_count - 1)], carried_rows
        )
        active = (tick_index - section_id >= 0) & (tick_index - section_id < micro_count)
        pair_active = active if micro_count == 1 and sections == 2 else None
        if pair_active is not None:
            expert_gather = functools.partial(paired_gather, active=active)
        else:
            def expert_gather(value, axis, split_axis):
                return lax.all_gather(value, "expert", axis=axis, tiled=True)
        segments = segment_ids[micro_index]
        lengths = prompt_lengths[micro_index]
        choices = expert_choice[0, micro_index]
        starts = jnp.cumsum(lengths) - lengths
        member = segments[:, None] == jnp.arange(lengths.shape[0], dtype=jnp.int32)[None, :]
        first_slot = jnp.sum(jnp.where(member, starts[None, :], 0), axis=1)
        positions = jnp.where(segments >= 0, slot_index - first_slot, 0).astype(jnp.float32)
        normed_full = norm_full_rows(incoming, attn_gain_full)
        projected = jnp.dot(
            normed_full, qkv_full.reshape(model_width, -1), preferred_element_type=jnp.float32
        )
        projected = projected.reshape(tokens_dev, kv_local, group + 2, head_width)
        queries = rotate_heads(projected[:, :, :group], positions).astype(jnp.bfloat16)
        key_rows = rotate_heads(projected[:, :, group], positions).astype(jnp.bfloat16)
        value_rows = projected[:, :, group + 1].astype(jnp.bfloat16)
        cache = jnp.stack(
            [key_rows.reshape(tokens_dev, -1), value_rows.reshape(tokens_dev, -1)], axis=1
        )
        kv_piece = expert_gather(cache.reshape(tokens_dev, -1), 0, 1)
        key_count = kv_piece.shape[0]
        kv_piece = kv_piece.reshape(key_count, 2, kv_local, head_width)
        key_slots = jnp.arange(key_count, dtype=jnp.int32)
        ends = jnp.cumsum(lengths)
        seg_piece = jnp.sum((key_slots[:, None] >= ends[None, :]).astype(jnp.int32), axis=1)
        seg_piece = jnp.where(key_slots < ends[-1], seg_piece, -1)
        allowed = (segments[:, None] == seg_piece[None, :]) & (segments[:, None] >= 0) & (
            key_slots[None, :] <= slot_index[:, None]
        ) | (key_slots[None, :] == slot_index[:, None])
        scores = (
            jnp.einsum(
                "tagd,nad->tagn", queries, kv_piece[:, 0], preferred_element_type=jnp.float32
            )
            * scale
        )
        weights_full = jnp.where(allowed[:, None, None, :], jnp.exp(scores), 0.0)
        numerator = jnp.einsum(
            "tagn,nad->tagd",
            weights_full.astype(jnp.bfloat16),
            kv_piece[:, 1],
            preferred_element_type=jnp.float32,
        )
        numerator, denominator = (numerator, jnp.sum(weights_full, axis=-1))
        attended = (numerator / denominator[..., None]).astype(jnp.bfloat16).reshape(tokens_dev, -1)
        attended_all = expert_gather(attended, 0, 1)
        attn_terms = lax.dot_general(
            attended_all, out_local, (((1,), (1,)), ((), ())), preferred_element_type=jnp.float32
        )
        attn_sum = terms_to_slots(attn_terms.astype(jnp.bfloat16), pair_active).astype(jnp.float32)
        after_attn = (incoming.astype(jnp.float32) + attn_sum).astype(jnp.bfloat16)
        moe_rows = norm_full_rows(after_attn, ffn_gain_full)
        moe_all = expert_gather(moe_rows, 0, 1)
        shared_hidden = jnp.dot(
            moe_all,
            shared_in_cols.reshape(model_width, 2 * shared_cols),
            preferred_element_type=jnp.float32,
        )
        shared_act = (
            jax.nn.silu(shared_hidden[:, :shared_cols]) * shared_hidden[:, shared_cols:]
        ).astype(jnp.bfloat16)
        shared_act = expert_gather(shared_act.T, 0, 1)
        shared_terms = lax.dot_general(
            shared_act,
            shared_down_local,
            (((0,), (1,)), ((), ())),
            preferred_element_type=jnp.float32,
        )
        shared_sum = terms_to_slots(shared_terms.astype(jnp.bfloat16), pair_active)
        shared_out = lax.optimization_barrier(shared_sum).astype(jnp.float32)
        logits = jnp.dot(
            moe_rows.astype(jnp.float32), router_full, precision=lax.Precision.HIGHEST
        )
        expert_ids = jnp.arange(logits.shape[1], dtype=jnp.int32)
        picked = jnp.sum(
            jnp.where(choices[:, :, None] == expert_ids[None, None, :], logits[:, None, :], 0.0),
            axis=2,
        )
        raised = jnp.exp(picked)
        gate_weights = raised / jnp.sum(raised, axis=1, keepdims=True)
        flat_choice = choices.reshape(-1)
        onehot = (flat_choice[:, None] == expert_ids[None, :]).astype(jnp.int32)
        slot_rank = jnp.sum(onehot * (running_count(onehot, 0) - onehot), axis=1)
        slot_ids = flat_choice * capacity + slot_rank
        choices_all = choices_every[:, micro_index]
        mine = jnp.any(choices_all == expert_id, axis=2)
        mine_rank = running_count(mine, 1) - 1
        source_ids = jnp.broadcast_to(
            jnp.arange(experts_count, dtype=jnp.int32)[:, None], mine.shape
        )
        token_ids = jnp.broadcast_to(jnp.arange(tokens_dev, dtype=jnp.int32)[None, :], mine.shape)
        rank_at = jnp.where(mine, mine_rank, capacity)
        table = (
            jnp.zeros((experts_count, capacity), jnp.int32)
            .at[source_ids, rank_at]
            .set(source_ids * tokens_dev + token_ids, mode="drop")
        )
        filled = (
            jnp.zeros((experts_count, capacity), jnp.bool_)
            .at[source_ids, rank_at]
            .set(True, mode="drop")
        )
        incoming_rows = jnp.where(filled[..., None], moe_all[table], jnp.zeros((), jnp.bfloat16))
        returned = expert_path(incoming_rows, w_in_local, w_down_local, pair_active)
        combined = returned.reshape(experts_count * capacity, columns)[slot_ids].astype(jnp.float32)
        combined = combined * gate_weights.reshape(-1)[:, None]
        moe_out = jnp.sum(combined.reshape(tokens_dev, top_count, columns), axis=1)
        output = (after_attn.astype(jnp.float32) + shared_out + moe_out).astype(jnp.bfloat16)
        output, cache = (output, cache)
        states = jnp.where(active, states.at[micro_index].set(output), states)
        caches = jnp.where(active, caches.at[micro_index].set(cache), caches)
        if tick_index + 1 < ticks:
            carried_rows = passed_along(output, "section", 1)
    return (states[None], caches[None])


def solution(mesh):
    placed = (
        P(None, "expert", "tensor"),
        P(None, "expert"),
        P(),
        P("section", None, "expert", None),
        P("section", "tensor"),
        P("section", "tensor"),
        P("section", "expert", "tensor", None),
        P("section", "expert", "tensor"),
        P("section", "expert", None, "tensor"),
        P("section", "expert", "tensor"),
        P("section", "tensor", None),
        P("section", "expert", None, None, "tensor"),
        P("section", "expert", "tensor", None),
    )
    return jax.shard_map(
        local,
        mesh=mesh,
        in_specs=placed,
        out_specs=(
            P("section", None, "expert", "tensor"),
            P("section", None, "expert", None, "tensor"),
        ),
        check_vma=False,
    )
```

```python
import functools

import jax
import jax.numpy as jnp
from jax import lax
from jax.sharding import PartitionSpec as P

HD = 128


NORM_EPS = 1e-05
ROPE_BASE = 500000.0


def passed_along(value, axis, steps):
    count = lax.axis_size(axis)
    leading, last = (max(0, -steps), min(count, count - steps))
    return lax.ppermute(value, axis, [(source, source + steps) for source in range(leading, last)])


def rotate_heads(values_in, positions):
    head_width = values_in.shape[-1]
    half_width = head_width // 2
    frequency = ROPE_BASE ** (-(jnp.arange(half_width, dtype=jnp.float32) * (2.0 / head_width)))
    angles = positions[:, None] * frequency[None, :]
    angles = angles.reshape((positions.shape[0],) + (1,) * (values_in.ndim - 2) + (half_width,))
    cosines = jnp.cos(angles)
    sines = jnp.sin(angles)
    first_half = values_in[..., :half_width]
    second_half = values_in[..., half_width:]
    return jnp.concatenate(
        [first_half * cosines - second_half * sines, second_half * cosines + first_half * sines],
        axis=-1,
    )


def norm_full_rows(values_in, gain_full):
    widened = tensor_gather(values_in, 1).astype(jnp.float32)
    squares = jnp.mean(widened * widened, axis=-1)
    return (widened * lax.rsqrt(squares + NORM_EPS)[:, None] * gain_full).astype(jnp.bfloat16)


def swap_cores(value):
    count = lax.axis_size("section")
    return lax.ppermute(value, "section", [(source, (source + 1) % count) for source in range(count)])


def paired_gather(value, axis, split_axis, active):
    value = jnp.where(active, value, swap_cores(value))
    first, second = jnp.split(value, 2, axis=split_axis)
    gathered = lax.all_gather(jnp.where(active, first, second), "expert", axis=axis, tiled=True)
    theirs = swap_cores(gathered)
    lead = jnp.where(active, gathered, theirs)
    trail = jnp.where(active, theirs, gathered)
    return jnp.concatenate([lead, trail], axis=split_axis)


def running_count(flags, axis):
    size = flags.shape[axis]
    steps = jnp.arange(size, dtype=jnp.int32)
    lower = (steps[:, None] >= steps[None, :]).astype(jnp.bfloat16)
    counted = jnp.tensordot(lower, flags.astype(jnp.bfloat16), axes=((1,), (axis,)),
                            preferred_element_type=jnp.float32)
    return jnp.moveaxis(counted, 0, axis).astype(jnp.int32)


def swap_tensor(value):
    count = lax.axis_size("tensor")
    return lax.ppermute(value, "tensor", [(source, (source + 1) % count) for source in range(count)])


def tensor_sum_scatter(value, axis):
    if lax.axis_size("tensor") != 2:
        return lax.psum_scatter(value, "tensor", scatter_dimension=axis, tiled=True)
    first, second = jnp.split(value, 2, axis=axis)
    lower = lax.axis_index("tensor") == 0
    kept = jnp.where(lower, first, second)
    sent = jnp.where(lower, second, first)
    return (kept.astype(jnp.float32) + swap_tensor(sent).astype(jnp.float32)).astype(value.dtype)


def tensor_gather(value, axis):
    if lax.axis_size("tensor") != 2:
        return lax.all_gather(value, "tensor", axis=axis, tiled=True)
    other = swap_tensor(value)
    lower = lax.axis_index("tensor") == 0
    return jnp.concatenate(
        [jnp.where(lower, value, other), jnp.where(lower, other, value)], axis=axis
    )


def paired_apply(step, value, in_axis, out_axis, active):
    if active is None:
        return step(value)
    value = jnp.where(active, value, swap_cores(value))
    first, second = jnp.split(value, 2, axis=in_axis)
    done = step(jnp.where(active, first, second))
    theirs = swap_cores(done)
    return jnp.concatenate(
        [jnp.where(active, done, theirs), jnp.where(active, theirs, done)], axis=out_axis
    )


def layer_weights(shard, owner):
    count = lax.axis_size("expert")

    def step(part):
        return lax.all_gather(part, "expert", axis=0, tiled=False)

    stacked = paired_apply(step, shard, 0, 1, owner)
    return stacked.reshape((count * shard.shape[0],) + shard.shape[1:])


def terms_to_slots(terms, active):
    count = lax.axis_size("expert")
    blocks = terms.reshape(count, terms.shape[0] // count, terms.shape[1])

    def step(part):
        by_slot = lax.all_to_all(
            part.reshape(-1, part.shape[2]), "expert", split_axis=0, concat_axis=1, tiled=True
        )
        return tensor_sum_scatter(by_slot, 1)

    return paired_apply(step, blocks, 1, 0, active)


def expert_path(full_rows, w_in_local, w_down_local, active):
    sources, slot_count, model_width = full_rows.shape
    local_width = w_down_local.shape[0]
    hidden = jnp.dot(
        full_rows.reshape(sources * slot_count, model_width),
        w_in_local.reshape(model_width, 2 * local_width),
        preferred_element_type=jnp.float32,
    )
    activated = (jax.nn.silu(hidden[:, :local_width]) * hidden[:, local_width:]).astype(
        jnp.bfloat16
    )
    partial_value = jnp.dot(activated, w_down_local, preferred_element_type=jnp.float32)
    partial_value = partial_value.reshape(sources, slot_count, model_width)

    def step(part):
        summed = tensor_sum_scatter(part, 2)
        return lax.all_to_all(summed, "expert", split_axis=0, concat_axis=0, tiled=True)

    return paired_apply(step, partial_value.astype(jnp.bfloat16), 1, 1, active)


def local(
    hidden_in,
    segment_ids,
    prompt_lengths,
    expert_choice,
    attn_gain,
    ffn_gain,
    w_qkv,
    w_out,
    w_shared_in,
    w_shared_down,
    router_weight,
    w_in,
    w_down,
):
    sections = lax.axis_size("section")
    section_id = lax.axis_index("section")
    experts_count = lax.axis_size("expert")
    expert_id = lax.axis_index("expert")
    micro_count, tokens_dev, columns = hidden_in.shape
    micro_count = hidden_in.shape[0]
    relay_pairs = micro_count == 1 and sections == 2
    qkv_own = w_qkv[0]
    if relay_pairs:
        qkv_full = layer_weights(qkv_own, section_id == 0)
    else:
        qkv_full = lax.all_gather(qkv_own, "expert", axis=0, tiled=True)
    out_local = w_out[0]
    shared_down_local = w_shared_down[0]
    shared_in_cols = lax.all_to_all(w_shared_in[0], "expert", split_axis=2, concat_axis=0, tiled=True)
    choices_every = lax.all_gather(expert_choice[0], "expert", axis=0, tiled=False)
    router_full = lax.all_gather(router_weight[0], "tensor", axis=0, tiled=True)
    attn_gain_full = lax.all_gather(attn_gain[0], "tensor", axis=0, tiled=True)
    ffn_gain_full = lax.all_gather(ffn_gain[0], "tensor", axis=0, tiled=True)
    w_in_local = w_in[0, 0]
    w_down_local = w_down[0, 0]
    (
        qkv_full,
        shared_in_cols,
        choices_every,
        router_full,
        attn_gain_full,
        ffn_gain_full,
        w_in_local,
        w_down_local,
    ) = lax.optimization_barrier(
        (
            qkv_full,
            shared_in_cols,
            choices_every,
            router_full,
            attn_gain_full,
            ffn_gain_full,
            w_in_local,
            w_down_local,
        )
    )
    model_width, kv_local, group_cols = qkv_full.shape
    qkv_layers = [qkv_full]
    shared_cols = shared_in_cols.shape[2]
    head_width = HD
    group = group_cols // head_width - 2
    scale = head_width ** (-0.5)
    top_count = expert_choice.shape[-1]
    capacity = 5 * tokens_dev * top_count // (4 * experts_count)
    slot_index = expert_id * tokens_dev + jnp.arange(tokens_dev, dtype=jnp.int32)
    carried_rows = jnp.zeros((tokens_dev, columns), jnp.bfloat16)
    states = jnp.zeros((micro_count, tokens_dev, columns), jnp.bfloat16)
    caches = jnp.zeros((micro_count, tokens_dev, 2, kv_local * head_width), jnp.bfloat16)
    ticks = micro_count + sections - 1
    for tick_index in range(ticks):
        micro_index = jnp.clip(tick_index - section_id, 0, micro_count - 1)
        incoming = jnp.where(
            section_id == 0, hidden_in[min(tick_index, micro_count - 1)], carried_rows
        )
        active = (tick_index - section_id >= 0) & (tick_index - section_id < micro_count)
        pair_active = active if micro_count == 1 and sections == 2 else None
        if pair_active is not None:
            expert_gather = functools.partial(paired_gather, active=active)
        else:
            def expert_gather(value, axis, split_axis):
                return lax.all_gather(value, "expert", axis=axis, tiled=True)
        segments = segment_ids[micro_index]
        lengths = prompt_lengths[micro_index]
        choices = expert_choice[0, micro_index]
        starts = jnp.cumsum(lengths) - lengths
        member = segments[:, None] == jnp.arange(lengths.shape[0], dtype=jnp.int32)[None, :]
        first_slot = jnp.sum(jnp.where(member, starts[None, :], 0), axis=1)
        positions = jnp.where(segments >= 0, slot_index - first_slot, 0).astype(jnp.float32)
        normed_full = norm_full_rows(incoming, attn_gain_full)
        projected = jnp.dot(
            normed_full,
            qkv_layers[min(tick_index, len(qkv_layers) - 1)].reshape(model_width, -1),
            preferred_element_type=jnp.float32,
        )
        projected = projected.reshape(tokens_dev, kv_local, group + 2, head_width)
        queries = rotate_heads(projected[:, :, :group], positions).astype(jnp.bfloat16)
        key_rows = rotate_heads(projected[:, :, group], positions).astype(jnp.bfloat16)
        value_rows = projected[:, :, group + 1].astype(jnp.bfloat16)
        cache = jnp.stack(
            [key_rows.reshape(tokens_dev, -1), value_rows.reshape(tokens_dev, -1)], axis=1
        )
        kv_piece = expert_gather(cache.reshape(tokens_dev, -1), 0, 1)
        key_count = kv_piece.shape[0]
        kv_piece = kv_piece.reshape(key_count, 2, kv_local, head_width)
        key_slots = jnp.arange(key_count, dtype=jnp.int32)
        ends = jnp.cumsum(lengths)
        seg_piece = jnp.sum((key_slots[:, None] >= ends[None, :]).astype(jnp.int32), axis=1)
        seg_piece = jnp.where(key_slots < ends[-1], seg_piece, -1)
        allowed = (segments[:, None] == seg_piece[None, :]) & (segments[:, None] >= 0) & (
            key_slots[None, :] <= slot_index[:, None]
        ) | (key_slots[None, :] == slot_index[:, None])
        scores = (
            jnp.einsum(
                "tagd,nad->tagn", queries, kv_piece[:, 0], preferred_element_type=jnp.float32
            )
            * scale
        )
        weights_full = jnp.where(allowed[:, None, None, :], jnp.exp(scores), 0.0)
        numerator = jnp.einsum(
            "tagn,nad->tagd",
            weights_full.astype(jnp.bfloat16),
            kv_piece[:, 1],
            preferred_element_type=jnp.float32,
        )
        numerator, denominator = (numerator, jnp.sum(weights_full, axis=-1))
        attended = (numerator / denominator[..., None]).astype(jnp.bfloat16).reshape(tokens_dev, -1)
        attended_all = expert_gather(attended, 0, 1)
        attn_terms = lax.dot_general(
            attended_all, out_local, (((1,), (1,)), ((), ())), preferred_element_type=jnp.float32
        )
        attn_sum = terms_to_slots(attn_terms.astype(jnp.bfloat16), pair_active).astype(jnp.float32)
        after_attn = (incoming.astype(jnp.float32) + attn_sum).astype(jnp.bfloat16)
        moe_rows = norm_full_rows(after_attn, ffn_gain_full)
        moe_all = expert_gather(moe_rows, 0, 1)
        shared_hidden = jnp.dot(
            moe_all,
            shared_in_cols.reshape(model_width, 2 * shared_cols),
            preferred_element_type=jnp.float32,
        )
        shared_act = (
            jax.nn.silu(shared_hidden[:, :shared_cols]) * shared_hidden[:, shared_cols:]
        ).astype(jnp.bfloat16)
        shared_act = expert_gather(shared_act.T, 0, 1)
        if relay_pairs and tick_index == 0:
            qkv_later, _ = lax.optimization_barrier((qkv_own, shared_act))
            qkv_layers.append(layer_weights(qkv_later, section_id == 1))
        shared_terms = lax.dot_general(
            shared_act,
            shared_down_local,
            (((0,), (1,)), ((), ())),
            preferred_element_type=jnp.float32,
        )
        shared_sum = terms_to_slots(shared_terms.astype(jnp.bfloat16), pair_active)
        shared_out = lax.optimization_barrier(shared_sum).astype(jnp.float32)
        logits = jnp.dot(
            moe_rows.astype(jnp.float32), router_full, precision=lax.Precision.HIGHEST
        )
        expert_ids = jnp.arange(logits.shape[1], dtype=jnp.int32)
        picked = jnp.sum(
            jnp.where(choices[:, :, None] == expert_ids[None, None, :], logits[:, None, :], 0.0),
            axis=2,
        )
        raised = jnp.exp(picked)
        gate_weights = raised / jnp.sum(raised, axis=1, keepdims=True)
        flat_choice = choices.reshape(-1)
        onehot = (flat_choice[:, None] == expert_ids[None, :]).astype(jnp.int32)
        slot_rank = jnp.sum(onehot * (running_count(onehot, 0) - onehot), axis=1)
        slot_ids = flat_choice * capacity + slot_rank
        choices_all = choices_every[:, micro_index]
        mine = jnp.any(choices_all == expert_id, axis=2)
        mine_rank = running_count(mine, 1) - 1
        source_ids = jnp.broadcast_to(
            jnp.arange(experts_count, dtype=jnp.int32)[:, None], mine.shape
        )
        token_ids = jnp.broadcast_to(jnp.arange(tokens_dev, dtype=jnp.int32)[None, :], mine.shape)
        rank_at = jnp.where(mine, mine_rank, capacity)
        table = (
            jnp.zeros((experts_count, capacity), jnp.int32)
            .at[source_ids, rank_at]
            .set(source_ids * tokens_dev + token_ids, mode="drop")
        )
        filled = (
            jnp.zeros((experts_count, capacity), jnp.bool_)
            .at[source_ids, rank_at]
            .set(True, mode="drop")
        )
        incoming_rows = jnp.where(filled[..., None], moe_all[table], jnp.zeros((), jnp.bfloat16))
        returned = expert_path(incoming_rows, w_in_local, w_down_local, pair_active)
        combined = returned.reshape(experts_count * capacity, columns)[slot_ids].astype(jnp.float32)
        combined = combined * gate_weights.reshape(-1)[:, None]
        moe_out = jnp.sum(combined.reshape(tokens_dev, top_count, columns), axis=1)
        output = (after_attn.astype(jnp.float32) + shared_out + moe_out).astype(jnp.bfloat16)
        output, cache = (output, cache)
        states = jnp.where(active, states.at[micro_index].set(output), states)
        caches = jnp.where(active, caches.at[micro_index].set(cache), caches)
        if tick_index + 1 < ticks:
            carried_rows = passed_along(output, "section", 1)
    return (states[None], caches[None])


def solution(mesh):
    placed = (
        P(None, "expert", "tensor"),
        P(None, "expert"),
        P(),
        P("section", None, "expert", None),
        P("section", "tensor"),
        P("section", "tensor"),
        P("section", "expert", "tensor", None),
        P("section", "expert", "tensor"),
        P("section", "expert", None, "tensor"),
        P("section", "expert", "tensor"),
        P("section", "tensor", None),
        P("section", "expert", None, None, "tensor"),
        P("section", "expert", "tensor", None),
    )
    return jax.shard_map(
        local,
        mesh=mesh,
        in_specs=placed,
        out_specs=(
            P("section", None, "expert", "tensor"),
            P("section", None, "expert", None, "tensor"),
        ),
        check_vma=False,
    )
```

```python
import functools

import jax
import jax.numpy as jnp
from jax import lax
from jax.sharding import PartitionSpec as P

HD = 128


NORM_EPS = 1e-05
ROPE_BASE = 500000.0


def passed_along(value, axis, steps):
    count = lax.axis_size(axis)
    leading, last = (max(0, -steps), min(count, count - steps))
    return lax.ppermute(value, axis, [(source, source + steps) for source in range(leading, last)])


def rotate_heads(values_in, positions):
    head_width = values_in.shape[-1]
    half_width = head_width // 2
    frequency = ROPE_BASE ** (-(jnp.arange(half_width, dtype=jnp.float32) * (2.0 / head_width)))
    angles = positions[:, None] * frequency[None, :]
    angles = angles.reshape((positions.shape[0],) + (1,) * (values_in.ndim - 2) + (half_width,))
    cosines = jnp.cos(angles)
    sines = jnp.sin(angles)
    first_half = values_in[..., :half_width]
    second_half = values_in[..., half_width:]
    return jnp.concatenate(
        [first_half * cosines - second_half * sines, second_half * cosines + first_half * sines],
        axis=-1,
    )


def norm_full_rows(values_in, gain_full):
    widened = tensor_gather(values_in, 1).astype(jnp.float32)
    squares = jnp.mean(widened * widened, axis=-1)
    return (widened * lax.rsqrt(squares + NORM_EPS)[:, None] * gain_full).astype(jnp.bfloat16)


def swap_cores(value):
    count = lax.axis_size("section")
    return lax.ppermute(value, "section", [(source, (source + 1) % count) for source in range(count)])


def paired_gather(value, axis, split_axis, active):
    value = jnp.where(active, value, swap_cores(value))
    first, second = jnp.split(value, 2, axis=split_axis)
    gathered = lax.all_gather(jnp.where(active, first, second), "expert", axis=axis, tiled=True)
    theirs = swap_cores(gathered)
    lead = jnp.where(active, gathered, theirs)
    trail = jnp.where(active, theirs, gathered)
    return jnp.concatenate([lead, trail], axis=split_axis)


def running_count(flags, axis):
    size = flags.shape[axis]
    steps = jnp.arange(size, dtype=jnp.int32)
    lower = (steps[:, None] >= steps[None, :]).astype(jnp.bfloat16)
    counted = jnp.tensordot(lower, flags.astype(jnp.bfloat16), axes=((1,), (axis,)),
                            preferred_element_type=jnp.float32)
    return jnp.moveaxis(counted, 0, axis).astype(jnp.int32)


def swap_tensor(value):
    count = lax.axis_size("tensor")
    return lax.ppermute(value, "tensor", [(source, (source + 1) % count) for source in range(count)])


def tensor_sum_scatter(value, axis):
    if lax.axis_size("tensor") != 2:
        return lax.psum_scatter(value, "tensor", scatter_dimension=axis, tiled=True)
    first, second = jnp.split(value, 2, axis=axis)
    lower = lax.axis_index("tensor") == 0
    kept = jnp.where(lower, first, second)
    sent = jnp.where(lower, second, first)
    return (kept.astype(jnp.float32) + swap_tensor(sent).astype(jnp.float32)).astype(value.dtype)


def tensor_gather(value, axis):
    if lax.axis_size("tensor") != 2:
        return lax.all_gather(value, "tensor", axis=axis, tiled=True)
    other = swap_tensor(value)
    lower = lax.axis_index("tensor") == 0
    return jnp.concatenate(
        [jnp.where(lower, value, other), jnp.where(lower, other, value)], axis=axis
    )


def paired_apply(step, value, in_axis, out_axis, active):
    if active is None:
        return step(value)
    value = jnp.where(active, value, swap_cores(value))
    first, second = jnp.split(value, 2, axis=in_axis)
    done = step(jnp.where(active, first, second))
    theirs = swap_cores(done)
    return jnp.concatenate(
        [jnp.where(active, done, theirs), jnp.where(active, theirs, done)], axis=out_axis
    )


def layer_weights(shard, owner):
    count = lax.axis_size("expert")

    def step(part):
        return lax.all_gather(part, "expert", axis=0, tiled=False)

    stacked = paired_apply(step, shard, 0, 1, owner)
    return stacked.reshape((count * shard.shape[0],) + shard.shape[1:])


def terms_to_slots(terms, active):
    count = lax.axis_size("expert")
    blocks = terms.reshape(count, terms.shape[0] // count, terms.shape[1])

    def step(part):
        by_slot = lax.all_to_all(
            part.reshape(-1, part.shape[2]), "expert", split_axis=0, concat_axis=1, tiled=True
        )
        return tensor_sum_scatter(by_slot, 1)

    return paired_apply(step, blocks, 1, 0, active)


def expert_path(full_rows, w_in_local, w_down_local, active):
    sources, slot_count, model_width = full_rows.shape
    local_width = w_down_local.shape[0]
    hidden = jnp.dot(
        full_rows.reshape(sources * slot_count, model_width),
        w_in_local.reshape(model_width, 2 * local_width),
        preferred_element_type=jnp.float32,
    )
    activated = (jax.nn.silu(hidden[:, :local_width]) * hidden[:, local_width:]).astype(
        jnp.bfloat16
    )
    partial_value = jnp.dot(activated, w_down_local, preferred_element_type=jnp.float32)
    partial_value = partial_value.reshape(sources, slot_count, model_width)

    def step(part):
        summed = tensor_sum_scatter(part, 2)
        return lax.all_to_all(summed, "expert", split_axis=0, concat_axis=0, tiled=True)

    return paired_apply(step, partial_value.astype(jnp.bfloat16), 1, 1, active)


def local(
    hidden_in,
    segment_ids,
    prompt_lengths,
    expert_choice,
    attn_gain,
    ffn_gain,
    w_qkv,
    w_out,
    w_shared_in,
    w_shared_down,
    router_weight,
    w_in,
    w_down,
):
    sections = lax.axis_size("section")
    section_id = lax.axis_index("section")
    experts_count = lax.axis_size("expert")
    expert_id = lax.axis_index("expert")
    micro_count, tokens_dev, columns = hidden_in.shape
    micro_count = hidden_in.shape[0]
    relay_pairs = micro_count == 1 and sections == 2
    qkv_own = w_qkv[0]
    if relay_pairs:
        qkv_full = layer_weights(qkv_own, section_id == 0)
    else:
        qkv_full = lax.all_gather(qkv_own, "expert", axis=0, tiled=True)
    out_local = w_out[0]
    shared_down_local = w_shared_down[0]
    shared_in_cols = lax.all_to_all(w_shared_in[0], "expert", split_axis=2, concat_axis=0, tiled=True)
    choices_every = lax.all_gather(expert_choice[0], "expert", axis=0, tiled=False)
    router_full = lax.all_gather(router_weight[0], "tensor", axis=0, tiled=True)
    attn_gain_full = lax.all_gather(attn_gain[0], "tensor", axis=0, tiled=True)
    ffn_gain_full = lax.all_gather(ffn_gain[0], "tensor", axis=0, tiled=True)
    w_in_local = w_in[0, 0]
    w_down_local = w_down[0, 0]
    (
        qkv_full,
        shared_in_cols,
        choices_every,
        router_full,
        attn_gain_full,
        ffn_gain_full,
        w_in_local,
        w_down_local,
    ) = lax.optimization_barrier(
        (
            qkv_full,
            shared_in_cols,
            choices_every,
            router_full,
            attn_gain_full,
            ffn_gain_full,
            w_in_local,
            w_down_local,
        )
    )
    model_width, kv_local, group_cols = qkv_full.shape
    qkv_layers = [qkv_full]
    if relay_pairs:
        qkv_layers.append(layer_weights(qkv_own, section_id == 1))
    shared_cols = shared_in_cols.shape[2]
    head_width = HD
    group = group_cols // head_width - 2
    scale = head_width ** (-0.5)
    top_count = expert_choice.shape[-1]
    capacity = 5 * tokens_dev * top_count // (4 * experts_count)
    slot_index = expert_id * tokens_dev + jnp.arange(tokens_dev, dtype=jnp.int32)
    carried_rows = jnp.zeros((tokens_dev, columns), jnp.bfloat16)
    states = jnp.zeros((micro_count, tokens_dev, columns), jnp.bfloat16)
    caches = jnp.zeros((micro_count, tokens_dev, 2, kv_local * head_width), jnp.bfloat16)
    ticks = micro_count + sections - 1
    for tick_index in range(ticks):
        micro_index = jnp.clip(tick_index - section_id, 0, micro_count - 1)
        incoming = jnp.where(
            section_id == 0, hidden_in[min(tick_index, micro_count - 1)], carried_rows
        )
        active = (tick_index - section_id >= 0) & (tick_index - section_id < micro_count)
        pair_active = active if micro_count == 1 and sections == 2 else None
        if pair_active is not None:
            expert_gather = functools.partial(paired_gather, active=active)
        else:
            def expert_gather(value, axis, split_axis):
                return lax.all_gather(value, "expert", axis=axis, tiled=True)
        segments = segment_ids[micro_index]
        lengths = prompt_lengths[micro_index]
        choices = expert_choice[0, micro_index]
        starts = jnp.cumsum(lengths) - lengths
        member = segments[:, None] == jnp.arange(lengths.shape[0], dtype=jnp.int32)[None, :]
        first_slot = jnp.sum(jnp.where(member, starts[None, :], 0), axis=1)
        positions = jnp.where(segments >= 0, slot_index - first_slot, 0).astype(jnp.float32)
        normed_full = norm_full_rows(incoming, attn_gain_full)
        projected = jnp.dot(
            normed_full,
            qkv_layers[min(tick_index, len(qkv_layers) - 1)].reshape(model_width, -1),
            preferred_element_type=jnp.float32,
        )
        projected = projected.reshape(tokens_dev, kv_local, group + 2, head_width)
        queries = rotate_heads(projected[:, :, :group], positions).astype(jnp.bfloat16)
        key_rows = rotate_heads(projected[:, :, group], positions).astype(jnp.bfloat16)
        value_rows = projected[:, :, group + 1].astype(jnp.bfloat16)
        cache = jnp.stack(
            [key_rows.reshape(tokens_dev, -1), value_rows.reshape(tokens_dev, -1)], axis=1
        )
        kv_piece = expert_gather(cache.reshape(tokens_dev, -1), 0, 1)
        key_count = kv_piece.shape[0]
        kv_piece = kv_piece.reshape(key_count, 2, kv_local, head_width)
        key_slots = jnp.arange(key_count, dtype=jnp.int32)
        ends = jnp.cumsum(lengths)
        seg_piece = jnp.sum((key_slots[:, None] >= ends[None, :]).astype(jnp.int32), axis=1)
        seg_piece = jnp.where(key_slots < ends[-1], seg_piece, -1)
        allowed = (segments[:, None] == seg_piece[None, :]) & (segments[:, None] >= 0) & (
            key_slots[None, :] <= slot_index[:, None]
        ) | (key_slots[None, :] == slot_index[:, None])
        scores = (
            jnp.einsum(
                "tagd,nad->tagn", queries, kv_piece[:, 0], preferred_element_type=jnp.float32
            )
            * scale
        )
        weights_full = jnp.where(allowed[:, None, None, :], jnp.exp(scores), 0.0)
        numerator = jnp.einsum(
            "tagn,nad->tagd",
            weights_full.astype(jnp.bfloat16),
            kv_piece[:, 1],
            preferred_element_type=jnp.float32,
        )
        numerator, denominator = (numerator, jnp.sum(weights_full, axis=-1))
        attended = (numerator / denominator[..., None]).astype(jnp.bfloat16).reshape(tokens_dev, -1)
        attended_all = expert_gather(attended, 0, 1)
        attn_terms = lax.dot_general(
            attended_all, out_local, (((1,), (1,)), ((), ())), preferred_element_type=jnp.float32
        )
        attn_sum = terms_to_slots(attn_terms.astype(jnp.bfloat16), pair_active).astype(jnp.float32)
        after_attn = (incoming.astype(jnp.float32) + attn_sum).astype(jnp.bfloat16)
        moe_rows = norm_full_rows(after_attn, ffn_gain_full)
        moe_all = expert_gather(moe_rows, 0, 1)
        shared_hidden = jnp.dot(
            moe_all,
            shared_in_cols.reshape(model_width, 2 * shared_cols),
            preferred_element_type=jnp.float32,
        )
        shared_act = (
            jax.nn.silu(shared_hidden[:, :shared_cols]) * shared_hidden[:, shared_cols:]
        ).astype(jnp.bfloat16)
        shared_act = expert_gather(shared_act.T, 0, 1)
        shared_terms = lax.dot_general(
            shared_act,
            shared_down_local,
            (((0,), (1,)), ((), ())),
            preferred_element_type=jnp.float32,
        )
        shared_sum = terms_to_slots(shared_terms.astype(jnp.bfloat16), pair_active)
        shared_out = lax.optimization_barrier(shared_sum).astype(jnp.float32)
        logits = jnp.dot(
            moe_rows.astype(jnp.float32), router_full, precision=lax.Precision.HIGHEST
        )
        expert_ids = jnp.arange(logits.shape[1], dtype=jnp.int32)
        picked = jnp.sum(
            jnp.where(choices[:, :, None] == expert_ids[None, None, :], logits[:, None, :], 0.0),
            axis=2,
        )
        raised = jnp.exp(picked)
        gate_weights = raised / jnp.sum(raised, axis=1, keepdims=True)
        flat_choice = choices.reshape(-1)
        onehot = (flat_choice[:, None] == expert_ids[None, :]).astype(jnp.int32)
        slot_rank = jnp.sum(onehot * (running_count(onehot, 0) - onehot), axis=1)
        slot_ids = flat_choice * capacity + slot_rank
        choices_all = choices_every[:, micro_index]
        mine = jnp.any(choices_all == expert_id, axis=2)
        mine_rank = running_count(mine, 1) - 1
        source_ids = jnp.broadcast_to(
            jnp.arange(experts_count, dtype=jnp.int32)[:, None], mine.shape
        )
        token_ids = jnp.broadcast_to(jnp.arange(tokens_dev, dtype=jnp.int32)[None, :], mine.shape)
        rank_at = jnp.where(mine, mine_rank, capacity)
        table = (
            jnp.zeros((experts_count, capacity), jnp.int32)
            .at[source_ids, rank_at]
            .set(source_ids * tokens_dev + token_ids, mode="drop")
        )
        filled = (
            jnp.zeros((experts_count, capacity), jnp.bool_)
            .at[source_ids, rank_at]
            .set(True, mode="drop")
        )
        incoming_rows = jnp.where(filled[..., None], moe_all[table], jnp.zeros((), jnp.bfloat16))
        returned = expert_path(incoming_rows, w_in_local, w_down_local, pair_active)
        combined = returned.reshape(experts_count * capacity, columns)[slot_ids].astype(jnp.float32)
        combined = combined * gate_weights.reshape(-1)[:, None]
        moe_out = jnp.sum(combined.reshape(tokens_dev, top_count, columns), axis=1)
        output = (after_attn.astype(jnp.float32) + shared_out + moe_out).astype(jnp.bfloat16)
        output, cache = (output, cache)
        states = jnp.where(active, states.at[micro_index].set(output), states)
        caches = jnp.where(active, caches.at[micro_index].set(cache), caches)
        if tick_index + 1 < ticks:
            carried_rows = passed_along(output, "section", 1)
    return (states[None], caches[None])


def solution(mesh):
    placed = (
        P(None, "expert", "tensor"),
        P(None, "expert"),
        P(),
        P("section", None, "expert", None),
        P("section", "tensor"),
        P("section", "tensor"),
        P("section", "expert", "tensor", None),
        P("section", "expert", "tensor"),
        P("section", "expert", None, "tensor"),
        P("section", "expert", "tensor"),
        P("section", "tensor", None),
        P("section", "expert", None, None, "tensor"),
        P("section", "expert", "tensor", None),
    )
    return jax.shard_map(
        local,
        mesh=mesh,
        in_specs=placed,
        out_specs=(
            P("section", None, "expert", "tensor"),
            P("section", None, "expert", None, "tensor"),
        ),
        check_vma=False,
    )
```

```python
import functools

import jax
import jax.numpy as jnp
from jax import lax
from jax.sharding import PartitionSpec as P

HD = 128


NORM_EPS = 1e-05
ROPE_BASE = 500000.0


def passed_along(value, axis, steps):
    count = lax.axis_size(axis)
    leading, last = (max(0, -steps), min(count, count - steps))
    return lax.ppermute(value, axis, [(source, source + steps) for source in range(leading, last)])


def rotate_heads(values_in, positions):
    head_width = values_in.shape[-1]
    half_width = head_width // 2
    frequency = ROPE_BASE ** (-(jnp.arange(half_width, dtype=jnp.float32) * (2.0 / head_width)))
    angles = positions[:, None] * frequency[None, :]
    angles = angles.reshape((positions.shape[0],) + (1,) * (values_in.ndim - 2) + (half_width,))
    cosines = jnp.cos(angles)
    sines = jnp.sin(angles)
    first_half = values_in[..., :half_width]
    second_half = values_in[..., half_width:]
    return jnp.concatenate(
        [first_half * cosines - second_half * sines, second_half * cosines + first_half * sines],
        axis=-1,
    )


def norm_full_rows(values_in, gain_full):
    widened = tensor_gather(values_in, 1).astype(jnp.float32)
    squares = jnp.mean(widened * widened, axis=-1)
    return (widened * lax.rsqrt(squares + NORM_EPS)[:, None] * gain_full).astype(jnp.bfloat16)


def swap_cores(value):
    count = lax.axis_size("section")
    return lax.ppermute(value, "section", [(source, (source + 1) % count) for source in range(count)])


def paired_gather(value, axis, split_axis, active):
    value = jnp.where(active, value, swap_cores(value))
    first, second = jnp.split(value, 2, axis=split_axis)
    gathered = lax.all_gather(jnp.where(active, first, second), "expert", axis=axis, tiled=True)
    theirs = swap_cores(gathered)
    lead = jnp.where(active, gathered, theirs)
    trail = jnp.where(active, theirs, gathered)
    return jnp.concatenate([lead, trail], axis=split_axis)


def running_count(flags, axis):
    size = flags.shape[axis]
    steps = jnp.arange(size, dtype=jnp.int32)
    lower = (steps[:, None] >= steps[None, :]).astype(jnp.bfloat16)
    counted = jnp.tensordot(lower, flags.astype(jnp.bfloat16), axes=((1,), (axis,)),
                            preferred_element_type=jnp.float32)
    return jnp.moveaxis(counted, 0, axis).astype(jnp.int32)


def swap_tensor(value):
    count = lax.axis_size("tensor")
    return lax.ppermute(value, "tensor", [(source, (source + 1) % count) for source in range(count)])


def tensor_sum_scatter(value, axis):
    if lax.axis_size("tensor") != 2:
        return lax.psum_scatter(value, "tensor", scatter_dimension=axis, tiled=True)
    first, second = jnp.split(value, 2, axis=axis)
    lower = lax.axis_index("tensor") == 0
    kept = jnp.where(lower, first, second)
    sent = jnp.where(lower, second, first)
    return (kept.astype(jnp.float32) + swap_tensor(sent).astype(jnp.float32)).astype(value.dtype)


def tensor_gather(value, axis):
    if lax.axis_size("tensor") != 2:
        return lax.all_gather(value, "tensor", axis=axis, tiled=True)
    other = swap_tensor(value)
    lower = lax.axis_index("tensor") == 0
    return jnp.concatenate(
        [jnp.where(lower, value, other), jnp.where(lower, other, value)], axis=axis
    )


def paired_apply(step, value, in_axis, out_axis, active):
    if active is None:
        return step(value)
    value = jnp.where(active, value, swap_cores(value))
    first, second = jnp.split(value, 2, axis=in_axis)
    done = step(jnp.where(active, first, second))
    theirs = swap_cores(done)
    return jnp.concatenate(
        [jnp.where(active, done, theirs), jnp.where(active, theirs, done)], axis=out_axis
    )


def terms_to_slots(terms, active):
    count = lax.axis_size("expert")
    blocks = terms.reshape(count, terms.shape[0] // count, terms.shape[1])

    def step(part):
        by_slot = lax.all_to_all(
            part.reshape(-1, part.shape[2]), "expert", split_axis=0, concat_axis=1, tiled=True
        )
        return tensor_sum_scatter(by_slot, 1)

    return paired_apply(step, blocks, 1, 0, active)


def expert_path(full_rows, w_in_local, w_down_local, active):
    sources, slot_count, model_width = full_rows.shape
    local_width = w_down_local.shape[0]
    hidden = jnp.dot(
        full_rows.reshape(sources * slot_count, model_width),
        w_in_local.reshape(model_width, 2 * local_width),
        preferred_element_type=jnp.float32,
    )
    activated = (jax.nn.silu(hidden[:, :local_width]) * hidden[:, local_width:]).astype(
        jnp.bfloat16
    )
    partial_value = jnp.dot(activated, w_down_local, preferred_element_type=jnp.float32)
    partial_value = partial_value.reshape(sources, slot_count, model_width)

    def step(part):
        summed = tensor_sum_scatter(part, 2)
        return lax.all_to_all(summed, "expert", split_axis=0, concat_axis=0, tiled=True)

    return paired_apply(step, partial_value.astype(jnp.bfloat16), 1, 1, active)


def local(
    hidden_in,
    segment_ids,
    prompt_lengths,
    expert_choice,
    attn_gain,
    ffn_gain,
    w_qkv,
    w_out,
    w_shared_in,
    w_shared_down,
    router_weight,
    w_in,
    w_down,
):
    sections = lax.axis_size("section")
    section_id = lax.axis_index("section")
    experts_count = lax.axis_size("expert")
    expert_id = lax.axis_index("expert")
    micro_count, tokens_dev, columns = hidden_in.shape
    qkv_blocks = lax.all_gather(w_qkv[0], "expert", axis=0, tiled=False)
    out_local = w_out[0]
    shared_down_local = w_shared_down[0]
    shared_in_cols = lax.all_to_all(w_shared_in[0], "expert", split_axis=2, concat_axis=0, tiled=True)
    choices_every = lax.all_gather(expert_choice[0], "expert", axis=0, tiled=False)
    router_full = lax.all_gather(router_weight[0], "tensor", axis=0, tiled=True)
    attn_gain_full = lax.all_gather(attn_gain[0], "tensor", axis=0, tiled=True)
    ffn_gain_full = lax.all_gather(ffn_gain[0], "tensor", axis=0, tiled=True)
    w_in_local = w_in[0, 0]
    w_down_local = w_down[0, 0]
    (
        qkv_blocks,
        shared_in_cols,
        choices_every,
        router_full,
        attn_gain_full,
        ffn_gain_full,
        w_in_local,
        w_down_local,
    ) = lax.optimization_barrier(
        (
            qkv_blocks,
            shared_in_cols,
            choices_every,
            router_full,
            attn_gain_full,
            ffn_gain_full,
            w_in_local,
            w_down_local,
        )
    )
    model_width = qkv_blocks.shape[0] * qkv_blocks.shape[1]
    kv_local, group_cols = qkv_blocks.shape[2:]
    shared_cols = shared_in_cols.shape[2]
    head_width = HD
    group = group_cols // head_width - 2
    scale = head_width ** (-0.5)
    top_count = expert_choice.shape[-1]
    capacity = 5 * tokens_dev * top_count // (4 * experts_count)
    slot_index = expert_id * tokens_dev + jnp.arange(tokens_dev, dtype=jnp.int32)
    carried_rows = jnp.zeros((tokens_dev, columns), jnp.bfloat16)
    states = jnp.zeros((micro_count, tokens_dev, columns), jnp.bfloat16)
    caches = jnp.zeros((micro_count, tokens_dev, 2, kv_local * head_width), jnp.bfloat16)
    ticks = micro_count + sections - 1
    for tick_index in range(ticks):
        micro_index = jnp.clip(tick_index - section_id, 0, micro_count - 1)
        incoming = jnp.where(
            section_id == 0, hidden_in[min(tick_index, micro_count - 1)], carried_rows
        )
        active = (tick_index - section_id >= 0) & (tick_index - section_id < micro_count)
        pair_active = active if micro_count == 1 and sections == 2 else None
        if pair_active is not None:
            expert_gather = functools.partial(paired_gather, active=active)
        else:
            def expert_gather(value, axis, split_axis):
                return lax.all_gather(value, "expert", axis=axis, tiled=True)
        segments = segment_ids[micro_index]
        lengths = prompt_lengths[micro_index]
        choices = expert_choice[0, micro_index]
        starts = jnp.cumsum(lengths) - lengths
        member = segments[:, None] == jnp.arange(lengths.shape[0], dtype=jnp.int32)[None, :]
        first_slot = jnp.sum(jnp.where(member, starts[None, :], 0), axis=1)
        positions = jnp.where(segments >= 0, slot_index - first_slot, 0).astype(jnp.float32)
        normed_full = norm_full_rows(incoming, attn_gain_full)
        projected = jnp.tensordot(
            normed_full.reshape(tokens_dev, qkv_blocks.shape[0], qkv_blocks.shape[1]),
            qkv_blocks.reshape(qkv_blocks.shape[0], qkv_blocks.shape[1], -1),
            axes=((1, 2), (0, 1)),
            preferred_element_type=jnp.float32,
        )
        projected = projected.reshape(tokens_dev, kv_local, group + 2, head_width)
        queries = rotate_heads(projected[:, :, :group], positions).astype(jnp.bfloat16)
        key_rows = rotate_heads(projected[:, :, group], positions).astype(jnp.bfloat16)
        value_rows = projected[:, :, group + 1].astype(jnp.bfloat16)
        cache = jnp.stack(
            [key_rows.reshape(tokens_dev, -1), value_rows.reshape(tokens_dev, -1)], axis=1
        )
        kv_piece = expert_gather(cache.reshape(tokens_dev, -1), 0, 1)
        key_count = kv_piece.shape[0]
        kv_piece = kv_piece.reshape(key_count, 2, kv_local, head_width)
        key_slots = jnp.arange(key_count, dtype=jnp.int32)
        ends = jnp.cumsum(lengths)
        seg_piece = jnp.sum((key_slots[:, None] >= ends[None, :]).astype(jnp.int32), axis=1)
        seg_piece = jnp.where(key_slots < ends[-1], seg_piece, -1)
        allowed = (segments[:, None] == seg_piece[None, :]) & (segments[:, None] >= 0) & (
            key_slots[None, :] <= slot_index[:, None]
        ) | (key_slots[None, :] == slot_index[:, None])
        scores = (
            jnp.einsum(
                "tagd,nad->tagn", queries, kv_piece[:, 0], preferred_element_type=jnp.float32
            )
            * scale
        )
        weights_full = jnp.where(allowed[:, None, None, :], jnp.exp(scores), 0.0)
        numerator = jnp.einsum(
            "tagn,nad->tagd",
            weights_full.astype(jnp.bfloat16),
            kv_piece[:, 1],
            preferred_element_type=jnp.float32,
        )
        numerator, denominator = (numerator, jnp.sum(weights_full, axis=-1))
        attended = (numerator / denominator[..., None]).astype(jnp.bfloat16).reshape(tokens_dev, -1)
        attended_all = expert_gather(attended, 0, 1)
        attn_terms = lax.dot_general(
            attended_all, out_local, (((1,), (1,)), ((), ())), preferred_element_type=jnp.float32
        )
        attn_sum = terms_to_slots(attn_terms.astype(jnp.bfloat16), pair_active).astype(jnp.float32)
        after_attn = (incoming.astype(jnp.float32) + attn_sum).astype(jnp.bfloat16)
        moe_rows = norm_full_rows(after_attn, ffn_gain_full)
        moe_all = expert_gather(moe_rows, 0, 1)
        shared_hidden = jnp.dot(
            moe_all,
            shared_in_cols.reshape(model_width, 2 * shared_cols),
            preferred_element_type=jnp.float32,
        )
        shared_act = (
            jax.nn.silu(shared_hidden[:, :shared_cols]) * shared_hidden[:, shared_cols:]
        ).astype(jnp.bfloat16)
        shared_act = expert_gather(shared_act.T, 0, 1)
        shared_terms = lax.dot_general(
            shared_act,
            shared_down_local,
            (((0,), (1,)), ((), ())),
            preferred_element_type=jnp.float32,
        )
        shared_sum = terms_to_slots(shared_terms.astype(jnp.bfloat16), pair_active)
        shared_out = lax.optimization_barrier(shared_sum).astype(jnp.float32)
        logits = jnp.dot(
            moe_rows.astype(jnp.float32), router_full, precision=lax.Precision.HIGHEST
        )
        expert_ids = jnp.arange(logits.shape[1], dtype=jnp.int32)
        picked = jnp.sum(
            jnp.where(choices[:, :, None] == expert_ids[None, None, :], logits[:, None, :], 0.0),
            axis=2,
        )
        raised = jnp.exp(picked)
        gate_weights = raised / jnp.sum(raised, axis=1, keepdims=True)
        flat_choice = choices.reshape(-1)
        onehot = (flat_choice[:, None] == expert_ids[None, :]).astype(jnp.int32)
        slot_rank = jnp.sum(onehot * (running_count(onehot, 0) - onehot), axis=1)
        slot_ids = flat_choice * capacity + slot_rank
        choices_all = choices_every[:, micro_index]
        mine = jnp.any(choices_all == expert_id, axis=2)
        mine_rank = running_count(mine, 1) - 1
        source_ids = jnp.broadcast_to(
            jnp.arange(experts_count, dtype=jnp.int32)[:, None], mine.shape
        )
        token_ids = jnp.broadcast_to(jnp.arange(tokens_dev, dtype=jnp.int32)[None, :], mine.shape)
        rank_at = jnp.where(mine, mine_rank, capacity)
        table = (
            jnp.zeros((experts_count, capacity), jnp.int32)
            .at[source_ids, rank_at]
            .set(source_ids * tokens_dev + token_ids, mode="drop")
        )
        filled = (
            jnp.zeros((experts_count, capacity), jnp.bool_)
            .at[source_ids, rank_at]
            .set(True, mode="drop")
        )
        incoming_rows = jnp.where(filled[..., None], moe_all[table], jnp.zeros((), jnp.bfloat16))
        returned = expert_path(incoming_rows, w_in_local, w_down_local, pair_active)
        combined = returned.reshape(experts_count * capacity, columns)[slot_ids].astype(jnp.float32)
        combined = combined * gate_weights.reshape(-1)[:, None]
        moe_out = jnp.sum(combined.reshape(tokens_dev, top_count, columns), axis=1)
        output = (after_attn.astype(jnp.float32) + shared_out + moe_out).astype(jnp.bfloat16)
        output, cache = (output, cache)
        states = jnp.where(active, states.at[micro_index].set(output), states)
        caches = jnp.where(active, caches.at[micro_index].set(cache), caches)
        if tick_index + 1 < ticks:
            carried_rows = passed_along(output, "section", 1)
    return (states[None], caches[None])


def solution(mesh):
    placed = (
        P(None, "expert", "tensor"),
        P(None, "expert"),
        P(),
        P("section", None, "expert", None),
        P("section", "tensor"),
        P("section", "tensor"),
        P("section", "expert", "tensor", None),
        P("section", "expert", "tensor"),
        P("section", "expert", None, "tensor"),
        P("section", "expert", "tensor"),
        P("section", "tensor", None),
        P("section", "expert", None, None, "tensor"),
        P("section", "expert", "tensor", None),
    )
    return jax.shard_map(
        local,
        mesh=mesh,
        in_specs=placed,
        out_specs=(
            P("section", None, "expert", "tensor"),
            P("section", None, "expert", None, "tensor"),
        ),
        check_vma=False,
    )
```

```python
import functools

import jax
import jax.numpy as jnp
from jax import lax
from jax.sharding import PartitionSpec as P

HD = 128


NORM_EPS = 1e-05
ROPE_BASE = 500000.0


def passed_along(value, axis, steps):
    count = lax.axis_size(axis)
    leading, last = (max(0, -steps), min(count, count - steps))
    return lax.ppermute(value, axis, [(source, source + steps) for source in range(leading, last)])


def rotate_heads(values_in, positions):
    head_width = values_in.shape[-1]
    half_width = head_width // 2
    frequency = ROPE_BASE ** (-(jnp.arange(half_width, dtype=jnp.float32) * (2.0 / head_width)))
    angles = positions[:, None] * frequency[None, :]
    angles = angles.reshape((positions.shape[0],) + (1,) * (values_in.ndim - 2) + (half_width,))
    cosines = jnp.cos(angles)
    sines = jnp.sin(angles)
    first_half = values_in[..., :half_width]
    second_half = values_in[..., half_width:]
    return jnp.concatenate(
        [first_half * cosines - second_half * sines, second_half * cosines + first_half * sines],
        axis=-1,
    )


def norm_full_rows(values_in, gain_full):
    widened = tensor_gather(values_in, 1).astype(jnp.float32)
    squares = jnp.mean(widened * widened, axis=-1)
    return (widened * lax.rsqrt(squares + NORM_EPS)[:, None] * gain_full).astype(jnp.bfloat16)


def swap_cores(value):
    count = lax.axis_size("section")
    return lax.ppermute(value, "section", [(source, (source + 1) % count) for source in range(count)])


def paired_gather(value, axis, split_axis, active):
    value = jnp.where(active, value, swap_cores(value))
    first, second = jnp.split(value, 2, axis=split_axis)
    gathered = lax.all_gather(jnp.where(active, first, second), "expert", axis=axis, tiled=True)
    theirs = swap_cores(gathered)
    lead = jnp.where(active, gathered, theirs)
    trail = jnp.where(active, theirs, gathered)
    return jnp.concatenate([lead, trail], axis=split_axis)


def running_count(flags, axis):
    size = flags.shape[axis]
    steps = jnp.arange(size, dtype=jnp.int32)
    lower = (steps[:, None] >= steps[None, :]).astype(jnp.bfloat16)
    counted = jnp.tensordot(lower, flags.astype(jnp.bfloat16), axes=((1,), (axis,)),
                            preferred_element_type=jnp.float32)
    return jnp.moveaxis(counted, 0, axis).astype(jnp.int32)


def swap_tensor(value):
    count = lax.axis_size("tensor")
    return lax.ppermute(value, "tensor", [(source, (source + 1) % count) for source in range(count)])


def tensor_sum_scatter(value, axis):
    if lax.axis_size("tensor") != 2:
        return lax.psum_scatter(value, "tensor", scatter_dimension=axis, tiled=True)
    first, second = jnp.split(value, 2, axis=axis)
    lower = lax.axis_index("tensor") == 0
    kept = jnp.where(lower, first, second)
    sent = jnp.where(lower, second, first)
    return (kept.astype(jnp.float32) + swap_tensor(sent).astype(jnp.float32)).astype(value.dtype)


def tensor_gather(value, axis):
    if lax.axis_size("tensor") != 2:
        return lax.all_gather(value, "tensor", axis=axis, tiled=True)
    other = swap_tensor(value)
    lower = lax.axis_index("tensor") == 0
    return jnp.concatenate(
        [jnp.where(lower, value, other), jnp.where(lower, other, value)], axis=axis
    )


def paired_apply(step, value, in_axis, out_axis, active):
    if active is None:
        return step(value)
    value = jnp.where(active, value, swap_cores(value))
    first, second = jnp.split(value, 2, axis=in_axis)
    done = step(jnp.where(active, first, second))
    theirs = swap_cores(done)
    return jnp.concatenate(
        [jnp.where(active, done, theirs), jnp.where(active, theirs, done)], axis=out_axis
    )


def quad_gather(rows, active):
    value = jnp.where(active, rows, swap_cores(rows))
    quarters = jnp.split(value, 4, axis=1)
    lower = lax.axis_index("tensor") == 0
    lead = jnp.where(lower, quarters[0], quarters[2])
    trail = jnp.where(lower, quarters[1], quarters[3])
    gathered = lax.all_gather(jnp.where(active, lead, trail), "expert", axis=0, tiled=True)
    sibling = swap_cores(gathered)
    half = jnp.concatenate(
        [jnp.where(active, gathered, sibling), jnp.where(active, sibling, gathered)], axis=1
    )
    other = swap_tensor(half)
    return jnp.concatenate(
        [jnp.where(lower, half, other), jnp.where(lower, other, half)], axis=1
    )


def terms_to_slots(terms, active):
    count = lax.axis_size("expert")
    blocks = terms.reshape(count, terms.shape[0] // count, terms.shape[1])

    def step(part):
        by_slot = lax.all_to_all(
            part.reshape(-1, part.shape[2]), "expert", split_axis=0, concat_axis=1, tiled=True
        )
        return tensor_sum_scatter(by_slot, 1)

    return paired_apply(step, blocks, 1, 0, active)


def expert_path(full_rows, w_in_local, w_down_local, active):
    sources, slot_count, model_width = full_rows.shape
    local_width = w_down_local.shape[0]
    hidden = jnp.dot(
        full_rows.reshape(sources * slot_count, model_width),
        w_in_local.reshape(model_width, 2 * local_width),
        preferred_element_type=jnp.float32,
    )
    activated = (jax.nn.silu(hidden[:, :local_width]) * hidden[:, local_width:]).astype(
        jnp.bfloat16
    )
    partial_value = jnp.dot(activated, w_down_local, preferred_element_type=jnp.float32)
    partial_value = partial_value.reshape(sources, slot_count, model_width)

    def step(part):
        summed = tensor_sum_scatter(part, 2)
        return lax.all_to_all(summed, "expert", split_axis=0, concat_axis=0, tiled=True)

    return paired_apply(step, partial_value.astype(jnp.bfloat16), 1, 1, active)


def local(
    hidden_in,
    segment_ids,
    prompt_lengths,
    expert_choice,
    attn_gain,
    ffn_gain,
    w_qkv,
    w_out,
    w_shared_in,
    w_shared_down,
    router_weight,
    w_in,
    w_down,
):
    sections = lax.axis_size("section")
    section_id = lax.axis_index("section")
    experts_count = lax.axis_size("expert")
    expert_id = lax.axis_index("expert")
    micro_count, tokens_dev, columns = hidden_in.shape
    qkv_full = lax.all_gather(w_qkv[0], "expert", axis=0, tiled=True)
    out_local = w_out[0]
    shared_down_local = w_shared_down[0]
    shared_in_cols = lax.all_to_all(w_shared_in[0], "expert", split_axis=2, concat_axis=0, tiled=True)
    choices_every = lax.all_gather(expert_choice[0], "expert", axis=0, tiled=False)
    router_full = lax.all_gather(router_weight[0], "tensor", axis=0, tiled=True)
    attn_gain_full = lax.all_gather(attn_gain[0], "tensor", axis=0, tiled=True)
    ffn_gain_full = lax.all_gather(ffn_gain[0], "tensor", axis=0, tiled=True)
    w_in_local = w_in[0, 0]
    w_down_local = w_down[0, 0]
    (
        qkv_full,
        shared_in_cols,
        choices_every,
        router_full,
        attn_gain_full,
        ffn_gain_full,
        w_in_local,
        w_down_local,
    ) = lax.optimization_barrier(
        (
            qkv_full,
            shared_in_cols,
            choices_every,
            router_full,
            attn_gain_full,
            ffn_gain_full,
            w_in_local,
            w_down_local,
        )
    )
    model_width, kv_local, group_cols = qkv_full.shape
    shared_cols = shared_in_cols.shape[2]
    head_width = HD
    group = group_cols // head_width - 2
    scale = head_width ** (-0.5)
    top_count = expert_choice.shape[-1]
    capacity = 5 * tokens_dev * top_count // (4 * experts_count)
    slot_index = expert_id * tokens_dev + jnp.arange(tokens_dev, dtype=jnp.int32)
    carried_rows = jnp.zeros((tokens_dev, columns), jnp.bfloat16)
    states = jnp.zeros((micro_count, tokens_dev, columns), jnp.bfloat16)
    caches = jnp.zeros((micro_count, tokens_dev, 2, kv_local * head_width), jnp.bfloat16)
    ticks = micro_count + sections - 1
    for tick_index in range(ticks):
        micro_index = jnp.clip(tick_index - section_id, 0, micro_count - 1)
        incoming = jnp.where(
            section_id == 0, hidden_in[min(tick_index, micro_count - 1)], carried_rows
        )
        active = (tick_index - section_id >= 0) & (tick_index - section_id < micro_count)
        pair_active = active if micro_count == 1 and sections == 2 else None
        if pair_active is not None:
            expert_gather = functools.partial(paired_gather, active=active)
        else:
            def expert_gather(value, axis, split_axis):
                return lax.all_gather(value, "expert", axis=axis, tiled=True)
        segments = segment_ids[micro_index]
        lengths = prompt_lengths[micro_index]
        choices = expert_choice[0, micro_index]
        starts = jnp.cumsum(lengths) - lengths
        member = segments[:, None] == jnp.arange(lengths.shape[0], dtype=jnp.int32)[None, :]
        first_slot = jnp.sum(jnp.where(member, starts[None, :], 0), axis=1)
        positions = jnp.where(segments >= 0, slot_index - first_slot, 0).astype(jnp.float32)
        normed_full = norm_full_rows(incoming, attn_gain_full)
        projected = jnp.dot(
            normed_full, qkv_full.reshape(model_width, -1), preferred_element_type=jnp.float32
        )
        projected = projected.reshape(tokens_dev, kv_local, group + 2, head_width)
        queries = rotate_heads(projected[:, :, :group], positions).astype(jnp.bfloat16)
        key_rows = rotate_heads(projected[:, :, group], positions).astype(jnp.bfloat16)
        value_rows = projected[:, :, group + 1].astype(jnp.bfloat16)
        cache = jnp.stack(
            [key_rows.reshape(tokens_dev, -1), value_rows.reshape(tokens_dev, -1)], axis=1
        )
        kv_piece = expert_gather(cache.reshape(tokens_dev, -1), 0, 1)
        key_count = kv_piece.shape[0]
        kv_piece = kv_piece.reshape(key_count, 2, kv_local, head_width)
        key_slots = jnp.arange(key_count, dtype=jnp.int32)
        ends = jnp.cumsum(lengths)
        seg_piece = jnp.sum((key_slots[:, None] >= ends[None, :]).astype(jnp.int32), axis=1)
        seg_piece = jnp.where(key_slots < ends[-1], seg_piece, -1)
        allowed = (segments[:, None] == seg_piece[None, :]) & (segments[:, None] >= 0) & (
            key_slots[None, :] <= slot_index[:, None]
        ) | (key_slots[None, :] == slot_index[:, None])
        scores = (
            jnp.einsum(
                "tagd,nad->tagn", queries, kv_piece[:, 0], preferred_element_type=jnp.float32
            )
            * scale
        )
        weights_full = jnp.where(allowed[:, None, None, :], jnp.exp(scores), 0.0)
        numerator = jnp.einsum(
            "tagn,nad->tagd",
            weights_full.astype(jnp.bfloat16),
            kv_piece[:, 1],
            preferred_element_type=jnp.float32,
        )
        numerator, denominator = (numerator, jnp.sum(weights_full, axis=-1))
        attended = (numerator / denominator[..., None]).astype(jnp.bfloat16).reshape(tokens_dev, -1)
        attended_all = expert_gather(attended, 0, 1)
        attn_terms = lax.dot_general(
            attended_all, out_local, (((1,), (1,)), ((), ())), preferred_element_type=jnp.float32
        )
        attn_sum = terms_to_slots(attn_terms.astype(jnp.bfloat16), pair_active).astype(jnp.float32)
        after_attn = (incoming.astype(jnp.float32) + attn_sum).astype(jnp.bfloat16)
        moe_rows = norm_full_rows(after_attn, ffn_gain_full)
        if pair_active is not None and lax.axis_size("tensor") == 2:
            moe_all = quad_gather(moe_rows, pair_active)
        else:
            moe_all = expert_gather(moe_rows, 0, 1)
        shared_hidden = jnp.dot(
            moe_all,
            shared_in_cols.reshape(model_width, 2 * shared_cols),
            preferred_element_type=jnp.float32,
        )
        shared_act = (
            jax.nn.silu(shared_hidden[:, :shared_cols]) * shared_hidden[:, shared_cols:]
        ).astype(jnp.bfloat16)
        shared_act = expert_gather(shared_act.T, 0, 1)
        shared_terms = lax.dot_general(
            shared_act,
            shared_down_local,
            (((0,), (1,)), ((), ())),
            preferred_element_type=jnp.float32,
        )
        shared_sum = terms_to_slots(shared_terms.astype(jnp.bfloat16), pair_active)
        shared_out = lax.optimization_barrier(shared_sum).astype(jnp.float32)
        logits = jnp.dot(
            moe_rows.astype(jnp.float32), router_full, precision=lax.Precision.HIGHEST
        )
        expert_ids = jnp.arange(logits.shape[1], dtype=jnp.int32)
        picked = jnp.sum(
            jnp.where(choices[:, :, None] == expert_ids[None, None, :], logits[:, None, :], 0.0),
            axis=2,
        )
        raised = jnp.exp(picked)
        gate_weights = raised / jnp.sum(raised, axis=1, keepdims=True)
        flat_choice = choices.reshape(-1)
        onehot = (flat_choice[:, None] == expert_ids[None, :]).astype(jnp.int32)
        slot_rank = jnp.sum(onehot * (running_count(onehot, 0) - onehot), axis=1)
        slot_ids = flat_choice * capacity + slot_rank
        choices_all = choices_every[:, micro_index]
        mine = jnp.any(choices_all == expert_id, axis=2)
        mine_rank = running_count(mine, 1) - 1
        source_ids = jnp.broadcast_to(
            jnp.arange(experts_count, dtype=jnp.int32)[:, None], mine.shape
        )
        token_ids = jnp.broadcast_to(jnp.arange(tokens_dev, dtype=jnp.int32)[None, :], mine.shape)
        rank_at = jnp.where(mine, mine_rank, capacity)
        table = (
            jnp.zeros((experts_count, capacity), jnp.int32)
            .at[source_ids, rank_at]
            .set(source_ids * tokens_dev + token_ids, mode="drop")
        )
        filled = (
            jnp.zeros((experts_count, capacity), jnp.bool_)
            .at[source_ids, rank_at]
            .set(True, mode="drop")
        )
        incoming_rows = jnp.where(filled[..., None], moe_all[table], jnp.zeros((), jnp.bfloat16))
        returned = expert_path(incoming_rows, w_in_local, w_down_local, pair_active)
        combined = returned.reshape(experts_count * capacity, columns)[slot_ids].astype(jnp.float32)
        combined = combined * gate_weights.reshape(-1)[:, None]
        moe_out = jnp.sum(combined.reshape(tokens_dev, top_count, columns), axis=1)
        output = (after_attn.astype(jnp.float32) + shared_out + moe_out).astype(jnp.bfloat16)
        output, cache = (output, cache)
        states = jnp.where(active, states.at[micro_index].set(output), states)
        caches = jnp.where(active, caches.at[micro_index].set(cache), caches)
        if tick_index + 1 < ticks:
            carried_rows = passed_along(output, "section", 1)
    return (states[None], caches[None])


def solution(mesh):
    placed = (
        P(None, "expert", "tensor"),
        P(None, "expert"),
        P(),
        P("section", None, "expert", None),
        P("section", "tensor"),
        P("section", "tensor"),
        P("section", "expert", "tensor", None),
        P("section", "expert", "tensor"),
        P("section", "expert", None, "tensor"),
        P("section", "expert", "tensor"),
        P("section", "tensor", None),
        P("section", "expert", None, None, "tensor"),
        P("section", "expert", "tensor", None),
    )
    return jax.shard_map(
        local,
        mesh=mesh,
        in_specs=placed,
        out_specs=(
            P("section", None, "expert", "tensor"),
            P("section", None, "expert", None, "tensor"),
        ),
        check_vma=False,
    )
```

```python
import functools

import jax
import jax.numpy as jnp
from jax import lax
from jax.sharding import PartitionSpec as P

HD = 128


NORM_EPS = 1e-05
ROPE_BASE = 500000.0


def passed_along(value, axis, steps):
    count = lax.axis_size(axis)
    leading, last = (max(0, -steps), min(count, count - steps))
    return lax.ppermute(value, axis, [(source, source + steps) for source in range(leading, last)])


def rotate_heads(values_in, positions):
    head_width = values_in.shape[-1]
    half_width = head_width // 2
    frequency = ROPE_BASE ** (-(jnp.arange(half_width, dtype=jnp.float32) * (2.0 / head_width)))
    angles = positions[:, None] * frequency[None, :]
    angles = angles.reshape((positions.shape[0],) + (1,) * (values_in.ndim - 2) + (half_width,))
    cosines = jnp.cos(angles)
    sines = jnp.sin(angles)
    first_half = values_in[..., :half_width]
    second_half = values_in[..., half_width:]
    return jnp.concatenate(
        [first_half * cosines - second_half * sines, second_half * cosines + first_half * sines],
        axis=-1,
    )


def norm_full_rows(values_in, gain_full):
    widened = tensor_gather(values_in, 1).astype(jnp.float32)
    squares = jnp.mean(widened * widened, axis=-1)
    return (widened * lax.rsqrt(squares + NORM_EPS)[:, None] * gain_full).astype(jnp.bfloat16)


def swap_cores(value):
    count = lax.axis_size("section")
    return lax.ppermute(value, "section", [(source, (source + 1) % count) for source in range(count)])


def paired_gather(value, axis, split_axis, active):
    value = jnp.where(active, value, swap_cores(value))
    first, second = jnp.split(value, 2, axis=split_axis)
    gathered = lax.all_gather(jnp.where(active, first, second), "expert", axis=axis, tiled=True)
    theirs = swap_cores(gathered)
    lead = jnp.where(active, gathered, theirs)
    trail = jnp.where(active, theirs, gathered)
    return jnp.concatenate([lead, trail], axis=split_axis)


def running_count(flags, axis):
    size = flags.shape[axis]
    steps = jnp.arange(size, dtype=jnp.int32)
    lower = (steps[:, None] >= steps[None, :]).astype(jnp.bfloat16)
    counted = jnp.tensordot(lower, flags.astype(jnp.bfloat16), axes=((1,), (axis,)),
                            preferred_element_type=jnp.float32)
    return jnp.moveaxis(counted, 0, axis).astype(jnp.int32)


def swap_tensor(value):
    count = lax.axis_size("tensor")
    return lax.ppermute(value, "tensor", [(source, (source + 1) % count) for source in range(count)])


def tensor_sum_scatter(value, axis):
    if lax.axis_size("tensor") != 2:
        return lax.psum_scatter(value, "tensor", scatter_dimension=axis, tiled=True)
    first, second = jnp.split(value, 2, axis=axis)
    lower = lax.axis_index("tensor") == 0
    kept = jnp.where(lower, first, second)
    sent = jnp.where(lower, second, first)
    return (kept.astype(jnp.float32) + swap_tensor(sent).astype(jnp.float32)).astype(value.dtype)


def tensor_gather(value, axis):
    if lax.axis_size("tensor") != 2:
        return lax.all_gather(value, "tensor", axis=axis, tiled=True)
    other = swap_tensor(value)
    lower = lax.axis_index("tensor") == 0
    return jnp.concatenate(
        [jnp.where(lower, value, other), jnp.where(lower, other, value)], axis=axis
    )


def paired_apply(step, value, in_axis, out_axis, active):
    if active is None:
        return step(value)
    value = jnp.where(active, value, swap_cores(value))
    first, second = jnp.split(value, 2, axis=in_axis)
    done = step(jnp.where(active, first, second))
    theirs = swap_cores(done)
    return jnp.concatenate(
        [jnp.where(active, done, theirs), jnp.where(active, theirs, done)], axis=out_axis
    )


def terms_to_slots(terms, active):
    count = lax.axis_size("expert")
    blocks = terms.reshape(count, terms.shape[0] // count, terms.shape[1])

    def step(part):
        by_slot = lax.all_to_all(
            part.reshape(-1, part.shape[2]), "expert", split_axis=0, concat_axis=1, tiled=True
        )
        return tensor_sum_scatter(by_slot, 1)

    return paired_apply(step, blocks, 1, 0, active)


def expert_path(full_rows, w_in_local, w_down_local, active):
    sources, slot_count, model_width = full_rows.shape
    local_width = w_down_local.shape[0]
    hidden = jnp.dot(
        full_rows.reshape(sources * slot_count, model_width),
        w_in_local.reshape(model_width, 2 * local_width),
        preferred_element_type=jnp.float32,
    )
    activated = (jax.nn.silu(hidden[:, :local_width]) * hidden[:, local_width:]).astype(
        jnp.bfloat16
    )
    partial_value = jnp.dot(activated, w_down_local, preferred_element_type=jnp.float32)
    partial_value = partial_value.reshape(sources, slot_count, model_width)

    def step(part):
        summed = tensor_sum_scatter(part, 2)
        return lax.all_to_all(summed, "expert", split_axis=0, concat_axis=0, tiled=True)

    return paired_apply(step, partial_value.astype(jnp.bfloat16), 1, 1, active)


def local(
    hidden_in,
    segment_ids,
    prompt_lengths,
    expert_choice,
    attn_gain,
    ffn_gain,
    w_qkv,
    w_out,
    w_shared_in,
    w_shared_down,
    router_weight,
    w_in,
    w_down,
):
    sections = lax.axis_size("section")
    section_id = lax.axis_index("section")
    experts_count = lax.axis_size("expert")
    expert_id = lax.axis_index("expert")
    micro_count, tokens_dev, columns = hidden_in.shape
    qkv_full = lax.all_gather(w_qkv[0], "expert", axis=0, tiled=True)
    out_local = w_out[0]
    shared_down_local = w_shared_down[0]
    shared_in_cols = lax.all_to_all(w_shared_in[0], "expert", split_axis=2, concat_axis=0, tiled=True)
    choices_every = lax.all_gather(expert_choice[0], "expert", axis=0, tiled=False)
    router_full = lax.all_gather(router_weight[0], "tensor", axis=0, tiled=True)
    attn_gain_full = lax.all_gather(attn_gain[0], "tensor", axis=0, tiled=True)
    ffn_gain_full = lax.all_gather(ffn_gain[0], "tensor", axis=0, tiled=True)
    w_in_local = w_in[0, 0]
    w_down_local = w_down[0, 0]
    (
        qkv_full,
        shared_in_cols,
        choices_every,
        router_full,
        attn_gain_full,
        ffn_gain_full,
        w_in_local,
        w_down_local,
    ) = lax.optimization_barrier(
        (
            qkv_full,
            shared_in_cols,
            choices_every,
            router_full,
            attn_gain_full,
            ffn_gain_full,
            w_in_local,
            w_down_local,
        )
    )
    model_width, kv_local, group_cols = qkv_full.shape
    shared_cols = shared_in_cols.shape[2]
    head_width = HD
    group = group_cols // head_width - 2
    scale = head_width ** (-0.5)
    top_count = expert_choice.shape[-1]
    capacity = 5 * tokens_dev * top_count // (4 * experts_count)
    slot_index = expert_id * tokens_dev + jnp.arange(tokens_dev, dtype=jnp.int32)
    carried_rows = jnp.zeros((tokens_dev, columns), jnp.bfloat16)
    states = jnp.zeros((micro_count, tokens_dev, columns), jnp.bfloat16)
    caches = jnp.zeros((micro_count, tokens_dev, 2, kv_local * head_width), jnp.bfloat16)
    ticks = micro_count + sections - 1
    for tick_index in range(ticks):
        micro_index = jnp.clip(tick_index - section_id, 0, micro_count - 1)
        incoming = jnp.where(
            section_id == 0, hidden_in[min(tick_index, micro_count - 1)], carried_rows
        )
        active = (tick_index - section_id >= 0) & (tick_index - section_id < micro_count)
        pair_active = active if micro_count == 1 and sections == 2 else None
        if pair_active is not None:
            expert_gather = functools.partial(paired_gather, active=active)
        else:
            def expert_gather(value, axis, split_axis):
                return lax.all_gather(value, "expert", axis=axis, tiled=True)
        segments = segment_ids[micro_index]
        lengths = prompt_lengths[micro_index]
        choices = expert_choice[0, micro_index]
        starts = jnp.cumsum(lengths) - lengths
        member = segments[:, None] == jnp.arange(lengths.shape[0], dtype=jnp.int32)[None, :]
        first_slot = jnp.sum(jnp.where(member, starts[None, :], 0), axis=1)
        positions = jnp.where(segments >= 0, slot_index - first_slot, 0).astype(jnp.float32)
        normed_full = norm_full_rows(incoming, attn_gain_full)
        projected = jnp.dot(
            normed_full, qkv_full.reshape(model_width, -1), preferred_element_type=jnp.float32
        )
        projected = projected.reshape(tokens_dev, kv_local, group + 2, head_width)
        queries = rotate_heads(projected[:, :, :group], positions).astype(jnp.bfloat16)
        key_rows = rotate_heads(projected[:, :, group], positions).astype(jnp.bfloat16)
        value_rows = projected[:, :, group + 1].astype(jnp.bfloat16)
        cache = jnp.stack(
            [key_rows.reshape(tokens_dev, -1), value_rows.reshape(tokens_dev, -1)], axis=1
        )
        kv_piece = expert_gather(cache.reshape(tokens_dev, -1), 0, 1)
        key_count = kv_piece.shape[0]
        kv_piece = kv_piece.reshape(key_count, 2, kv_local, head_width)
        key_slots = jnp.arange(key_count, dtype=jnp.int32)
        ends = jnp.cumsum(lengths)
        seg_piece = jnp.sum((key_slots[:, None] >= ends[None, :]).astype(jnp.int32), axis=1)
        seg_piece = jnp.where(key_slots < ends[-1], seg_piece, -1)
        allowed = (segments[:, None] == seg_piece[None, :]) & (segments[:, None] >= 0) & (
            key_slots[None, :] <= slot_index[:, None]
        ) | (key_slots[None, :] == slot_index[:, None])
        scores = (
            jnp.einsum(
                "tagd,nad->tagn", queries, kv_piece[:, 0], preferred_element_type=jnp.float32
            )
            * scale
        )
        weights_full = jnp.where(allowed[:, None, None, :], jnp.exp(scores), 0.0)
        numerator = jnp.einsum(
            "tagn,nad->tagd",
            weights_full.astype(jnp.bfloat16),
            kv_piece[:, 1],
            preferred_element_type=jnp.float32,
        )
        numerator, denominator = (numerator, jnp.sum(weights_full, axis=-1))
        attended = (numerator / denominator[..., None]).astype(jnp.bfloat16).reshape(tokens_dev, -1)
        attended_all = expert_gather(attended, 0, 1)
        attn_terms = lax.dot_general(
            attended_all, out_local, (((1,), (1,)), ((), ())), preferred_element_type=jnp.float32
        )
        attn_sum = terms_to_slots(attn_terms.astype(jnp.bfloat16), pair_active).astype(jnp.float32)
        after_attn = (incoming.astype(jnp.float32) + attn_sum).astype(jnp.bfloat16)
        moe_rows = norm_full_rows(after_attn, ffn_gain_full)
        moe_all = expert_gather(moe_rows, 0, 1)
        shared_hidden = jnp.dot(
            moe_all,
            shared_in_cols.reshape(model_width, 2 * shared_cols),
            preferred_element_type=jnp.float32,
        )
        shared_act = (
            jax.nn.silu(shared_hidden[:, :shared_cols]) * shared_hidden[:, shared_cols:]
        ).astype(jnp.bfloat16)
        shared_act = expert_gather(shared_act.T, 0, 1)
        shared_terms = lax.dot_general(
            shared_act,
            shared_down_local,
            (((0,), (1,)), ((), ())),
            preferred_element_type=jnp.float32,
        )
        shared_sum = terms_to_slots(shared_terms.astype(jnp.bfloat16), pair_active)
        shared_out = lax.optimization_barrier(shared_sum).astype(jnp.float32)
        logits = jnp.dot(
            moe_rows.astype(jnp.float32), router_full, precision=lax.Precision.HIGHEST
        )
        expert_ids = jnp.arange(logits.shape[1], dtype=jnp.int32)
        picked = jnp.sum(
            jnp.where(choices[:, :, None] == expert_ids[None, None, :], logits[:, None, :], 0.0),
            axis=2,
        )
        raised = jnp.exp(picked)
        gate_weights = raised / jnp.sum(raised, axis=1, keepdims=True)
        flat_choice = choices.reshape(-1)
        onehot = (flat_choice[:, None] == expert_ids[None, :]).astype(jnp.int32)
        slot_rank = jnp.sum(onehot * (running_count(onehot, 0) - onehot), axis=1)
        slot_ids = flat_choice * capacity + slot_rank
        choices_all = choices_every[:, micro_index]
        mine = jnp.any(choices_all == expert_id, axis=2)
        mine_rank = running_count(mine, 1) - 1
        source_ids = jnp.broadcast_to(
            jnp.arange(experts_count, dtype=jnp.int32)[:, None], mine.shape
        )
        token_ids = jnp.broadcast_to(jnp.arange(tokens_dev, dtype=jnp.int32)[None, :], mine.shape)
        rank_at = jnp.where(mine, mine_rank, capacity)
        table = (
            jnp.zeros((experts_count, capacity), jnp.int32)
            .at[source_ids, rank_at]
            .set(source_ids * tokens_dev + token_ids, mode="drop")
        )
        filled = (
            jnp.zeros((experts_count, capacity), jnp.bool_)
            .at[source_ids, rank_at]
            .set(True, mode="drop")
        )
        picks = (
            (table[..., None] == jnp.arange(moe_all.shape[0], dtype=jnp.int32)) & filled[..., None]
        ).astype(jnp.bfloat16)
        incoming_rows = jnp.einsum(
            "scn,nd->scd", picks, moe_all, preferred_element_type=jnp.float32
        ).astype(jnp.bfloat16)
        returned = expert_path(incoming_rows, w_in_local, w_down_local, pair_active)
        combined = returned.reshape(experts_count * capacity, columns)[slot_ids].astype(jnp.float32)
        combined = combined * gate_weights.reshape(-1)[:, None]
        moe_out = jnp.sum(combined.reshape(tokens_dev, top_count, columns), axis=1)
        output = (after_attn.astype(jnp.float32) + shared_out + moe_out).astype(jnp.bfloat16)
        output, cache = (output, cache)
        states = jnp.where(active, states.at[micro_index].set(output), states)
        caches = jnp.where(active, caches.at[micro_index].set(cache), caches)
        if tick_index + 1 < ticks:
            carried_rows = passed_along(output, "section", 1)
    return (states[None], caches[None])


def solution(mesh):
    placed = (
        P(None, "expert", "tensor"),
        P(None, "expert"),
        P(),
        P("section", None, "expert", None),
        P("section", "tensor"),
        P("section", "tensor"),
        P("section", "expert", "tensor", None),
        P("section", "expert", "tensor"),
        P("section", "expert", None, "tensor"),
        P("section", "expert", "tensor"),
        P("section", "tensor", None),
        P("section", "expert", None, None, "tensor"),
        P("section", "expert", "tensor", None),
    )
    return jax.shard_map(
        local,
        mesh=mesh,
        in_specs=placed,
        out_specs=(
            P("section", None, "expert", "tensor"),
            P("section", None, "expert", None, "tensor"),
        ),
        check_vma=False,
    )
```
